32 devices in a mesh: box: 16 (over z, y, core), grp: 2 (over x).
Axes of the slice: x: 2, y: 2, z: 4, core: 2. Of those that a mesh axis runs over, the one named last changes fastest.
Arguments:
- phi_start: float32 [1024, 64, 256], P('box', 'grp'), may hold values from -6 to 6
- right_side: float32 [1024, 64, 256], P('box', 'grp'), may hold values from -6 to 6
- sigma: float32 [1024, 64, 256], P('box', 'grp'), may hold values from 0.2 to 5
Outputs:
- phi_smooth: float32 [1024, 64, 256], P('box', 'grp')
- coarse_residual: float32 [512, 32, 128], P('box')
The draws below stay inside these ranges and needn't reach their ends.
All inputs are finite; a program needn't handle non-finite values.
Results may differ from the reference program's by a relative error of at most 0.00002.
Values sent between devices are 32-bit elements; how exact they have to be, the bound alone decides.
No kernel may reach another device: no remote copies, remote signals or barrier semaphores. Data moves between devices by JAX's collectives and lax.ppermute only.
A program may use at most 128 MiB of HBM per device.

```python
import math
import jax
import jax.numpy as jnp

NZ = 256
SWEEPS = 2
NX = 1024
NY = 64


def shard_levels(stream_key, dims, cuts, least, top_value):
    level, own = 1.0, jax.random.fold_in(stream_key, 6)
    for axis_at, blocks in cuts:
        draws = jnp.exp(jax.random.uniform(jax.random.fold_in(own, axis_at), (blocks,), jnp.float32, least / len(cuts), top_value / len(cuts)))
        level = level * jnp.repeat(draws, dims[axis_at] // blocks).reshape([-1 if axis == axis_at else 1 for axis in range(len(dims))])
    return level


def normal_values(own_key, extent, spread, reach, cuts=(), kind=jnp.bfloat16):
    values = spread * jax.random.normal(own_key, extent, jnp.float32)
    if cuts:
        values = values * shard_levels(own_key, extent, cuts, -0.22, 0.18)
    return jnp.clip(values, -reach, reach).astype(kind)


def setup_inputs(seed: int = 0) -> dict:
    arg_keys = jax.random.split(jax.random.key(seed), 4)
    phi_start = normal_values(arg_keys[0], (NX, NY, NZ), 1.0, 6.0, ((0, 16), (1, 2)), jnp.float32)
    right_side = normal_values(arg_keys[1], (NX, NY, NZ), 1.0, 6.0, ((0, 16), (1, 2)), jnp.float32)
    sigma = jnp.clip(jnp.exp(math.log(5.0) - 3.218876 * jax.random.uniform(arg_keys[2], (NX, NY, NZ), jnp.float32) ** shard_levels(arg_keys[2], (NX, NY, NZ), ((0, 16), (1, 2)), -0.2, 0.2)), 0.2, 5.0)
    return {"phi_start": phi_start, "right_side": right_side, "sigma": sigma}


def neighbours(padded):
    centre = padded[1:-1, 1:-1]
    zero_layer = jnp.zeros(centre.shape[:2] + (1,), centre.dtype)
    below_z = jnp.concatenate([zero_layer, centre[:, :, :-1]], axis=2)
    above_z = jnp.concatenate([centre[:, :, 1:], zero_layer], axis=2)
    return (centre, padded[:-2, 1:-1], padded[2:, 1:-1], padded[1:-1, :-2], padded[1:-1, 2:], below_z, above_z)


def face_weights(sig_padded, centre_sig, edges):
    pieces = neighbours(sig_padded)
    result = []
    for beside, at_edge in zip(pieces[1:], edges):
        result.append(jnp.where(at_edge, centre_sig, 2.0 * centre_sig * beside / (centre_sig + beside)))
    return tuple(result)


def relax(padded, weights, diagonal, source, chosen):
    pieces = neighbours(padded)
    summed = source
    for weight, beside in zip(weights, pieces[1:]):
        summed = summed + weight * beside
    updated = summed / diagonal
    return padded.at[1:-1, 1:-1].set(jnp.where(chosen, updated, pieces[0]))


def defect(padded, weights, diagonal, source):
    pieces = neighbours(padded)
    coupled = weights[0] * pieces[1]
    for weight, beside in zip(weights[1:], pieces[2:]):
        coupled = coupled + weight * beside
    return source - (diagonal * pieces[0] - coupled)


def restrict(defect_field):
    coarser = defect_field[0::2] + defect_field[1::2]
    coarser = coarser[:, 0::2] + coarser[:, 1::2]
    coarser = coarser[:, :, 0::2] + coarser[:, :, 1::2]
    return 0.125 * coarser


def surround(field):
    return jnp.pad(field, ((1, 1), (1, 1), (0, 0)))


def reference(phi_start, right_side, sigma):
    extent_x, extent_y, extent_z = phi_start.shape
    index_x = jnp.arange(extent_x, dtype=jnp.int32)[:, None, None]
    index_y = jnp.arange(extent_y, dtype=jnp.int32)[None, :, None]
    index_z = jnp.arange(extent_z, dtype=jnp.int32)[None, None, :]
    edges = (index_x == 0, index_x == extent_x - 1, index_y == 0, index_y == extent_y - 1, index_z == 0, index_z == extent_z - 1)
    weights = face_weights(surround(sigma), sigma, edges)
    diagonal = weights[0]
    for weight in weights[1:]:
        diagonal = diagonal + weight
    parity = (index_x + index_y + index_z) % 2
    padded = surround(phi_start)
    for sweep_turn in range(2 * SWEEPS):
        padded = relax(padded, weights, diagonal, right_side, parity == sweep_turn % 2)
    defect_field = defect(padded, weights, diagonal, right_side)
    return padded[1:-1, 1:-1], restrict(defect_field)
```

```python
import functools

import jax
import jax.numpy as jnp
import numpy as np
from jax import lax
from jax.experimental import pallas as pl
from jax.experimental.pallas import tpu as pltpu
from jax.sharding import PartitionSpec as P

SWEEPS = 2
HALO = 2 * SWEEPS + 1
ROW_PAD = 8


def harmonic(s, t):
    return 2.0 * s * t / (s + t)


def smooth_kernel(nx, ny, idx_ref, qy_ref, pz_ref, ph, rs, sg, phi_out, coarse_out,
                  fx, fy, fz, dg, inv, par):
    planes, rows, lanes = ph.shape
    gx0 = idx_ref[0]
    gy0 = idx_ref[1]
    row = lax.broadcasted_iota(jnp.int32, (rows, lanes), 0)
    lane = lax.broadcasted_iota(jnp.int32, (rows, lanes), 1)
    gy = gy0 + row
    iny = (gy >= 0) & (gy < ny)
    par[...] = jnp.where(iny, (gy + lane) & 1, 2)

    def faces_x(i, carry):
        gx = gx0 + i
        ok = (gx >= 0) & (gx + 1 < nx)
        s0 = sg[i]
        s1 = sg[i + 1]
        gyv = gy0 + lax.broadcasted_iota(jnp.int32, (rows, lanes), 0)
        inside = (gyv >= 0) & (gyv < ny) & ok
        fx[i] = jnp.where(inside, harmonic(s0, s1), 0.0)
        return carry

    lax.fori_loop(0, planes - 1, faces_x, 0)

    def faces_yz(i, carry):
        gx = gx0 + i
        inx = (gx >= 0) & (gx < nx)
        r = lax.broadcasted_iota(jnp.int32, (rows, lanes), 0)
        k = lax.broadcasted_iota(jnp.int32, (rows, lanes), 1)
        gyv = gy0 + r
        inyv = (gyv >= 0) & (gyv < ny)
        s = sg[i]
        s_yu = pltpu.roll(s, rows - 1, 0)
        s_zu = pltpu.roll(s, lanes - 1, 1)
        wy = jnp.where(inx & (gyv >= 0) & (gyv + 1 < ny), harmonic(s, s_yu), 0.0)
        wz = jnp.where(inx & inyv & (k < lanes - 1), harmonic(s, s_zu), 0.0)
        fy[i] = wy
        fz[i] = wz
        wxl = jnp.where(gx == 0, s, fx[i - 1])
        wxu = jnp.where(gx == nx - 1, s, fx[i])
        wyl = jnp.where(gyv == 0, s, pltpu.roll(wy, 1, 0))
        wyu = jnp.where(gyv == ny - 1, s, wy)
        wzl = jnp.where(k == 0, s, pltpu.roll(wz, 1, 1))
        wzu = jnp.where(k == lanes - 1, s, wz)
        d = wxl + wxu + wyl + wyu + wzl + wzu
        dg[i] = d
        inv[i] = 1.0 / d
        return carry

    lax.fori_loop(1, planes - 1, faces_yz, 0)

    def coupled_sum(i, pc):
        wy = fy[i]
        wz = fz[i]
        terms = (
            (fx[i - 1], ph[i - 1]),
            (fx[i], ph[i + 1]),
            (pltpu.roll(wy, 1, 0), pltpu.roll(pc, 1, 0)),
            (wy, pltpu.roll(pc, rows - 1, 0)),
            (pltpu.roll(wz, 1, 1), pltpu.roll(pc, 1, 1)),
            (wz, pltpu.roll(pc, lanes - 1, 1)),
        )
        return terms

    for turn in range(2 * SWEEPS):
        colour = turn % 2

        def relax(i, carry, colour=colour):
            gx = gx0 + i
            inx = (gx >= 0) & (gx < nx)
            target = jnp.where(inx, (gx + colour) & 1, 3)
            pc = ph[i]
            summed = rs[i]
            for w, nb in coupled_sum(i, pc):
                summed = summed + w * nb
            ph[i] = jnp.where(par[...] == target, summed * inv[i], pc)
            return carry

        lax.fori_loop(turn + 1, planes - 1 - turn, relax, 0)

    own_rows = rows - 2 * ROW_PAD
    qy = qy_ref[...]
    pz = pz_ref[...]

    def defect_plane(i):
        pc = ph[i]
        terms = coupled_sum(i, pc)
        coupled = terms[0][0] * terms[0][1]
        for w, nb in terms[1:]:
            coupled = coupled + w * nb
        d = rs[i] - (dg[i] * pc - coupled)
        phi_out[i - HALO] = pc[ROW_PAD:ROW_PAD + own_rows]
        return d[ROW_PAD:ROW_PAD + own_rows]

    def restrict(j, carry):
        i = HALO + 2 * j
        pair = defect_plane(i) + defect_plane(i + 1)
        cy = jnp.dot(qy, pair, precision=lax.Precision.HIGHEST,
                     preferred_element_type=jnp.float32)
        cz = jnp.dot(cy, pz, precision=lax.Precision.HIGHEST,
                     preferred_element_type=jnp.float32)
        coarse_out[j] = 0.125 * cz
        return carry

    lax.fori_loop(0, (planes - 2 * HALO) // 2, restrict, 0)


def exchange(arrays):
    boxes = lax.axis_size("box")
    grps = lax.axis_size("grp")
    h = HALO
    stack = lambda parts: jnp.stack(parts)
    down_box = [(i, i + 1) for i in range(boxes - 1)]
    up_box = [(i + 1, i) for i in range(boxes - 1)]
    down_grp = [(i, i + 1) for i in range(grps - 1)]
    up_grp = [(i + 1, i) for i in range(grps - 1)]

    def lin(b, g):
        return b * grps + g

    def diag(db, dg_):
        pairs = []
        for b in range(boxes):
            for g in range(grps):
                sb, sgp = b - db, g - dg_
                if 0 <= sb < boxes and 0 <= sgp < grps:
                    pairs.append((lin(sb, sgp), lin(b, g)))
        return pairs

    both = ("box", "grp")
    x_lo = lax.ppermute(stack([a[-h:] for a in arrays]), "box", down_box)
    x_hi = lax.ppermute(stack([a[:h] for a in arrays]), "box", up_box)
    y_lo = lax.ppermute(stack([a[:, -h:] for a in arrays]), "grp", down_grp)
    y_hi = lax.ppermute(stack([a[:, :h] for a in arrays]), "grp", up_grp)
    c_ll = lax.ppermute(stack([a[-h:, -h:] for a in arrays]), both, diag(1, 1))
    c_lu = lax.ppermute(stack([a[-h:, :h] for a in arrays]), both, diag(1, -1))
    c_ul = lax.ppermute(stack([a[:h, -h:] for a in arrays]), both, diag(-1, 1))
    c_uu = lax.ppermute(stack([a[:h, :h] for a in arrays]), both, diag(-1, -1))
    own = stack(arrays)
    cells_x = own.shape[1]
    zeros = lambda n: jnp.zeros(own.shape[:1] + (n, ROW_PAD - h) + own.shape[3:], own.dtype)
    lower = jnp.concatenate([zeros(h), c_ll, x_lo, c_lu, zeros(h)], axis=2)
    middle = jnp.concatenate([zeros(cells_x), y_lo, own, y_hi, zeros(cells_x)], axis=2)
    upper = jnp.concatenate([zeros(h), c_ul, x_hi, c_uu, zeros(h)], axis=2)
    ext = jnp.concatenate([lower, middle, upper], axis=1)
    return ext[0], ext[1], ext[2]


def local(phi_start, right_side, sigma):
    cells_x, cells_y, cells_z = phi_start.shape
    boxes = lax.axis_size("box")
    grps = lax.axis_size("grp")
    nx = cells_x * boxes
    ny = cells_y * grps
    b = lax.axis_index("box")
    g = lax.axis_index("grp")
    ph, rs, sg = exchange((phi_start, right_side, sigma))
    planes, rows, lanes = ph.shape
    idx = jnp.stack([b * cells_x - HALO, g * cells_y - ROW_PAD]).astype(jnp.int32)
    qy = jnp.asarray(np.kron(np.eye(cells_y // 2), np.ones((1, 2))), jnp.float32)
    pz = jnp.asarray(np.kron(np.eye(cells_z // 2), np.ones((2, 1))), jnp.float32)
    vmem = pltpu.MemorySpace.VMEM
    full = pl.BlockSpec(memory_space=vmem)
    big = pltpu.VMEM((planes, rows, lanes), jnp.float32)
    phi_smooth, coarse = pl.pallas_call(
        functools.partial(smooth_kernel, nx, ny),
        out_shape=(
            jax.ShapeDtypeStruct((cells_x, cells_y, cells_z), jnp.float32),
            jax.ShapeDtypeStruct((cells_x // 2, cells_y // 2, cells_z // 2), jnp.float32),
        ),
        in_specs=[pl.BlockSpec(memory_space=pltpu.MemorySpace.SMEM)] + [full] * 5,
        out_specs=(full, full),
        scratch_shapes=[big, big, big, big, big, pltpu.VMEM((rows, lanes), jnp.int32)],
        compiler_params=pltpu.CompilerParams(vmem_limit_bytes=60 * 1024 * 1024),
    )(idx, qy, pz, ph, rs, sg)
    if grps == 2:
        other = lax.ppermute(coarse, "grp", [(0, 1), (1, 0)])
        group_coarse = jnp.where(
            g == 0,
            jnp.concatenate([coarse, other], axis=1),
            jnp.concatenate([other, coarse], axis=1),
        )
    else:
        group_coarse = lax.all_gather(coarse, "grp", axis=1, tiled=True)
    return phi_smooth, group_coarse


def solution(mesh):
    placed = (P("box", "grp", None), P("box", "grp", None), P("box", "grp", None))
    return jax.shard_map(
        local,
        mesh=mesh,
        in_specs=placed,
        out_specs=(P("box", "grp", None), P("box", None, None)),
        check_vma=False,
    )
```

```python
import functools

import jax
import jax.numpy as jnp
import numpy as np
from jax import lax
from jax.experimental import pallas as pl
from jax.experimental.pallas import tpu as pltpu
from jax.sharding import PartitionSpec as P

SWEEPS = 2
HALO = 2 * SWEEPS + 1
ROW_PAD = 8


def harmonic(s, t):
    return 2.0 * s * t / (s + t)


def smooth_kernel(nx, ny, idx_ref, qy_ref, pz_ref, own_phi, own_rhs, own_sig,
                  x_lo, x_hi, y_lo, y_hi, c_ll, c_lu, c_ul, c_uu,
                  phi_out, coarse_out, ph, rs, sg, fx, fy, fz, fzl, dg, inv, par, sems):
    planes, rows, lanes = ph.shape
    h = HALO
    cells_x = planes - 2 * h
    cells_y = rows - 2 * ROW_PAD
    gx0 = idx_ref[0]
    gy0 = idx_ref[1]
    mid = pl.ds(h, cells_x)
    lo_p = pl.ds(0, h)
    hi_p = pl.ds(h + cells_x, h)
    own_r = pl.ds(ROW_PAD, cells_y)
    lo_r = pl.ds(ROW_PAD - h, h)
    hi_r = pl.ds(ROW_PAD + cells_y, h)
    copies = []
    for a, dst, own in ((2, sg, own_sig), (0, ph, own_phi), (1, rs, own_rhs)):
        pieces = (
            (own, dst.at[mid, own_r]),
            (x_lo.at[a], dst.at[lo_p, own_r]),
            (x_hi.at[a], dst.at[hi_p, own_r]),
            (y_lo.at[a], dst.at[mid, lo_r]),
            (y_hi.at[a], dst.at[mid, hi_r]),
            (c_ll.at[a], dst.at[lo_p, lo_r]),
            (c_lu.at[a], dst.at[lo_p, hi_r]),
            (c_ul.at[a], dst.at[hi_p, lo_r]),
            (c_uu.at[a], dst.at[hi_p, hi_r]),
        )
        group = []
        for src_ref, dst_ref in pieces:
            cp = pltpu.make_async_copy(src_ref, dst_ref, sems.at[len(copies) + len(group)])
            cp.start()
            group.append(cp)
        copies.extend(group)
    for cp in copies[:9]:
        cp.wait()
    row = lax.broadcasted_iota(jnp.int32, (rows, lanes), 0)
    lane = lax.broadcasted_iota(jnp.int32, (rows, lanes), 1)
    gy = gy0 + row
    iny = (gy >= 0) & (gy < ny)
    par[...] = jnp.where(iny, (gy + lane) & 1, 2)

    def faces_x(i, carry):
        gx = gx0 + i
        ok = (gx >= 0) & (gx + 1 < nx)
        s0 = sg[i]
        s1 = sg[i + 1]
        gyv = gy0 + lax.broadcasted_iota(jnp.int32, (rows, lanes), 0)
        inside = (gyv >= 0) & (gyv < ny) & ok
        fx[i] = jnp.where(inside, harmonic(s0, s1), 0.0)
        return carry

    lax.fori_loop(0, planes - 1, faces_x, 0, unroll=2)

    def faces_yz(i, carry):
        gx = gx0 + i
        inx = (gx >= 0) & (gx < nx)
        r = lax.broadcasted_iota(jnp.int32, (rows, lanes), 0)
        k = lax.broadcasted_iota(jnp.int32, (rows, lanes), 1)
        gyv = gy0 + r
        inyv = (gyv >= 0) & (gyv < ny)
        s = sg[i]
        s_yu = pltpu.roll(s, rows - 1, 0)
        s_zu = pltpu.roll(s, lanes - 1, 1)
        wy = jnp.where(inx & (gyv >= 0) & (gyv + 1 < ny), harmonic(s, s_yu), 0.0)
        wz = jnp.where(inx & inyv & (k < lanes - 1), harmonic(s, s_zu), 0.0)
        wy_lo = pltpu.roll(wy, 1, 0)
        wz_lo = pltpu.roll(wz, 1, 1)
        fy[i] = wy
        fz[i] = wz
        fzl[i] = wz_lo
        wxl = jnp.where(gx == 0, s, fx[i - 1])
        wxu = jnp.where(gx == nx - 1, s, fx[i])
        wyl = jnp.where(gyv == 0, s, wy_lo)
        wyu = jnp.where(gyv == ny - 1, s, wy)
        wzl = jnp.where(k == 0, s, wz_lo)
        wzu = jnp.where(k == lanes - 1, s, wz)
        d = wxl + wxu + wyl + wyu + wzl + wzu
        dg[i] = d
        inv[i] = 1.0 / d
        sg[i] = wy_lo
        return carry

    lax.fori_loop(1, planes - 1, faces_yz, 0, unroll=2)
    for cp in copies[9:]:
        cp.wait()

    def coupled_sum(i, pc):
        wy = fy[i]
        wz = fz[i]
        terms = (
            (fx[i - 1], ph[i - 1]),
            (fx[i], ph[i + 1]),
            (sg[i], pltpu.roll(pc, 1, 0)),
            (wy, pltpu.roll(pc, rows - 1, 0)),
            (fzl[i], pltpu.roll(pc, 1, 1)),
            (wz, pltpu.roll(pc, lanes - 1, 1)),
        )
        return terms

    for turn in range(2 * SWEEPS):
        colour = turn % 2

        def relax(i, carry, colour=colour):
            gx = gx0 + i
            inx = (gx >= 0) & (gx < nx)
            target = jnp.where(inx, (gx + colour) & 1, 3)
            pc = ph[i]
            summed = rs[i]
            for w, nb in coupled_sum(i, pc):
                summed = summed + w * nb
            ph[i] = jnp.where(par[...] == target, summed * inv[i], pc)
            return carry

        lax.fori_loop(turn + 1, planes - 1 - turn, relax, 0, unroll=2)

    own_rows = rows - 2 * ROW_PAD
    qy = qy_ref[...]
    pz = pz_ref[...]

    def defect_plane(i):
        pc = ph[i]
        terms = coupled_sum(i, pc)
        coupled = terms[0][0] * terms[0][1]
        for w, nb in terms[1:]:
            coupled = coupled + w * nb
        d = rs[i] - (dg[i] * pc - coupled)
        phi_out[i - HALO] = pc[ROW_PAD:ROW_PAD + own_rows]
        return d[ROW_PAD:ROW_PAD + own_rows]

    def restrict(j, carry):
        i = HALO + 2 * j
        pair = defect_plane(i) + defect_plane(i + 1)
        cy = jnp.dot(qy, pair, precision=lax.Precision.HIGHEST,
                     preferred_element_type=jnp.float32)
        cz = jnp.dot(cy, pz, precision=lax.Precision.HIGHEST,
                     preferred_element_type=jnp.float32)
        coarse_out[j] = 0.125 * cz
        return carry

    lax.fori_loop(0, (planes - 2 * HALO) // 2, restrict, 0)


def exchange(arrays):
    boxes = lax.axis_size("box")
    grps = lax.axis_size("grp")
    h = HALO
    stack = lambda parts: jnp.stack(parts)
    down_box = [(i, i + 1) for i in range(boxes - 1)]
    up_box = [(i + 1, i) for i in range(boxes - 1)]
    down_grp = [(i, i + 1) for i in range(grps - 1)]
    up_grp = [(i + 1, i) for i in range(grps - 1)]

    def lin(b, g):
        return b * grps + g

    def diag(db, dg_):
        pairs = []
        for b in range(boxes):
            for g in range(grps):
                sb, sgp = b - db, g - dg_
                if 0 <= sb < boxes and 0 <= sgp < grps:
                    pairs.append((lin(sb, sgp), lin(b, g)))
        return pairs

    both = ("box", "grp")
    x_lo = lax.ppermute(stack([a[-h:] for a in arrays]), "box", down_box)
    x_hi = lax.ppermute(stack([a[:h] for a in arrays]), "box", up_box)
    y_lo = lax.ppermute(stack([a[:, -h:] for a in arrays]), "grp", down_grp)
    y_hi = lax.ppermute(stack([a[:, :h] for a in arrays]), "grp", up_grp)
    c_ll = lax.ppermute(stack([a[-h:, -h:] for a in arrays]), both, diag(1, 1))
    c_lu = lax.ppermute(stack([a[-h:, :h] for a in arrays]), both, diag(1, -1))
    c_ul = lax.ppermute(stack([a[:h, -h:] for a in arrays]), both, diag(-1, 1))
    c_uu = lax.ppermute(stack([a[:h, :h] for a in arrays]), both, diag(-1, -1))
    return x_lo, x_hi, y_lo, y_hi, c_ll, c_lu, c_ul, c_uu


def local(phi_start, right_side, sigma):
    cells_x, cells_y, cells_z = phi_start.shape
    boxes = lax.axis_size("box")
    grps = lax.axis_size("grp")
    nx = cells_x * boxes
    ny = cells_y * grps
    b = lax.axis_index("box")
    g = lax.axis_index("grp")
    pieces = exchange((phi_start, right_side, sigma))
    planes = cells_x + 2 * HALO
    rows = cells_y + 2 * ROW_PAD
    lanes = cells_z
    idx = jnp.stack([b * cells_x - HALO, g * cells_y - ROW_PAD]).astype(jnp.int32)
    qy = jnp.asarray(np.kron(np.eye(cells_y // 2), np.ones((1, 2))), jnp.float32)
    pz = jnp.asarray(np.kron(np.eye(cells_z // 2), np.ones((2, 1))), jnp.float32)
    full = pl.BlockSpec(memory_space=pltpu.MemorySpace.VMEM)
    anywhere = pl.BlockSpec(memory_space=pltpu.MemorySpace.HBM)
    big = pltpu.VMEM((planes, rows, lanes), jnp.float32)
    phi_smooth, coarse = pl.pallas_call(
        functools.partial(smooth_kernel, nx, ny),
        out_shape=(
            jax.ShapeDtypeStruct((cells_x, cells_y, cells_z), jnp.float32),
            jax.ShapeDtypeStruct((cells_x // 2, cells_y // 2, cells_z // 2), jnp.float32),
        ),
        in_specs=[pl.BlockSpec(memory_space=pltpu.MemorySpace.SMEM), full, full]
        + [anywhere] * 11,
        out_specs=(full, full),
        scratch_shapes=[big] * 9
        + [pltpu.VMEM((rows, lanes), jnp.int32), pltpu.SemaphoreType.DMA((27,))],
        compiler_params=pltpu.CompilerParams(vmem_limit_bytes=60 * 1024 * 1024),
    )(idx, qy, pz, phi_start, right_side, sigma, *pieces)
    if grps == 2:
        other = lax.ppermute(coarse, "grp", [(0, 1), (1, 0)])
        group_coarse = jnp.where(
            g == 0,
            jnp.concatenate([coarse, other], axis=1),
            jnp.concatenate([other, coarse], axis=1),
        )
    else:
        group_coarse = lax.all_gather(coarse, "grp", axis=1, tiled=True)
    return phi_smooth, group_coarse


def solution(mesh):
    placed = (P("box", "grp", None), P("box", "grp", None), P("box", "grp", None))
    return jax.shard_map(
        local,
        mesh=mesh,
        in_specs=placed,
        out_specs=(P("box", "grp", None), P("box", None, None)),
        check_vma=False,
    )
```

```python
import functools

import jax
import jax.numpy as jnp
import numpy as np
from jax import lax
from jax.experimental import pallas as pl
from jax.experimental.pallas import tpu as pltpu
from jax.sharding import PartitionSpec as P

SWEEPS = 2
HALO = 2 * SWEEPS + 1
ROW_PAD = 8


def harmonic(s, t):
    return 2.0 * s * t / (s + t)


def smooth_kernel(nx, ny, idx_ref, pz_ref, own_phi, own_rhs, own_sig,
                  x_lo, x_hi, y_lo, y_hi, c_lo, c_hi,
                  phi_out, coarse_out, ph, rs, sg, fx, fy, fz, fzl, dg, inv, par,
                  pair_buf, y_sums, sems):
    planes, rows, lanes = ph.shape
    h = HALO
    cells_x = planes - 2 * h
    cells_y = rows - 2 * ROW_PAD
    gx0 = idx_ref[0]
    gy0 = idx_ref[1]
    mid = pl.ds(h, cells_x)
    lo_p = pl.ds(0, h)
    hi_p = pl.ds(h + cells_x, h)
    own_r = pl.ds(ROW_PAD, cells_y)
    copies = []
    for a, dst, own in ((2, sg, own_sig), (0, ph, own_phi), (1, rs, own_rhs)):
        pieces = [
            (own, dst.at[mid, own_r]),
            (x_lo.at[a], dst.at[lo_p, own_r]),
            (x_hi.at[a], dst.at[hi_p, own_r]),
        ]
        for r in range(h):
            lo_row = ROW_PAD - h + r
            hi_row = ROW_PAD + cells_y + r
            pieces += [
                (y_lo.at[a, r], dst.at[mid, lo_row]),
                (y_hi.at[a, r], dst.at[mid, hi_row]),
                (c_lo.at[0, a, r], dst.at[lo_p, lo_row]),
                (c_lo.at[1, a, r], dst.at[lo_p, hi_row]),
                (c_hi.at[0, a, r], dst.at[hi_p, lo_row]),
                (c_hi.at[1, a, r], dst.at[hi_p, hi_row]),
            ]
        for src_ref, dst_ref in pieces:
            cp = pltpu.make_async_copy(src_ref, dst_ref, sems.at[len(copies)])
            cp.start()
            copies.append(cp)
    per_array = len(copies) // 3
    for cp in copies[:per_array]:
        cp.wait()
    row = lax.broadcasted_iota(jnp.int32, (rows, lanes), 0)
    lane = lax.broadcasted_iota(jnp.int32, (rows, lanes), 1)
    gy = gy0 + row
    iny = (gy >= 0) & (gy < ny)
    par[...] = jnp.where(iny, (gy + lane) & 1, 2)

    def faces_x(i, carry):
        gx = gx0 + i
        ok = (gx >= 0) & (gx + 1 < nx)
        s0 = sg[i]
        s1 = sg[i + 1]
        gyv = gy0 + lax.broadcasted_iota(jnp.int32, (rows, lanes), 0)
        inside = (gyv >= 0) & (gyv < ny) & ok
        fx[i] = jnp.where(inside, harmonic(s0, s1), 0.0)
        return carry

    lax.fori_loop(0, planes - 1, faces_x, 0, unroll=2)

    def faces_yz(i, carry):
        gx = gx0 + i
        inx = (gx >= 0) & (gx < nx)
        r = lax.broadcasted_iota(jnp.int32, (rows, lanes), 0)
        k = lax.broadcasted_iota(jnp.int32, (rows, lanes), 1)
        gyv = gy0 + r
        inyv = (gyv >= 0) & (gyv < ny)
        s = sg[i]
        s_yu = pltpu.roll(s, rows - 1, 0)
        s_zu = pltpu.roll(s, lanes - 1, 1)
        wy = jnp.where(inx & (gyv >= 0) & (gyv + 1 < ny), harmonic(s, s_yu), 0.0)
        wz = jnp.where(inx & inyv & (k < lanes - 1), harmonic(s, s_zu), 0.0)
        wy_lo = pltpu.roll(wy, 1, 0)
        wz_lo = pltpu.roll(wz, 1, 1)
        fy[i] = wy
        fz[i] = wz
        fzl[i] = wz_lo
        wxl = jnp.where(gx == 0, s, fx[i - 1])
        wxu = jnp.where(gx == nx - 1, s, fx[i])
        wyl = jnp.where(gyv == 0, s, wy_lo)
        wyu = jnp.where(gyv == ny - 1, s, wy)
        wzl = jnp.where(k == 0, s, wz_lo)
        wzu = jnp.where(k == lanes - 1, s, wz)
        d = wxl + wxu + wyl + wyu + wzl + wzu
        dg[i] = d
        inv[i] = 1.0 / d
        sg[i] = wy_lo
        return carry

    lax.fori_loop(1, planes - 1, faces_yz, 0, unroll=2)
    for cp in copies[per_array:]:
        cp.wait()

    def coupled_sum(i, pc):
        wy = fy[i]
        wz = fz[i]
        terms = (
            (fx[i - 1], ph[i - 1]),
            (fx[i], ph[i + 1]),
            (sg[i], pltpu.roll(pc, 1, 0)),
            (wy, pltpu.roll(pc, rows - 1, 0)),
            (fzl[i], pltpu.roll(pc, 1, 1)),
            (wz, pltpu.roll(pc, lanes - 1, 1)),
        )
        return terms

    for turn in range(2 * SWEEPS):
        colour = turn % 2

        def relax(i, carry, colour=colour):
            gx = gx0 + i
            inx = (gx >= 0) & (gx < nx)
            target = jnp.where(inx, (gx + colour) & 1, 3)
            pc = ph[i]
            summed = rs[i]
            for w, nb in coupled_sum(i, pc):
                summed = summed + w * nb
            ph[i] = jnp.where(par[...] == target, summed * inv[i], pc)
            return carry

        lax.fori_loop(turn + 1, planes - 1 - turn, relax, 0, unroll=2)

    own_rows = rows - 2 * ROW_PAD
    half_rows = own_rows // 2

    def defect_plane(i):
        pc = ph[i]
        terms = coupled_sum(i, pc)
        coupled = terms[0][0] * terms[0][1]
        for w, nb in terms[1:]:
            coupled = coupled + w * nb
        d = rs[i] - (dg[i] * pc - coupled)
        phi_out[i - HALO] = pc[ROW_PAD:ROW_PAD + own_rows]
        return d[ROW_PAD:ROW_PAD + own_rows]

    def restrict(j, carry):
        i = HALO + 2 * j
        pair = defect_plane(i) + defect_plane(i + 1)
        halves = []
        for q in range(lanes // 128):
            pair_buf[q] = pair[:, q * 128:(q + 1) * 128]
            even = pair_buf[q, pl.ds(0, half_rows, stride=2), :]
            odd = pair_buf[q, pl.ds(1, half_rows, stride=2), :]
            halves.append(even + odd)
        y_sums[pl.ds(pl.multiple_of(j * half_rows, half_rows), half_rows), :] = (
            jnp.concatenate(halves, axis=1))
        return carry

    lax.fori_loop(0, (planes - 2 * HALO) // 2, restrict, 0)
    coarse_out[...] = 0.125 * jnp.dot(
        y_sums[...], pz_ref[...], precision=lax.Precision.HIGHEST,
        preferred_element_type=jnp.float32)


def exchange(arrays):
    boxes = lax.axis_size("box")
    grps = lax.axis_size("grp")
    h = HALO
    down_box = [(i, i + 1) for i in range(boxes - 1)]
    up_box = [(i + 1, i) for i in range(boxes - 1)]
    down_grp = [(i, i + 1) for i in range(grps - 1)]
    up_grp = [(i + 1, i) for i in range(grps - 1)]
    rows_major = lambda part: jnp.swapaxes(part, 0, 1)
    y_lo = lax.ppermute(jnp.stack([rows_major(a[:, -h:]) for a in arrays]), "grp", down_grp)
    y_hi = lax.ppermute(jnp.stack([rows_major(a[:, :h]) for a in arrays]), "grp", up_grp)
    x_lo = lax.ppermute(jnp.stack([a[-h:] for a in arrays]), "box", down_box)
    x_hi = lax.ppermute(jnp.stack([a[:h] for a in arrays]), "box", up_box)
    c_lo = lax.ppermute(jnp.stack([y_lo[:, :, -h:], y_hi[:, :, -h:]]), "box", down_box)
    c_hi = lax.ppermute(jnp.stack([y_lo[:, :, :h], y_hi[:, :, :h]]), "box", up_box)
    return x_lo, x_hi, y_lo, y_hi, c_lo, c_hi


def local(phi_start, right_side, sigma):
    cells_x, cells_y, cells_z = phi_start.shape
    boxes = lax.axis_size("box")
    grps = lax.axis_size("grp")
    nx = cells_x * boxes
    ny = cells_y * grps
    b = lax.axis_index("box")
    g = lax.axis_index("grp")
    pieces = exchange((phi_start, right_side, sigma))
    planes = cells_x + 2 * HALO
    rows = cells_y + 2 * ROW_PAD
    lanes = cells_z
    idx = jnp.stack([b * cells_x - HALO, g * cells_y - ROW_PAD]).astype(jnp.int32)
    pz = jnp.asarray(np.kron(np.eye(cells_z // 2), np.ones((2, 1))), jnp.float32)
    full = pl.BlockSpec(memory_space=pltpu.MemorySpace.VMEM)
    anywhere = pl.BlockSpec(memory_space=pltpu.MemorySpace.HBM)
    big = pltpu.VMEM((planes, rows, lanes), jnp.float32)
    phi_smooth, coarse = pl.pallas_call(
        functools.partial(smooth_kernel, nx, ny),
        out_shape=(
            jax.ShapeDtypeStruct((cells_x, cells_y, cells_z), jnp.float32),
            jax.ShapeDtypeStruct((cells_x // 2 * (cells_y // 2), cells_z // 2), jnp.float32),
        ),
        in_specs=[pl.BlockSpec(memory_space=pltpu.MemorySpace.SMEM), full]
        + [anywhere] * 9,
        out_specs=(full, full),
        scratch_shapes=[big] * 9
        + [
            pltpu.VMEM((rows, lanes), jnp.int32),
            pltpu.VMEM((lanes // 128, cells_y, 128), jnp.float32),
            pltpu.VMEM((cells_x // 2 * (cells_y // 2), lanes), jnp.float32),
            pltpu.SemaphoreType.DMA((3 * (3 + 6 * HALO),)),
        ],
        compiler_params=pltpu.CompilerParams(vmem_limit_bytes=60 * 1024 * 1024),
    )(idx, pz, phi_start, right_side, sigma, *pieces)
    coarse = coarse.reshape(cells_x // 2, cells_y // 2, cells_z // 2)
    if grps == 2:
        other = lax.ppermute(coarse, "grp", [(0, 1), (1, 0)])
        group_coarse = jnp.where(
            g == 0,
            jnp.concatenate([coarse, other], axis=1),
            jnp.concatenate([other, coarse], axis=1),
        )
    else:
        group_coarse = lax.all_gather(coarse, "grp", axis=1, tiled=True)
    return phi_smooth, group_coarse


def solution(mesh):
    placed = (P("box", "grp", None), P("box", "grp", None), P("box", "grp", None))
    return jax.shard_map(
        local,
        mesh=mesh,
        in_specs=placed,
        out_specs=(P("box", "grp", None), P("box", None, None)),
        check_vma=False,
    )
```

```python
import functools

import jax
import jax.numpy as jnp
import numpy as np
from jax import lax
from jax.experimental import pallas as pl
from jax.experimental.pallas import tpu as pltpu
from jax.sharding import PartitionSpec as P

SWEEPS = 2
HALO = 2 * SWEEPS + 1
ROW_PAD = 8


def harmonic(s, t):
    return 2.0 * s * t / (s + t)


def smooth_kernel(nx, ny, idx_ref, pz_ref, own_phi, own_rhs, own_sig,
                  x_lo, x_hi, y_lo, y_hi,
                  phi_out, coarse_out, ph, rs, sg, fx, fy, fz, fzl, dg, inv, par,
                  pair_buf, y_sums, sems):
    planes, rows, lanes = ph.shape
    h = HALO
    cells_x = planes - 2 * h
    cells_y = rows - 2 * ROW_PAD
    gx0 = idx_ref[0]
    gy0 = idx_ref[1]
    mid = pl.ds(h, cells_x)
    lo_p = pl.ds(0, h)
    hi_p = pl.ds(h + cells_x, h)
    own_r = pl.ds(ROW_PAD, cells_y)
    copies = []
    for a, dst, own in ((2, sg, own_sig), (0, ph, own_phi), (1, rs, own_rhs)):
        pieces = [
            (own, dst.at[mid, own_r]),
            (x_lo.at[a], dst.at[lo_p, own_r]),
            (x_hi.at[a], dst.at[hi_p, own_r]),
        ]
        for r in range(h):
            lo_row = ROW_PAD - h + r
            hi_row = ROW_PAD + cells_y + r
            pieces += [
                (y_lo.at[a, r], dst.at[:, lo_row]),
                (y_hi.at[a, r], dst.at[:, hi_row]),
            ]
        for src_ref, dst_ref in pieces:
            cp = pltpu.make_async_copy(src_ref, dst_ref, sems.at[len(copies)])
            cp.start()
            copies.append(cp)
    per_array = len(copies) // 3
    for cp in copies[:per_array]:
        cp.wait()
    row = lax.broadcasted_iota(jnp.int32, (rows, lanes), 0)
    lane = lax.broadcasted_iota(jnp.int32, (rows, lanes), 1)
    gy = gy0 + row
    iny = (gy >= 0) & (gy < ny)
    par[...] = jnp.where(iny, (gy + lane) & 1, 2)

    def faces_x(i, carry):
        gx = gx0 + i
        ok = (gx >= 0) & (gx + 1 < nx)
        s0 = sg[i]
        s1 = sg[i + 1]
        gyv = gy0 + lax.broadcasted_iota(jnp.int32, (rows, lanes), 0)
        inside = (gyv >= 0) & (gyv < ny) & ok
        fx[i] = jnp.where(inside, harmonic(s0, s1), 0.0)
        return carry

    lax.fori_loop(0, planes - 1, faces_x, 0, unroll=2)

    def faces_yz(i, carry):
        gx = gx0 + i
        inx = (gx >= 0) & (gx < nx)
        r = lax.broadcasted_iota(jnp.int32, (rows, lanes), 0)
        k = lax.broadcasted_iota(jnp.int32, (rows, lanes), 1)
        gyv = gy0 + r
        inyv = (gyv >= 0) & (gyv < ny)
        s = sg[i]
        s_yu = pltpu.roll(s, rows - 1, 0)
        s_zu = pltpu.roll(s, lanes - 1, 1)
        wy = jnp.where(inx & (gyv >= 0) & (gyv + 1 < ny), harmonic(s, s_yu), 0.0)
        wz = jnp.where(inx & inyv & (k < lanes - 1), harmonic(s, s_zu), 0.0)
        wy_lo = pltpu.roll(wy, 1, 0)
        wz_lo = pltpu.roll(wz, 1, 1)
        fy[i] = wy
        fz[i] = wz
        fzl[i] = wz_lo
        wxl = jnp.where(gx == 0, s, fx[i - 1])
        wxu = jnp.where(gx == nx - 1, s, fx[i])
        wyl = jnp.where(gyv == 0, s, wy_lo)
        wyu = jnp.where(gyv == ny - 1, s, wy)
        wzl = jnp.where(k == 0, s, wz_lo)
        wzu = jnp.where(k == lanes - 1, s, wz)
        d = wxl + wxu + wyl + wyu + wzl + wzu
        dg[i] = d
        inv[i] = 1.0 / d
        sg[i] = wy_lo
        return carry

    lax.fori_loop(1, planes - 1, faces_yz, 0, unroll=2)
    for cp in copies[per_array:]:
        cp.wait()

    def coupled_sum(i, pc):
        wy = fy[i]
        wz = fz[i]
        terms = (
            (fx[i - 1], ph[i - 1]),
            (fx[i], ph[i + 1]),
            (sg[i], pltpu.roll(pc, 1, 0)),
            (wy, pltpu.roll(pc, rows - 1, 0)),
            (fzl[i], pltpu.roll(pc, 1, 1)),
            (wz, pltpu.roll(pc, lanes - 1, 1)),
        )
        return terms

    for turn in range(2 * SWEEPS):
        colour = turn % 2

        def relax(i, carry, colour=colour):
            gx = gx0 + i
            inx = (gx >= 0) & (gx < nx)
            target = jnp.where(inx, (gx + colour) & 1, 3)
            pc = ph[i]
            summed = rs[i]
            for w, nb in coupled_sum(i, pc):
                summed = summed + w * nb
            ph[i] = jnp.where(par[...] == target, summed * inv[i], pc)
            return carry

        lax.fori_loop(turn + 1, planes - 1 - turn, relax, 0, unroll=2)

    own_rows = rows - 2 * ROW_PAD
    half_rows = own_rows // 2

    def defect_plane(i):
        pc = ph[i]
        terms = coupled_sum(i, pc)
        coupled = terms[0][0] * terms[0][1]
        for w, nb in terms[1:]:
            coupled = coupled + w * nb
        d = rs[i] - (dg[i] * pc - coupled)
        phi_out[i - HALO] = pc[ROW_PAD:ROW_PAD + own_rows]
        return d[ROW_PAD:ROW_PAD + own_rows]

    def restrict(j, carry):
        i = HALO + 2 * j
        pair = defect_plane(i) + defect_plane(i + 1)
        halves = []
        for q in range(lanes // 128):
            pair_buf[q] = pair[:, q * 128:(q + 1) * 128]
            even = pair_buf[q, pl.ds(0, half_rows, stride=2), :]
            odd = pair_buf[q, pl.ds(1, half_rows, stride=2), :]
            halves.append(even + odd)
        y_sums[pl.ds(pl.multiple_of(j * half_rows, half_rows), half_rows), :] = (
            jnp.concatenate(halves, axis=1))
        return carry

    lax.fori_loop(0, (planes - 2 * HALO) // 2, restrict, 0)
    coarse_out[...] = 0.125 * jnp.dot(
        y_sums[...], pz_ref[...], precision=lax.Precision.HIGHEST,
        preferred_element_type=jnp.float32)


def exchange(arrays):
    boxes = lax.axis_size("box")
    grps = lax.axis_size("grp")
    h = HALO
    down_box = [(i, i + 1) for i in range(boxes - 1)]
    up_box = [(i + 1, i) for i in range(boxes - 1)]
    down_grp = [(i, i + 1) for i in range(grps - 1)]
    up_grp = [(i + 1, i) for i in range(grps - 1)]
    x_lo = lax.ppermute(jnp.stack([a[-h:] for a in arrays]), "box", down_box)
    x_hi = lax.ppermute(jnp.stack([a[:h] for a in arrays]), "box", up_box)
    own = jnp.stack(arrays)

    def y_part(rows):
        part = jnp.concatenate([x_lo[:, :, rows], own[:, :, rows], x_hi[:, :, rows]], axis=1)
        return jnp.swapaxes(part, 1, 2)

    y_lo = lax.ppermute(y_part(slice(-h, None)), "grp", down_grp)
    y_hi = lax.ppermute(y_part(slice(0, h)), "grp", up_grp)
    return x_lo, x_hi, y_lo, y_hi


def local(phi_start, right_side, sigma):
    cells_x, cells_y, cells_z = phi_start.shape
    boxes = lax.axis_size("box")
    grps = lax.axis_size("grp")
    nx = cells_x * boxes
    ny = cells_y * grps
    b = lax.axis_index("box")
    g = lax.axis_index("grp")
    pieces = exchange((phi_start, right_side, sigma))
    planes = cells_x + 2 * HALO
    rows = cells_y + 2 * ROW_PAD
    lanes = cells_z
    idx = jnp.stack([b * cells_x - HALO, g * cells_y - ROW_PAD]).astype(jnp.int32)
    pz = jnp.asarray(np.kron(np.eye(cells_z // 2), np.ones((2, 1))), jnp.float32)
    full = pl.BlockSpec(memory_space=pltpu.MemorySpace.VMEM)
    anywhere = pl.BlockSpec(memory_space=pltpu.MemorySpace.HBM)
    big = pltpu.VMEM((planes, rows, lanes), jnp.float32)
    phi_smooth, coarse = pl.pallas_call(
        functools.partial(smooth_kernel, nx, ny),
        out_shape=(
            jax.ShapeDtypeStruct((cells_x, cells_y, cells_z), jnp.float32),
            jax.ShapeDtypeStruct((cells_x // 2 * (cells_y // 2), cells_z // 2), jnp.float32),
        ),
        in_specs=[pl.BlockSpec(memory_space=pltpu.MemorySpace.SMEM), full]
        + [anywhere] * 7,
        out_specs=(full, full),
        scratch_shapes=[big] * 9
        + [
            pltpu.VMEM((rows, lanes), jnp.int32),
            pltpu.VMEM((lanes // 128, cells_y, 128), jnp.float32),
            pltpu.VMEM((cells_x // 2 * (cells_y // 2), lanes), jnp.float32),
            pltpu.SemaphoreType.DMA((3 * (3 + 2 * HALO),)),
        ],
        compiler_params=pltpu.CompilerParams(vmem_limit_bytes=60 * 1024 * 1024),
    )(idx, pz, phi_start, right_side, sigma, *pieces)
    coarse = coarse.reshape(cells_x // 2, cells_y // 2, cells_z // 2)
    if grps == 2:
        other = lax.ppermute(coarse, "grp", [(0, 1), (1, 0)])
        group_coarse = jnp.where(
            g == 0,
            jnp.concatenate([coarse, other], axis=1),
            jnp.concatenate([other, coarse], axis=1),
        )
    else:
        group_coarse = lax.all_gather(coarse, "grp", axis=1, tiled=True)
    return phi_smooth, group_coarse


def solution(mesh):
    placed = (P("box", "grp", None), P("box", "grp", None), P("box", "grp", None))
    return jax.shard_map(
        local,
        mesh=mesh,
        in_specs=placed,
        out_specs=(P("box", "grp", None), P("box", None, None)),
        check_vma=False,
    )
```

```python
import functools

import jax
import jax.numpy as jnp
import numpy as np
from jax import lax
from jax.experimental import pallas as pl
from jax.experimental.pallas import tpu as pltpu
from jax.sharding import PartitionSpec as P

SWEEPS = 2
HALO = 2 * SWEEPS + 1
ROW_PAD = 8


def harmonic(s, t):
    return 2.0 * s * t / (s + t)


def smooth_kernel(nx, ny, idx_ref, pz_ref, own_phi, own_rhs, own_sig,
                  x_lo, x_hi, y_lo, y_hi, c_lo, c_hi,
                  phi_out, coarse_out, ph, rs, sg, fx, fy, fz, fzl, dg, inv, par,
                  pair_buf, y_sums, sems):
    planes, rows, lanes = ph.shape
    h = HALO
    cells_x = planes - 2 * h
    cells_y = rows - 2 * ROW_PAD
    gx0 = idx_ref[0]
    gy0 = idx_ref[1]
    mid = pl.ds(h, cells_x)
    lo_p = pl.ds(0, h)
    hi_p = pl.ds(h + cells_x, h)
    own_r = pl.ds(ROW_PAD, cells_y)
    copies = []
    for a, dst, own in ((2, sg, own_sig), (0, ph, own_phi), (1, rs, own_rhs)):
        pieces = [
            (own, dst.at[mid, own_r]),
            (x_lo.at[a], dst.at[lo_p, own_r]),
            (x_hi.at[a], dst.at[hi_p, own_r]),
        ]
        for r in range(h):
            lo_row = ROW_PAD - h + r
            hi_row = ROW_PAD + cells_y + r
            pieces += [
                (y_lo.at[a, r], dst.at[mid, lo_row]),
                (y_hi.at[a, r], dst.at[mid, hi_row]),
                (c_lo.at[0, a, r], dst.at[lo_p, lo_row]),
                (c_lo.at[1, a, r], dst.at[hi_p, lo_row]),
                (c_hi.at[0, a, r], dst.at[lo_p, hi_row]),
                (c_hi.at[1, a, r], dst.at[hi_p, hi_row]),
            ]
        for src_ref, dst_ref in pieces:
            cp = pltpu.make_async_copy(src_ref, dst_ref, sems.at[len(copies)])
            cp.start()
            copies.append(cp)
    per_array = len(copies) // 3
    for cp in copies[:per_array]:
        cp.wait()
    row = lax.broadcasted_iota(jnp.int32, (rows, lanes), 0)
    lane = lax.broadcasted_iota(jnp.int32, (rows, lanes), 1)
    gy = gy0 + row
    iny = (gy >= 0) & (gy < ny)
    par[...] = jnp.where(iny, (gy + lane) & 1, 2)

    def faces_x(i, carry):
        gx = gx0 + i
        ok = (gx >= 0) & (gx + 1 < nx)
        s0 = sg[i]
        s1 = sg[i + 1]
        gyv = gy0 + lax.broadcasted_iota(jnp.int32, (rows, lanes), 0)
        inside = (gyv >= 0) & (gyv < ny) & ok
        fx[i] = jnp.where(inside, harmonic(s0, s1), 0.0)
        return carry

    lax.fori_loop(0, planes - 1, faces_x, 0, unroll=2)

    def faces_yz(i, carry):
        gx = gx0 + i
        inx = (gx >= 0) & (gx < nx)
        r = lax.broadcasted_iota(jnp.int32, (rows, lanes), 0)
        k = lax.broadcasted_iota(jnp.int32, (rows, lanes), 1)
        gyv = gy0 + r
        inyv = (gyv >= 0) & (gyv < ny)
        s = sg[i]
        s_yu = pltpu.roll(s, rows - 1, 0)
        s_zu = pltpu.roll(s, lanes - 1, 1)
        wy = jnp.where(inx & (gyv >= 0) & (gyv + 1 < ny), harmonic(s, s_yu), 0.0)
        wz = jnp.where(inx & inyv & (k < lanes - 1), harmonic(s, s_zu), 0.0)
        wy_lo = pltpu.roll(wy, 1, 0)
        wz_lo = pltpu.roll(wz, 1, 1)
        fy[i] = wy
        fz[i] = wz
        fzl[i] = wz_lo
        wxl = jnp.where(gx == 0, s, fx[i - 1])
        wxu = jnp.where(gx == nx - 1, s, fx[i])
        wyl = jnp.where(gyv == 0, s, wy_lo)
        wyu = jnp.where(gyv == ny - 1, s, wy)
        wzl = jnp.where(k == 0, s, wz_lo)
        wzu = jnp.where(k == lanes - 1, s, wz)
        d = wxl + wxu + wyl + wyu + wzl + wzu
        dg[i] = d
        inv[i] = 1.0 / d
        sg[i] = wy_lo
        return carry

    lax.fori_loop(1, planes - 1, faces_yz, 0, unroll=2)
    for cp in copies[per_array:]:
        cp.wait()

    def coupled_sum(i, pc):
        wy = fy[i]
        wz = fz[i]
        terms = (
            (fx[i - 1], ph[i - 1]),
            (fx[i], ph[i + 1]),
            (sg[i], pltpu.roll(pc, 1, 0)),
            (wy, pltpu.roll(pc, rows - 1, 0)),
            (fzl[i], pltpu.roll(pc, 1, 1)),
            (wz, pltpu.roll(pc, lanes - 1, 1)),
        )
        return terms

    for turn in range(2 * SWEEPS):
        colour = turn % 2

        def relax(i, carry, colour=colour):
            gx = gx0 + i
            inx = (gx >= 0) & (gx < nx)
            target = jnp.where(inx, (gx + colour) & 1, 3)
            pc = ph[i]
            summed = rs[i]
            for w, nb in coupled_sum(i, pc):
                summed = summed + w * nb
            ph[i] = jnp.where(par[...] == target, summed * inv[i], pc)
            return carry

        lax.fori_loop(turn + 1, planes - 1 - turn, relax, 0, unroll=2)

    own_rows = rows - 2 * ROW_PAD
    half_rows = own_rows // 2

    def defect_plane(i):
        pc = ph[i]
        terms = coupled_sum(i, pc)
        coupled = terms[0][0] * terms[0][1]
        for w, nb in terms[1:]:
            coupled = coupled + w * nb
        d = rs[i] - (dg[i] * pc - coupled)
        phi_out[i - HALO] = pc[ROW_PAD:ROW_PAD + own_rows]
        return d[ROW_PAD:ROW_PAD + own_rows]

    def restrict(j, carry):
        i = HALO + 2 * j
        pair = defect_plane(i) + defect_plane(i + 1)
        halves = []
        for q in range(lanes // 128):
            pair_buf[q] = pair[:, q * 128:(q + 1) * 128]
            even = pair_buf[q, pl.ds(0, half_rows, stride=2), :]
            odd = pair_buf[q, pl.ds(1, half_rows, stride=2), :]
            halves.append(even + odd)
        y_sums[pl.ds(pl.multiple_of(j * half_rows, half_rows), half_rows), :] = (
            jnp.concatenate(halves, axis=1))
        return carry

    lax.fori_loop(0, (planes - 2 * HALO) // 2, restrict, 0)
    coarse_out[...] = 0.125 * jnp.dot(
        y_sums[...], pz_ref[...], precision=lax.Precision.HIGHEST,
        preferred_element_type=jnp.float32)


def exchange(arrays):
    boxes = lax.axis_size("box")
    grps = lax.axis_size("grp")
    h = HALO
    down_box = [(i, i + 1) for i in range(boxes - 1)]
    up_box = [(i + 1, i) for i in range(boxes - 1)]
    down_grp = [(i, i + 1) for i in range(grps - 1)]
    up_grp = [(i + 1, i) for i in range(grps - 1)]
    rows_major = lambda part: jnp.swapaxes(part, 0, 1)
    y_lo = lax.ppermute(jnp.stack([rows_major(a[:, -h:]) for a in arrays]), "grp", down_grp)
    y_hi = lax.ppermute(jnp.stack([rows_major(a[:, :h]) for a in arrays]), "grp", up_grp)
    x_lo = lax.ppermute(jnp.stack([a[-h:] for a in arrays]), "box", down_box)
    x_hi = lax.ppermute(jnp.stack([a[:h] for a in arrays]), "box", up_box)
    c_lo = lax.ppermute(jnp.stack([jnp.swapaxes(x_lo[:, :, -h:], 1, 2),
                                   jnp.swapaxes(x_hi[:, :, -h:], 1, 2)]), "grp", down_grp)
    c_hi = lax.ppermute(jnp.stack([jnp.swapaxes(x_lo[:, :, :h], 1, 2),
                                   jnp.swapaxes(x_hi[:, :, :h], 1, 2)]), "grp", up_grp)
    return x_lo, x_hi, y_lo, y_hi, c_lo, c_hi


def local(phi_start, right_side, sigma):
    cells_x, cells_y, cells_z = phi_start.shape
    boxes = lax.axis_size("box")
    grps = lax.axis_size("grp")
    nx = cells_x * boxes
    ny = cells_y * grps
    b = lax.axis_index("box")
    g = lax.axis_index("grp")
    pieces = exchange((phi_start, right_side, sigma))
    planes = cells_x + 2 * HALO
    rows = cells_y + 2 * ROW_PAD
    lanes = cells_z
    idx = jnp.stack([b * cells_x - HALO, g * cells_y - ROW_PAD]).astype(jnp.int32)
    pz = jnp.asarray(np.kron(np.eye(cells_z // 2), np.ones((2, 1))), jnp.float32)
    full = pl.BlockSpec(memory_space=pltpu.MemorySpace.VMEM)
    anywhere = pl.BlockSpec(memory_space=pltpu.MemorySpace.HBM)
    big = pltpu.VMEM((planes, rows, lanes), jnp.float32)
    phi_smooth, coarse = pl.pallas_call(
        functools.partial(smooth_kernel, nx, ny),
        out_shape=(
            jax.ShapeDtypeStruct((cells_x, cells_y, cells_z), jnp.float32),
            jax.ShapeDtypeStruct((cells_x // 2 * (cells_y // 2), cells_z // 2), jnp.float32),
        ),
        in_specs=[pl.BlockSpec(memory_space=pltpu.MemorySpace.SMEM), full]
        + [anywhere] * 9,
        out_specs=(full, full),
        scratch_shapes=[big] * 9
        + [
            pltpu.VMEM((rows, lanes), jnp.int32),
            pltpu.VMEM((lanes // 128, cells_y, 128), jnp.float32),
            pltpu.VMEM((cells_x // 2 * (cells_y // 2), lanes), jnp.float32),
            pltpu.SemaphoreType.DMA((3 * (3 + 6 * HALO),)),
        ],
        compiler_params=pltpu.CompilerParams(vmem_limit_bytes=60 * 1024 * 1024),
    )(idx, pz, phi_start, right_side, sigma, *pieces)
    coarse = coarse.reshape(cells_x // 2, cells_y // 2, cells_z // 2)
    if grps == 2:
        other = lax.ppermute(coarse, "grp", [(0, 1), (1, 0)])
        group_coarse = jnp.where(
            g == 0,
            jnp.concatenate([coarse, other], axis=1),
            jnp.concatenate([other, coarse], axis=1),
        )
    else:
        group_coarse = lax.all_gather(coarse, "grp", axis=1, tiled=True)
    return phi_smooth, group_coarse


def solution(mesh):
    placed = (P("box", "grp", None), P("box", "grp", None), P("box", "grp", None))
    return jax.shard_map(
        local,
        mesh=mesh,
        in_specs=placed,
        out_specs=(P("box", "grp", None), P("box", None, None)),
        check_vma=False,
    )
```

```python
import functools

import jax
import jax.numpy as jnp
import numpy as np
from jax import lax
from jax.experimental import pallas as pl
from jax.experimental.pallas import tpu as pltpu
from jax.sharding import PartitionSpec as P

SWEEPS = 2
HALO = 2 * SWEEPS + 1
ROW_PAD = 8


def harmonic(s, t):
    return 2.0 * s * t / (s + t)


def smooth_kernel(nx, ny, idx_ref, pz_ref, own_phi, own_rhs, own_sig,
                  x_lo, x_hi, y_lo, y_hi, c_lo, c_hi,
                  phi_out, coarse_out, group_out, ph, rs, sg, fx, fy, fz, fzl, dg, inv, par,
                  pair_buf, y_sums, sems):
    planes, rows, lanes = ph.shape
    h = HALO
    cells_x = planes - 2 * h
    cells_y = rows - 2 * ROW_PAD
    gx0 = idx_ref[0]
    gy0 = idx_ref[1]
    mid = pl.ds(h, cells_x)
    lo_p = pl.ds(0, h)
    hi_p = pl.ds(h + cells_x, h)
    own_r = pl.ds(ROW_PAD, cells_y)
    copies = []
    for a, dst, own in ((2, sg, own_sig), (0, ph, own_phi), (1, rs, own_rhs)):
        pieces = [
            (own, dst.at[mid, own_r]),
            (x_lo.at[a], dst.at[lo_p, own_r]),
            (x_hi.at[a], dst.at[hi_p, own_r]),
        ]
        for r in range(h):
            lo_row = ROW_PAD - h + r
            hi_row = ROW_PAD + cells_y + r
            pieces += [
                (y_lo.at[a, r], dst.at[mid, lo_row]),
                (y_hi.at[a, r], dst.at[mid, hi_row]),
                (c_lo.at[0, a, r], dst.at[lo_p, lo_row]),
                (c_lo.at[1, a, r], dst.at[hi_p, lo_row]),
                (c_hi.at[0, a, r], dst.at[lo_p, hi_row]),
                (c_hi.at[1, a, r], dst.at[hi_p, hi_row]),
            ]
        for src_ref, dst_ref in pieces:
            cp = pltpu.make_async_copy(src_ref, dst_ref, sems.at[len(copies)])
            cp.start()
            copies.append(cp)
    per_array = len(copies) // 3
    for cp in copies[:per_array]:
        cp.wait()
    row = lax.broadcasted_iota(jnp.int32, (rows, lanes), 0)
    lane = lax.broadcasted_iota(jnp.int32, (rows, lanes), 1)
    gy = gy0 + row
    iny = (gy >= 0) & (gy < ny)
    par[...] = jnp.where(iny, (gy + lane) & 1, 2)

    def faces_x(i, carry):
        gx = gx0 + i
        ok = (gx >= 0) & (gx + 1 < nx)
        s0 = sg[i]
        s1 = sg[i + 1]
        gyv = gy0 + lax.broadcasted_iota(jnp.int32, (rows, lanes), 0)
        inside = (gyv >= 0) & (gyv < ny) & ok
        fx[i] = jnp.where(inside, harmonic(s0, s1), 0.0)
        return carry

    lax.fori_loop(0, planes - 1, faces_x, 0, unroll=2)

    def faces_yz(i, carry):
        gx = gx0 + i
        inx = (gx >= 0) & (gx < nx)
        r = lax.broadcasted_iota(jnp.int32, (rows, lanes), 0)
        k = lax.broadcasted_iota(jnp.int32, (rows, lanes), 1)
        gyv = gy0 + r
        inyv = (gyv >= 0) & (gyv < ny)
        s = sg[i]
        s_yu = pltpu.roll(s, rows - 1, 0)
        s_zu = pltpu.roll(s, lanes - 1, 1)
        wy = jnp.where(inx & (gyv >= 0) & (gyv + 1 < ny), harmonic(s, s_yu), 0.0)
        wz = jnp.where(inx & inyv & (k < lanes - 1), harmonic(s, s_zu), 0.0)
        wy_lo = pltpu.roll(wy, 1, 0)
        wz_lo = pltpu.roll(wz, 1, 1)
        fy[i] = wy
        fz[i] = wz
        fzl[i] = wz_lo
        wxl = jnp.where(gx == 0, s, fx[i - 1])
        wxu = jnp.where(gx == nx - 1, s, fx[i])
        wyl = jnp.where(gyv == 0, s, wy_lo)
        wyu = jnp.where(gyv == ny - 1, s, wy)
        wzl = jnp.where(k == 0, s, wz_lo)
        wzu = jnp.where(k == lanes - 1, s, wz)
        d = wxl + wxu + wyl + wyu + wzl + wzu
        dg[i] = d
        inv[i] = 1.0 / d
        sg[i] = wy_lo
        return carry

    lax.fori_loop(1, planes - 1, faces_yz, 0, unroll=2)
    for cp in copies[per_array:]:
        cp.wait()

    def coupled_sum(i, pc):
        wy = fy[i]
        wz = fz[i]
        terms = (
            (fx[i - 1], ph[i - 1]),
            (fx[i], ph[i + 1]),
            (sg[i], pltpu.roll(pc, 1, 0)),
            (wy, pltpu.roll(pc, rows - 1, 0)),
            (fzl[i], pltpu.roll(pc, 1, 1)),
            (wz, pltpu.roll(pc, lanes - 1, 1)),
        )
        return terms

    for turn in range(2 * SWEEPS):
        colour = turn % 2

        def relax(i, carry, colour=colour):
            gx = gx0 + i
            inx = (gx >= 0) & (gx < nx)
            target = jnp.where(inx, (gx + colour) & 1, 3)
            pc = ph[i]
            summed = rs[i]
            for w, nb in coupled_sum(i, pc):
                summed = summed + w * nb
            ph[i] = jnp.where(par[...] == target, summed * inv[i], pc)
            return carry

        lax.fori_loop(turn + 1, planes - 1 - turn, relax, 0, unroll=2)

    own_rows = rows - 2 * ROW_PAD
    half_rows = own_rows // 2

    def defect_plane(i):
        pc = ph[i]
        terms = coupled_sum(i, pc)
        coupled = terms[0][0] * terms[0][1]
        for w, nb in terms[1:]:
            coupled = coupled + w * nb
        d = rs[i] - (dg[i] * pc - coupled)
        phi_out[i - HALO] = pc[ROW_PAD:ROW_PAD + own_rows]
        return d[ROW_PAD:ROW_PAD + own_rows]

    def restrict(j, carry):
        i = HALO + 2 * j
        pair = defect_plane(i) + defect_plane(i + 1)
        halves = []
        for q in range(lanes // 128):
            pair_buf[q] = pair[:, q * 128:(q + 1) * 128]
            even = pair_buf[q, pl.ds(0, half_rows, stride=2), :]
            odd = pair_buf[q, pl.ds(1, half_rows, stride=2), :]
            halves.append(even + odd)
        y_sums[pl.ds(pl.multiple_of(j * half_rows, half_rows), half_rows), :] = (
            jnp.concatenate(halves, axis=1))
        return carry

    lax.fori_loop(0, (planes - 2 * HALO) // 2, restrict, 0)
    coarse = 0.125 * jnp.dot(
        y_sums[...], pz_ref[...], precision=lax.Precision.HIGHEST,
        preferred_element_type=jnp.float32)
    coarse_out[...] = coarse
    first = idx_ref[2]
    for j in range(cells_x // 2):
        group_out[j, pl.ds(first, half_rows), :] = coarse[j * half_rows:(j + 1) * half_rows]


def exchange(arrays):
    boxes = lax.axis_size("box")
    grps = lax.axis_size("grp")
    h = HALO
    down_box = [(i, i + 1) for i in range(boxes - 1)]
    up_box = [(i + 1, i) for i in range(boxes - 1)]
    down_grp = [(i, i + 1) for i in range(grps - 1)]
    up_grp = [(i + 1, i) for i in range(grps - 1)]
    rows_major = lambda part: jnp.swapaxes(part, 0, 1)
    y_lo = lax.ppermute(jnp.stack([rows_major(a[:, -h:]) for a in arrays]), "grp", down_grp)
    y_hi = lax.ppermute(jnp.stack([rows_major(a[:, :h]) for a in arrays]), "grp", up_grp)
    x_lo = lax.ppermute(jnp.stack([a[-h:] for a in arrays]), "box", down_box)
    x_hi = lax.ppermute(jnp.stack([a[:h] for a in arrays]), "box", up_box)
    c_lo = lax.ppermute(jnp.stack([jnp.swapaxes(x_lo[:, :, -h:], 1, 2),
                                   jnp.swapaxes(x_hi[:, :, -h:], 1, 2)]), "grp", down_grp)
    c_hi = lax.ppermute(jnp.stack([jnp.swapaxes(x_lo[:, :, :h], 1, 2),
                                   jnp.swapaxes(x_hi[:, :, :h], 1, 2)]), "grp", up_grp)
    return x_lo, x_hi, y_lo, y_hi, c_lo, c_hi


def local(phi_start, right_side, sigma):
    cells_x, cells_y, cells_z = phi_start.shape
    boxes = lax.axis_size("box")
    grps = lax.axis_size("grp")
    nx = cells_x * boxes
    ny = cells_y * grps
    b = lax.axis_index("box")
    g = lax.axis_index("grp")
    pieces = exchange((phi_start, right_side, sigma))
    planes = cells_x + 2 * HALO
    rows = cells_y + 2 * ROW_PAD
    lanes = cells_z
    idx = jnp.stack([b * cells_x - HALO, g * cells_y - ROW_PAD, g * (cells_y // 2)]).astype(jnp.int32)
    pz = jnp.asarray(np.kron(np.eye(cells_z // 2), np.ones((2, 1))), jnp.float32)
    full = pl.BlockSpec(memory_space=pltpu.MemorySpace.VMEM)
    anywhere = pl.BlockSpec(memory_space=pltpu.MemorySpace.HBM)
    big = pltpu.VMEM((planes, rows, lanes), jnp.float32)
    phi_smooth, coarse, group_coarse = pl.pallas_call(
        functools.partial(smooth_kernel, nx, ny),
        out_shape=(
            jax.ShapeDtypeStruct((cells_x, cells_y, cells_z), jnp.float32),
            jax.ShapeDtypeStruct((cells_x // 2 * (cells_y // 2), cells_z // 2), jnp.float32),
            jax.ShapeDtypeStruct((cells_x // 2, ny // 2, cells_z // 2), jnp.float32),
        ),
        in_specs=[pl.BlockSpec(memory_space=pltpu.MemorySpace.SMEM), full]
        + [anywhere] * 9,
        out_specs=(full, full, full),
        scratch_shapes=[big] * 9
        + [
            pltpu.VMEM((rows, lanes), jnp.int32),
            pltpu.VMEM((lanes // 128, cells_y, 128), jnp.float32),
            pltpu.VMEM((cells_x // 2 * (cells_y // 2), lanes), jnp.float32),
            pltpu.SemaphoreType.DMA((3 * (3 + 6 * HALO),)),
        ],
        compiler_params=pltpu.CompilerParams(vmem_limit_bytes=60 * 1024 * 1024),
    )(idx, pz, phi_start, right_side, sigma, *pieces)
    coarse = coarse.reshape(cells_x // 2, cells_y // 2, cells_z // 2)
    if grps == 2:
        other = lax.ppermute(coarse, "grp", [(0, 1), (1, 0)])
        group_coarse = lax.dynamic_update_slice(
            group_coarse, other, (0, (1 - g) * (cells_y // 2), 0))
    else:
        group_coarse = lax.all_gather(coarse, "grp", axis=1, tiled=True)
    return phi_smooth, group_coarse


def solution(mesh):
    placed = (P("box", "grp", None), P("box", "grp", None), P("box", "grp", None))
    return jax.shard_map(
        local,
        mesh=mesh,
        in_specs=placed,
        out_specs=(P("box", "grp", None), P("box", None, None)),
        check_vma=False,
    )
```

```python
import functools

import jax
import jax.numpy as jnp
import numpy as np
from jax import lax
from jax.experimental import pallas as pl
from jax.experimental.pallas import tpu as pltpu
from jax.sharding import PartitionSpec as P

SWEEPS = 2
HALO = 2 * SWEEPS + 1
ROW_PAD = 8
Y_ROWS = (
    ((0, (1, 2)), (0, (3, 4)), (0, (5,)))
    + tuple((2, (d,)) for d in range(1, HALO + 1))
    + tuple((1, (d,)) for d in range(1, HALO))
)


def harmonic(s, t):
    return 2.0 * s * t / (s + t)


def smooth_kernel(nx, ny, idx_ref, pz_ref, own_phi, own_rhs, own_sig,
                  x_lo, x_hi, y_lo, y_hi, c_lo, c_hi,
                  phi_out, coarse_out, group_out, ph, rs, sg, fx, fy, fz, fzl, dg, inv, par,
                  pair_buf, y_sums, sems):
    planes, rows, lanes = ph.shape
    h = HALO
    cells_x = planes - 2 * h
    cells_y = rows - 2 * ROW_PAD
    gx0 = idx_ref[0]
    gy0 = idx_ref[1]
    mid = pl.ds(h, cells_x)
    lo_p = pl.ds(0, h)
    hi_p = pl.ds(h + cells_x, h)
    own_r = pl.ds(ROW_PAD, cells_y)
    copies = []
    for a, dst, own in ((2, sg, own_sig), (0, ph, own_phi), (1, rs, own_rhs)):
        pieces = [
            (own, dst.at[mid, own_r]),
            (x_lo.at[a], dst.at[lo_p, own_r]),
            (x_hi.at[a], dst.at[hi_p, own_r]),
        ]
        for k, (which, depths) in enumerate(Y_ROWS):
            for d in depths if which == a else ():
                pieces += [
                    (y_lo.at[k], dst.at[mid, ROW_PAD - d]),
                    (y_hi.at[k], dst.at[mid, ROW_PAD + cells_y - 1 + d]),
                ]
        for r in range(h):
            lo_row = ROW_PAD - h + r
            hi_row = ROW_PAD + cells_y + r
            pieces += [
                (c_lo.at[0, a, r], dst.at[lo_p, lo_row]),
                (c_lo.at[1, a, r], dst.at[hi_p, lo_row]),
                (c_hi.at[0, a, r], dst.at[lo_p, hi_row]),
                (c_hi.at[1, a, r], dst.at[hi_p, hi_row]),
            ]
        for src_ref, dst_ref in pieces:
            cp = pltpu.make_async_copy(src_ref, dst_ref, sems.at[len(copies)])
            cp.start()
            copies.append(cp)
        if a == 2:
            per_array = len(copies)
    for cp in copies[:per_array]:
        cp.wait()
    row = lax.broadcasted_iota(jnp.int32, (rows, lanes), 0)
    lane = lax.broadcasted_iota(jnp.int32, (rows, lanes), 1)
    gy = gy0 + row
    iny = (gy >= 0) & (gy < ny)
    par[...] = jnp.where(iny, (gy + lane) & 1, 2)

    def faces_x(i, carry):
        gx = gx0 + i
        ok = (gx >= 0) & (gx + 1 < nx)
        s0 = sg[i]
        s1 = sg[i + 1]
        gyv = gy0 + lax.broadcasted_iota(jnp.int32, (rows, lanes), 0)
        inside = (gyv >= 0) & (gyv < ny) & ok
        fx[i] = jnp.where(inside, harmonic(s0, s1), 0.0)
        return carry

    lax.fori_loop(0, planes - 1, faces_x, 0, unroll=2)

    def faces_yz(i, carry):
        gx = gx0 + i
        inx = (gx >= 0) & (gx < nx)
        r = lax.broadcasted_iota(jnp.int32, (rows, lanes), 0)
        k = lax.broadcasted_iota(jnp.int32, (rows, lanes), 1)
        gyv = gy0 + r
        inyv = (gyv >= 0) & (gyv < ny)
        s = sg[i]
        s_yu = pltpu.roll(s, rows - 1, 0)
        s_zu = pltpu.roll(s, lanes - 1, 1)
        wy = jnp.where(inx & (gyv >= 0) & (gyv + 1 < ny), harmonic(s, s_yu), 0.0)
        wz = jnp.where(inx & inyv & (k < lanes - 1), harmonic(s, s_zu), 0.0)
        wy_lo = pltpu.roll(wy, 1, 0)
        wz_lo = pltpu.roll(wz, 1, 1)
        fy[i] = wy
        fz[i] = wz
        fzl[i] = wz_lo
        wxl = jnp.where(gx == 0, s, fx[i - 1])
        wxu = jnp.where(gx == nx - 1, s, fx[i])
        wyl = jnp.where(gyv == 0, s, wy_lo)
        wyu = jnp.where(gyv == ny - 1, s, wy)
        wzl = jnp.where(k == 0, s, wz_lo)
        wzu = jnp.where(k == lanes - 1, s, wz)
        d = wxl + wxu + wyl + wyu + wzl + wzu
        dg[i] = d
        inv[i] = 1.0 / d
        sg[i] = wy_lo
        return carry

    lax.fori_loop(1, planes - 1, faces_yz, 0, unroll=2)
    for cp in copies[per_array:]:
        cp.wait()

    def coupled_sum(i, pc):
        wy = fy[i]
        wz = fz[i]
        terms = (
            (fx[i - 1], ph[i - 1]),
            (fx[i], ph[i + 1]),
            (sg[i], pltpu.roll(pc, 1, 0)),
            (wy, pltpu.roll(pc, rows - 1, 0)),
            (fzl[i], pltpu.roll(pc, 1, 1)),
            (wz, pltpu.roll(pc, lanes - 1, 1)),
        )
        return terms

    for turn in range(2 * SWEEPS):
        colour = turn % 2

        def relax(i, carry, colour=colour):
            gx = gx0 + i
            inx = (gx >= 0) & (gx < nx)
            target = jnp.where(inx, (gx + colour) & 1, 3)
            pc = ph[i]
            summed = rs[i]
            for w, nb in coupled_sum(i, pc):
                summed = summed + w * nb
            ph[i] = jnp.where(par[...] == target, summed * inv[i], pc)
            return carry

        lax.fori_loop(turn + 1, planes - 1 - turn, relax, 0, unroll=2)

    own_rows = rows - 2 * ROW_PAD
    half_rows = own_rows // 2

    def defect_plane(i):
        pc = ph[i]
        terms = coupled_sum(i, pc)
        coupled = terms[0][0] * terms[0][1]
        for w, nb in terms[1:]:
            coupled = coupled + w * nb
        d = rs[i] - (dg[i] * pc - coupled)
        phi_out[i - HALO] = pc[ROW_PAD:ROW_PAD + own_rows]
        return d[ROW_PAD:ROW_PAD + own_rows]

    def restrict(j, carry):
        i = HALO + 2 * j
        pair = defect_plane(i) + defect_plane(i + 1)
        halves = []
        for q in range(lanes // 128):
            pair_buf[q] = pair[:, q * 128:(q + 1) * 128]
            even = pair_buf[q, pl.ds(0, half_rows, stride=2), :]
            odd = pair_buf[q, pl.ds(1, half_rows, stride=2), :]
            halves.append(even + odd)
        y_sums[pl.ds(pl.multiple_of(j * half_rows, half_rows), half_rows), :] = (
            jnp.concatenate(halves, axis=1))
        return carry

    lax.fori_loop(0, (planes - 2 * HALO) // 2, restrict, 0)
    coarse = 0.125 * jnp.dot(
        y_sums[...], pz_ref[...], precision=lax.Precision.HIGHEST,
        preferred_element_type=jnp.float32)
    coarse_out[...] = coarse
    first = idx_ref[2]
    for j in range(cells_x // 2):
        group_out[j, pl.ds(first, half_rows), :] = coarse[j * half_rows:(j + 1) * half_rows]


def exchange(arrays):
    boxes = lax.axis_size("box")
    grps = lax.axis_size("grp")
    h = HALO
    down_box = [(i, i + 1) for i in range(boxes - 1)]
    up_box = [(i + 1, i) for i in range(boxes - 1)]
    down_grp = [(i, i + 1) for i in range(grps - 1)]
    up_grp = [(i + 1, i) for i in range(grps - 1)]
    cells_x, cells_y, cells_z = arrays[0].shape
    gx = lax.axis_index("box") * cells_x + jnp.arange(cells_x, dtype=jnp.int32)[:, None]
    z = jnp.arange(cells_z, dtype=jnp.int32)[None, :]

    def y_piece(row_of):
        rows = []
        for which, depths in Y_ROWS:
            first = row_of(depths[0])
            part = arrays[which][:, first]
            if len(depths) == 2:
                gy = lax.axis_index("grp") * cells_y + first
                colour1 = (gx + gy + z) % 2 == 1
                part = jnp.where(colour1, part, arrays[which][:, row_of(depths[1])])
            rows.append(part)
        return jnp.stack(rows)

    y_lo = lax.ppermute(y_piece(lambda d: cells_y - d), "grp", down_grp)
    y_hi = lax.ppermute(y_piece(lambda d: d - 1), "grp", up_grp)
    x_lo = lax.ppermute(jnp.stack([a[-h:] for a in arrays]), "box", down_box)
    x_hi = lax.ppermute(jnp.stack([a[:h] for a in arrays]), "box", up_box)
    c_lo = lax.ppermute(jnp.stack([jnp.swapaxes(x_lo[:, :, -h:], 1, 2),
                                   jnp.swapaxes(x_hi[:, :, -h:], 1, 2)]), "grp", down_grp)
    c_hi = lax.ppermute(jnp.stack([jnp.swapaxes(x_lo[:, :, :h], 1, 2),
                                   jnp.swapaxes(x_hi[:, :, :h], 1, 2)]), "grp", up_grp)
    return x_lo, x_hi, y_lo, y_hi, c_lo, c_hi


def local(phi_start, right_side, sigma):
    cells_x, cells_y, cells_z = phi_start.shape
    boxes = lax.axis_size("box")
    grps = lax.axis_size("grp")
    nx = cells_x * boxes
    ny = cells_y * grps
    b = lax.axis_index("box")
    g = lax.axis_index("grp")
    pieces = exchange((phi_start, right_side, sigma))
    planes = cells_x + 2 * HALO
    rows = cells_y + 2 * ROW_PAD
    lanes = cells_z
    idx = jnp.stack([b * cells_x - HALO, g * cells_y - ROW_PAD, g * (cells_y // 2)]).astype(jnp.int32)
    pz = jnp.asarray(np.kron(np.eye(cells_z // 2), np.ones((2, 1))), jnp.float32)
    full = pl.BlockSpec(memory_space=pltpu.MemorySpace.VMEM)
    anywhere = pl.BlockSpec(memory_space=pltpu.MemorySpace.HBM)
    big = pltpu.VMEM((planes, rows, lanes), jnp.float32)
    phi_smooth, coarse, group_coarse = pl.pallas_call(
        functools.partial(smooth_kernel, nx, ny),
        out_shape=(
            jax.ShapeDtypeStruct((cells_x, cells_y, cells_z), jnp.float32),
            jax.ShapeDtypeStruct((cells_x // 2 * (cells_y // 2), cells_z // 2), jnp.float32),
            jax.ShapeDtypeStruct((cells_x // 2, ny // 2, cells_z // 2), jnp.float32),
        ),
        in_specs=[pl.BlockSpec(memory_space=pltpu.MemorySpace.SMEM), full]
        + [anywhere] * 9,
        out_specs=(full, full, full),
        scratch_shapes=[big] * 9
        + [
            pltpu.VMEM((rows, lanes), jnp.int32),
            pltpu.VMEM((lanes // 128, cells_y, 128), jnp.float32),
            pltpu.VMEM((cells_x // 2 * (cells_y // 2), lanes), jnp.float32),
            pltpu.SemaphoreType.DMA((3 * (3 + 4 * HALO) + 2 * (2 * HALO + HALO - 1),)),
        ],
        compiler_params=pltpu.CompilerParams(vmem_limit_bytes=60 * 1024 * 1024),
    )(idx, pz, phi_start, right_side, sigma, *pieces)
    coarse = coarse.reshape(cells_x // 2, cells_y // 2, cells_z // 2)
    if grps == 2:
        other = lax.ppermute(coarse, "grp", [(0, 1), (1, 0)])
        group_coarse = lax.dynamic_update_slice(
            group_coarse, other, (0, (1 - g) * (cells_y // 2), 0))
    else:
        group_coarse = lax.all_gather(coarse, "grp", axis=1, tiled=True)
    return phi_smooth, group_coarse


def solution(mesh):
    placed = (P("box", "grp", None), P("box", "grp", None), P("box", "grp", None))
    return jax.shard_map(
        local,
        mesh=mesh,
        in_specs=placed,
        out_specs=(P("box", "grp", None), P("box", None, None)),
        check_vma=False,
    )
```

```python
import functools

import jax
import jax.numpy as jnp
import numpy as np
from jax import lax
from jax.experimental import pallas as pl
from jax.experimental.pallas import tpu as pltpu
from jax.sharding import PartitionSpec as P

SWEEPS = 2
HALO = 2 * SWEEPS + 1
ROW_PAD = 8
PHI_ROWS = ((0, (1, 2)), (0, (3, 4)), (0, (5,)))
Y_ROWS = {
    "lo": PHI_ROWS + tuple((2, (d,)) for d in range(HALO, 0, -1))
    + tuple((1, (d,)) for d in range(HALO - 1, 0, -1)),
    "hi": PHI_ROWS + tuple((2, (d,)) for d in range(1, HALO + 1))
    + tuple((1, (d,)) for d in range(1, HALO)),
}


def harmonic(s, t):
    return 2.0 * s * t / (s + t)


def smooth_kernel(nx, ny, idx_ref, pz_ref, own_phi, own_rhs, own_sig,
                  x_lo, x_hi, y_lo, y_hi, c_lo, c_hi,
                  phi_out, coarse_out, group_out, ph, rs, sg, fx, fy, fz, fzl, dg, inv, par,
                  pair_buf, y_sums, sems):
    planes, rows, lanes = ph.shape
    h = HALO
    cells_x = planes - 2 * h
    cells_y = rows - 2 * ROW_PAD
    gx0 = idx_ref[0]
    gy0 = idx_ref[1]
    mid = pl.ds(h, cells_x)
    lo_p = pl.ds(0, h)
    hi_p = pl.ds(h + cells_x, h)
    own_r = pl.ds(ROW_PAD, cells_y)
    copies = []
    for a, dst, own in ((2, sg, own_sig), (0, ph, own_phi), (1, rs, own_rhs)):
        pieces = [
            (own, dst.at[mid, own_r]),
            (x_lo.at[a], dst.at[lo_p, own_r]),
            (x_hi.at[a], dst.at[hi_p, own_r]),
        ]
        for k, (which, depths) in enumerate(Y_ROWS["lo"]):
            for d in depths if which == a else ():
                pieces.append((y_lo.at[k], dst.at[mid, ROW_PAD - d]))
        for k, (which, depths) in enumerate(Y_ROWS["hi"]):
            for d in depths if which == a else ():
                pieces.append((y_hi.at[k], dst.at[mid, ROW_PAD + cells_y - 1 + d]))
        for r in range(h):
            lo_row = ROW_PAD - h + r
            hi_row = ROW_PAD + cells_y + r
            pieces += [
                (c_lo.at[0, a, r], dst.at[lo_p, lo_row]),
                (c_lo.at[1, a, r], dst.at[hi_p, lo_row]),
                (c_hi.at[0, a, r], dst.at[lo_p, hi_row]),
                (c_hi.at[1, a, r], dst.at[hi_p, hi_row]),
            ]
        for src_ref, dst_ref in pieces:
            cp = pltpu.make_async_copy(src_ref, dst_ref, sems.at[len(copies)])
            cp.start()
            copies.append(cp)
        if a == 2:
            per_array = len(copies)
    for cp in copies[:per_array]:
        cp.wait()
    row = lax.broadcasted_iota(jnp.int32, (rows, lanes), 0)
    lane = lax.broadcasted_iota(jnp.int32, (rows, lanes), 1)
    gy = gy0 + row
    iny = (gy >= 0) & (gy < ny)
    par[...] = jnp.where(iny, (gy + lane) & 1, 2)

    def faces_x(i, carry):
        gx = gx0 + i
        ok = (gx >= 0) & (gx + 1 < nx)
        s0 = sg[i]
        s1 = sg[i + 1]
        gyv = gy0 + lax.broadcasted_iota(jnp.int32, (rows, lanes), 0)
        inside = (gyv >= 0) & (gyv < ny) & ok
        fx[i] = jnp.where(inside, harmonic(s0, s1), 0.0)
        return carry

    lax.fori_loop(0, planes - 1, faces_x, 0, unroll=2)

    def faces_yz(i, carry):
        gx = gx0 + i
        inx = (gx >= 0) & (gx < nx)
        r = lax.broadcasted_iota(jnp.int32, (rows, lanes), 0)
        k = lax.broadcasted_iota(jnp.int32, (rows, lanes), 1)
        gyv = gy0 + r
        inyv = (gyv >= 0) & (gyv < ny)
        s = sg[i]
        s_yu = pltpu.roll(s, rows - 1, 0)
        s_zu = pltpu.roll(s, lanes - 1, 1)
        wy = jnp.where(inx & (gyv >= 0) & (gyv + 1 < ny), harmonic(s, s_yu), 0.0)
        wz = jnp.where(inx & inyv & (k < lanes - 1), harmonic(s, s_zu), 0.0)
        wy_lo = pltpu.roll(wy, 1, 0)
        wz_lo = pltpu.roll(wz, 1, 1)
        fy[i] = wy
        fz[i] = wz
        fzl[i] = wz_lo
        wxl = jnp.where(gx == 0, s, fx[i - 1])
        wxu = jnp.where(gx == nx - 1, s, fx[i])
        wyl = jnp.where(gyv == 0, s, wy_lo)
        wyu = jnp.where(gyv == ny - 1, s, wy)
        wzl = jnp.where(k == 0, s, wz_lo)
        wzu = jnp.where(k == lanes - 1, s, wz)
        d = wxl + wxu + wyl + wyu + wzl + wzu
        dg[i] = d
        inv[i] = 1.0 / d
        sg[i] = wy_lo
        return carry

    lax.fori_loop(1, planes - 1, faces_yz, 0, unroll=2)
    for cp in copies[per_array:]:
        cp.wait()

    def coupled_sum(i, pc):
        wy = fy[i]
        wz = fz[i]
        terms = (
            (fx[i - 1], ph[i - 1]),
            (fx[i], ph[i + 1]),
            (sg[i], pltpu.roll(pc, 1, 0)),
            (wy, pltpu.roll(pc, rows - 1, 0)),
            (fzl[i], pltpu.roll(pc, 1, 1)),
            (wz, pltpu.roll(pc, lanes - 1, 1)),
        )
        return terms

    for turn in range(2 * SWEEPS):
        colour = turn % 2

        def relax(i, carry, colour=colour):
            gx = gx0 + i
            inx = (gx >= 0) & (gx < nx)
            target = jnp.where(inx, (gx + colour) & 1, 3)
            pc = ph[i]
            summed = rs[i]
            for w, nb in coupled_sum(i, pc):
                summed = summed + w * nb
            ph[i] = jnp.where(par[...] == target, summed * inv[i], pc)
            return carry

        lax.fori_loop(turn + 1, planes - 1 - turn, relax, 0, unroll=2)

    own_rows = rows - 2 * ROW_PAD
    half_rows = own_rows // 2

    def defect_plane(i):
        pc = ph[i]
        terms = coupled_sum(i, pc)
        coupled = terms[0][0] * terms[0][1]
        for w, nb in terms[1:]:
            coupled = coupled + w * nb
        d = rs[i] - (dg[i] * pc - coupled)
        phi_out[i - HALO] = pc[ROW_PAD:ROW_PAD + own_rows]
        return d[ROW_PAD:ROW_PAD + own_rows]

    def restrict(j, carry):
        i = HALO + 2 * j
        pair = defect_plane(i) + defect_plane(i + 1)
        halves = []
        for q in range(lanes // 128):
            pair_buf[q] = pair[:, q * 128:(q + 1) * 128]
            even = pair_buf[q, pl.ds(0, half_rows, stride=2), :]
            odd = pair_buf[q, pl.ds(1, half_rows, stride=2), :]
            halves.append(even + odd)
        y_sums[pl.ds(pl.multiple_of(j * half_rows, half_rows), half_rows), :] = (
            jnp.concatenate(halves, axis=1))
        return carry

    lax.fori_loop(0, (planes - 2 * HALO) // 2, restrict, 0)
    coarse = 0.125 * jnp.dot(
        y_sums[...], pz_ref[...], precision=lax.Precision.HIGHEST,
        preferred_element_type=jnp.float32)
    coarse_out[...] = coarse
    first = idx_ref[2]
    for j in range(cells_x // 2):
        group_out[j, pl.ds(first, half_rows), :] = coarse[j * half_rows:(j + 1) * half_rows]


def exchange(arrays):
    boxes = lax.axis_size("box")
    grps = lax.axis_size("grp")
    h = HALO
    down_box = [(i, i + 1) for i in range(boxes - 1)]
    up_box = [(i + 1, i) for i in range(boxes - 1)]
    down_grp = [(i, i + 1) for i in range(grps - 1)]
    up_grp = [(i + 1, i) for i in range(grps - 1)]
    cells_x, cells_y, cells_z = arrays[0].shape
    gx = lax.axis_index("box") * cells_x + jnp.arange(cells_x, dtype=jnp.int32)[:, None]
    z = jnp.arange(cells_z, dtype=jnp.int32)[None, :]

    gy0 = lax.axis_index("grp") * cells_y

    def y_piece(side, block, slab_of):
        slabs = [jnp.swapaxes(a[:, block], 0, 1) for a in arrays]
        row_of = (lambda d: cells_y - d) if side == "lo" else (lambda d: d - 1)
        pairs = [depths for _, depths in PHI_ROWS if len(depths) == 2]
        colour1 = jnp.stack([(gx + gy0 + row_of(p[0]) + z) % 2 == 1 for p in pairs])
        first = jnp.stack([slabs[0][slab_of(p[0])] for p in pairs])
        second = jnp.stack([slabs[0][slab_of(p[1])] for p in pairs])
        single = [slabs[0][slab_of(d)][None] for _, (d, *more) in PHI_ROWS if not more]
        sig = slabs[2]
        rhs = slabs[1][1:] if side == "lo" else slabs[1][:-1]
        return jnp.concatenate([jnp.where(colour1, first, second)] + single + [sig, rhs])

    y_lo = lax.ppermute(y_piece("lo", slice(-h, None), lambda d: h - d), "grp", down_grp)
    y_hi = lax.ppermute(y_piece("hi", slice(0, h), lambda d: d - 1), "grp", up_grp)
    x_lo = lax.ppermute(jnp.stack([a[-h:] for a in arrays]), "box", down_box)
    x_hi = lax.ppermute(jnp.stack([a[:h] for a in arrays]), "box", up_box)
    c_lo = lax.ppermute(jnp.stack([jnp.swapaxes(x_lo[:, :, -h:], 1, 2),
                                   jnp.swapaxes(x_hi[:, :, -h:], 1, 2)]), "grp", down_grp)
    c_hi = lax.ppermute(jnp.stack([jnp.swapaxes(x_lo[:, :, :h], 1, 2),
                                   jnp.swapaxes(x_hi[:, :, :h], 1, 2)]), "grp", up_grp)
    return x_lo, x_hi, y_lo, y_hi, c_lo, c_hi


def local(phi_start, right_side, sigma):
    cells_x, cells_y, cells_z = phi_start.shape
    boxes = lax.axis_size("box")
    grps = lax.axis_size("grp")
    nx = cells_x * boxes
    ny = cells_y * grps
    b = lax.axis_index("box")
    g = lax.axis_index("grp")
    pieces = exchange((phi_start, right_side, sigma))
    planes = cells_x + 2 * HALO
    rows = cells_y + 2 * ROW_PAD
    lanes = cells_z
    idx = jnp.stack([b * cells_x - HALO, g * cells_y - ROW_PAD, g * (cells_y // 2)]).astype(jnp.int32)
    pz = jnp.asarray(np.kron(np.eye(cells_z // 2), np.ones((2, 1))), jnp.float32)
    full = pl.BlockSpec(memory_space=pltpu.MemorySpace.VMEM)
    anywhere = pl.BlockSpec(memory_space=pltpu.MemorySpace.HBM)
    big = pltpu.VMEM((planes, rows, lanes), jnp.float32)
    phi_smooth, coarse, group_coarse = pl.pallas_call(
        functools.partial(smooth_kernel, nx, ny),
        out_shape=(
            jax.ShapeDtypeStruct((cells_x, cells_y, cells_z), jnp.float32),
            jax.ShapeDtypeStruct((cells_x // 2 * (cells_y // 2), cells_z // 2), jnp.float32),
            jax.ShapeDtypeStruct((cells_x // 2, ny // 2, cells_z // 2), jnp.float32),
        ),
        in_specs=[pl.BlockSpec(memory_space=pltpu.MemorySpace.SMEM), full]
        + [anywhere] * 9,
        out_specs=(full, full, full),
        scratch_shapes=[big] * 9
        + [
            pltpu.VMEM((rows, lanes), jnp.int32),
            pltpu.VMEM((lanes // 128, cells_y, 128), jnp.float32),
            pltpu.VMEM((cells_x // 2 * (cells_y // 2), lanes), jnp.float32),
            pltpu.SemaphoreType.DMA((3 * (3 + 4 * HALO) + 2 * (2 * HALO + HALO - 1),)),
        ],
        compiler_params=pltpu.CompilerParams(vmem_limit_bytes=60 * 1024 * 1024),
    )(idx, pz, phi_start, right_side, sigma, *pieces)
    coarse = coarse.reshape(cells_x // 2, cells_y // 2, cells_z // 2)
    if grps == 2:
        other = lax.ppermute(coarse, "grp", [(0, 1), (1, 0)])
        group_coarse = lax.dynamic_update_slice(
            group_coarse, other, (0, (1 - g) * (cells_y // 2), 0))
    else:
        group_coarse = lax.all_gather(coarse, "grp", axis=1, tiled=True)
    return phi_smooth, group_coarse


def solution(mesh):
    placed = (P("box", "grp", None), P("box", "grp", None), P("box", "grp", None))
    return jax.shard_map(
        local,
        mesh=mesh,
        in_specs=placed,
        out_specs=(P("box", "grp", None), P("box", None, None)),
        check_vma=False,
    )
```

```python
import functools

import jax
import jax.numpy as jnp
import numpy as np
from jax import lax
from jax.experimental import pallas as pl
from jax.experimental.pallas import tpu as pltpu
from jax.sharding import PartitionSpec as P

SWEEPS = 2
HALO = 2 * SWEEPS + 1
ROW_PAD = 8
PHI_ROWS = ((0, (1, 2)), (0, (3, 4)), (0, (5,)))
Y_ROWS = {
    "lo": PHI_ROWS + tuple((2, (d,)) for d in range(HALO, 0, -1))
    + tuple((1, (d,)) for d in range(HALO - 1, 0, -1)),
    "hi": PHI_ROWS + tuple((2, (d,)) for d in range(1, HALO + 1))
    + tuple((1, (d,)) for d in range(1, HALO)),
}


def harmonic(s, t):
    return 2.0 * s * t / (s + t)


def smooth_kernel(nx, ny, idx_ref, pz_ref, own_phi, own_rhs, own_sig,
                  x_lo, x_hi, y_lo, y_hi, c_lo, c_hi,
                  phi_out, coarse_out, group_out, ph, rs, sg, fx, fy, fz, fzl, dg, inv, par,
                  pair_buf, y_sums, sems):
    planes, rows, lanes = ph.shape
    h = HALO
    cells_x = planes - 2 * h
    cells_y = rows - 2 * ROW_PAD
    gx0 = idx_ref[0]
    gy0 = idx_ref[1]
    mid = pl.ds(h, cells_x)
    lo_p = pl.ds(0, h)
    hi_p = pl.ds(h + cells_x, h)
    own_r = pl.ds(ROW_PAD, cells_y)
    copies = []
    for a, dst, own in ((2, sg, own_sig), (0, ph, own_phi), (1, rs, own_rhs)):
        pieces = [
            (own, dst.at[mid, own_r]),
            (x_lo.at[a], dst.at[lo_p, own_r]),
            (x_hi.at[a], dst.at[hi_p, own_r]),
        ]
        for k, (which, depths) in enumerate(Y_ROWS["lo"]):
            for d in depths if which == a else ():
                pieces.append((y_lo.at[k], dst.at[mid, ROW_PAD - d]))
        for k, (which, depths) in enumerate(Y_ROWS["hi"]):
            for d in depths if which == a else ():
                pieces.append((y_hi.at[k], dst.at[mid, ROW_PAD + cells_y - 1 + d]))
        for r in range(h):
            lo_row = ROW_PAD - h + r
            hi_row = ROW_PAD + cells_y + r
            pieces += [
                (c_lo.at[0, a, r], dst.at[lo_p, lo_row]),
                (c_lo.at[1, a, r], dst.at[hi_p, lo_row]),
                (c_hi.at[0, a, r], dst.at[lo_p, hi_row]),
                (c_hi.at[1, a, r], dst.at[hi_p, hi_row]),
            ]
        for src_ref, dst_ref in pieces:
            cp = pltpu.make_async_copy(src_ref, dst_ref, sems.at[len(copies)])
            cp.start()
            copies.append(cp)
        if a == 2:
            per_array = len(copies)
    for cp in copies[:per_array]:
        cp.wait()
    row = lax.broadcasted_iota(jnp.int32, (rows, lanes), 0)
    lane = lax.broadcasted_iota(jnp.int32, (rows, lanes), 1)
    gy = gy0 + row
    iny = (gy >= 0) & (gy < ny)
    par[...] = jnp.where(iny, (gy + lane) & 1, 2)

    def faces_x(i, carry):
        gx = gx0 + i
        ok = (gx >= 0) & (gx + 1 < nx)
        s0 = sg[i]
        s1 = sg[i + 1]
        gyv = gy0 + lax.broadcasted_iota(jnp.int32, (rows, lanes), 0)
        inside = (gyv >= 0) & (gyv < ny) & ok
        fx[i] = jnp.where(inside, harmonic(s0, s1), 0.0)
        return carry

    lax.fori_loop(0, planes - 1, faces_x, 0, unroll=2)

    def faces_yz(i, carry):
        gx = gx0 + i
        inx = (gx >= 0) & (gx < nx)
        r = lax.broadcasted_iota(jnp.int32, (rows, lanes), 0)
        k = lax.broadcasted_iota(jnp.int32, (rows, lanes), 1)
        gyv = gy0 + r
        inyv = (gyv >= 0) & (gyv < ny)
        s = sg[i]
        s_yu = pltpu.roll(s, rows - 1, 0)
        s_zu = pltpu.roll(s, lanes - 1, 1)
        wy = jnp.where(inx & (gyv >= 0) & (gyv + 1 < ny), harmonic(s, s_yu), 0.0)
        wz = jnp.where(inx & inyv & (k < lanes - 1), harmonic(s, s_zu), 0.0)
        wy_lo = pltpu.roll(wy, 1, 0)
        wz_lo = pltpu.roll(wz, 1, 1)
        fy[i] = wy
        fz[i] = wz
        fzl[i] = wz_lo
        wxl = jnp.where(gx == 0, s, fx[i - 1])
        wxu = jnp.where(gx == nx - 1, s, fx[i])
        wyl = jnp.where(gyv == 0, s, wy_lo)
        wyu = jnp.where(gyv == ny - 1, s, wy)
        wzl = jnp.where(k == 0, s, wz_lo)
        wzu = jnp.where(k == lanes - 1, s, wz)
        d = wxl + wxu + wyl + wyu + wzl + wzu
        dg[i] = d
        inv[i] = 1.0 / d
        sg[i] = wy_lo
        return carry

    lax.fori_loop(1, planes - 1, faces_yz, 0, unroll=2)
    for cp in copies[per_array:]:
        cp.wait()

    def coupled_sum(i, pc):
        wy = fy[i]
        wz = fz[i]
        terms = (
            (fx[i - 1], ph[i - 1]),
            (fx[i], ph[i + 1]),
            (sg[i], pltpu.roll(pc, 1, 0)),
            (wy, pltpu.roll(pc, rows - 1, 0)),
            (fzl[i], pltpu.roll(pc, 1, 1)),
            (wz, pltpu.roll(pc, lanes - 1, 1)),
        )
        return terms

    for turn in range(2 * SWEEPS):
        colour = turn % 2

        def relax(i, carry, colour=colour):
            gx = gx0 + i
            inx = (gx >= 0) & (gx < nx)
            target = jnp.where(inx, (gx + colour) & 1, 3)
            pc = ph[i]
            summed = rs[i]
            for w, nb in coupled_sum(i, pc):
                summed = summed + w * nb
            ph[i] = jnp.where(par[...] == target, summed * inv[i], pc)
            return carry

        lax.fori_loop(turn + 1, planes - 1 - turn, relax, 0, unroll=2)

    own_rows = rows - 2 * ROW_PAD
    half_rows = own_rows // 2

    def defect_plane(i):
        pc = ph[i]
        terms = coupled_sum(i, pc)
        coupled = terms[0][0] * terms[0][1]
        for w, nb in terms[1:]:
            coupled = coupled + w * nb
        d = rs[i] - (dg[i] * pc - coupled)
        phi_out[i - HALO] = pc[ROW_PAD:ROW_PAD + own_rows]
        return d[ROW_PAD:ROW_PAD + own_rows]

    def restrict(j, carry):
        i = HALO + 2 * j
        pair = defect_plane(i) + defect_plane(i + 1)
        halves = []
        for q in range(lanes // 128):
            pair_buf[q] = pair[:, q * 128:(q + 1) * 128]
            even = pair_buf[q, pl.ds(0, half_rows, stride=2), :]
            odd = pair_buf[q, pl.ds(1, half_rows, stride=2), :]
            halves.append(even + odd)
        y_sums[pl.ds(pl.multiple_of(j * half_rows, half_rows), half_rows), :] = (
            jnp.concatenate(halves, axis=1))
        return carry

    lax.fori_loop(0, (planes - 2 * HALO) // 2, restrict, 0)
    coarse = 0.125 * jnp.dot(
        y_sums[...], pz_ref[...], precision=lax.Precision.HIGHEST,
        preferred_element_type=jnp.float32)
    coarse_out[...] = coarse
    first = idx_ref[2]
    for j in range(cells_x // 2):
        group_out[j, pl.ds(first, half_rows), :] = coarse[j * half_rows:(j + 1) * half_rows]


def exchange(arrays):
    boxes = lax.axis_size("box")
    grps = lax.axis_size("grp")
    h = HALO
    down_box = [(i, i + 1) for i in range(boxes - 1)]
    up_box = [(i + 1, i) for i in range(boxes - 1)]
    down_grp = [(i, i + 1) for i in range(grps - 1)]
    up_grp = [(i + 1, i) for i in range(grps - 1)]
    cells_x, cells_y, cells_z = arrays[0].shape
    gx = lax.axis_index("box") * cells_x + jnp.arange(cells_x, dtype=jnp.int32)[:, None]
    z = jnp.arange(cells_z, dtype=jnp.int32)[None, :]

    gy0 = lax.axis_index("grp") * cells_y

    def y_piece(side, block, slab_of):
        slabs = [jnp.swapaxes(a[:, block], 0, 1) for a in arrays]
        row_of = (lambda d: cells_y - d) if side == "lo" else (lambda d: d - 1)
        pairs = [depths for _, depths in PHI_ROWS if len(depths) == 2]
        colour1 = jnp.stack([(gx + gy0 + row_of(p[0]) + z) % 2 == 1 for p in pairs])
        first = jnp.stack([slabs[0][slab_of(p[0])] for p in pairs])
        second = jnp.stack([slabs[0][slab_of(p[1])] for p in pairs])
        single = [slabs[0][slab_of(d)][None] for _, (d, *more) in PHI_ROWS if not more]
        sig = slabs[2]
        rhs = slabs[1][1:] if side == "lo" else slabs[1][:-1]
        return jnp.concatenate([jnp.where(colour1, first, second)] + single + [sig, rhs])

    y_lo_send = y_piece("lo", slice(-h, None), lambda d: h - d)
    y_hi_send = y_piece("hi", slice(0, h), lambda d: d - 1)
    g = lax.axis_index("grp")
    swap = [(0, 1), (1, 0)]
    if grps == 2:
        y_lo = y_hi = lax.ppermute(jnp.where(g == 0, y_lo_send, y_hi_send), "grp", swap)
    else:
        y_lo = lax.ppermute(y_lo_send, "grp", down_grp)
        y_hi = lax.ppermute(y_hi_send, "grp", up_grp)
    x_lo = lax.ppermute(jnp.stack([a[-h:] for a in arrays]), "box", down_box)
    x_hi = lax.ppermute(jnp.stack([a[:h] for a in arrays]), "box", up_box)
    c_lo_send = jnp.stack([jnp.swapaxes(x_lo[:, :, -h:], 1, 2),
                           jnp.swapaxes(x_hi[:, :, -h:], 1, 2)])
    c_hi_send = jnp.stack([jnp.swapaxes(x_lo[:, :, :h], 1, 2),
                           jnp.swapaxes(x_hi[:, :, :h], 1, 2)])
    if grps == 2:
        c_lo = c_hi = lax.ppermute(jnp.where(g == 0, c_lo_send, c_hi_send), "grp", swap)
    else:
        c_lo = lax.ppermute(c_lo_send, "grp", down_grp)
        c_hi = lax.ppermute(c_hi_send, "grp", up_grp)
    return x_lo, x_hi, y_lo, y_hi, c_lo, c_hi


def local(phi_start, right_side, sigma):
    cells_x, cells_y, cells_z = phi_start.shape
    boxes = lax.axis_size("box")
    grps = lax.axis_size("grp")
    nx = cells_x * boxes
    ny = cells_y * grps
    b = lax.axis_index("box")
    g = lax.axis_index("grp")
    pieces = exchange((phi_start, right_side, sigma))
    planes = cells_x + 2 * HALO
    rows = cells_y + 2 * ROW_PAD
    lanes = cells_z
    idx = jnp.stack([b * cells_x - HALO, g * cells_y - ROW_PAD, g * (cells_y // 2)]).astype(jnp.int32)
    pz = jnp.asarray(np.kron(np.eye(cells_z // 2), np.ones((2, 1))), jnp.float32)
    full = pl.BlockSpec(memory_space=pltpu.MemorySpace.VMEM)
    anywhere = pl.BlockSpec(memory_space=pltpu.MemorySpace.HBM)
    big = pltpu.VMEM((planes, rows, lanes), jnp.float32)
    phi_smooth, coarse, group_coarse = pl.pallas_call(
        functools.partial(smooth_kernel, nx, ny),
        out_shape=(
            jax.ShapeDtypeStruct((cells_x, cells_y, cells_z), jnp.float32),
            jax.ShapeDtypeStruct((cells_x // 2 * (cells_y // 2), cells_z // 2), jnp.float32),
            jax.ShapeDtypeStruct((cells_x // 2, ny // 2, cells_z // 2), jnp.float32),
        ),
        in_specs=[pl.BlockSpec(memory_space=pltpu.MemorySpace.SMEM), full]
        + [anywhere] * 9,
        out_specs=(full, full, full),
        scratch_shapes=[big] * 9
        + [
            pltpu.VMEM((rows, lanes), jnp.int32),
            pltpu.VMEM((lanes // 128, cells_y, 128), jnp.float32),
            pltpu.VMEM((cells_x // 2 * (cells_y // 2), lanes), jnp.float32),
            pltpu.SemaphoreType.DMA((3 * (3 + 4 * HALO) + 2 * (2 * HALO + HALO - 1),)),
        ],
        compiler_params=pltpu.CompilerParams(vmem_limit_bytes=60 * 1024 * 1024),
    )(idx, pz, phi_start, right_side, sigma, *pieces)
    coarse = coarse.reshape(cells_x // 2, cells_y // 2, cells_z // 2)
    if grps == 2:
        other = lax.ppermute(coarse, "grp", [(0, 1), (1, 0)])
        group_coarse = lax.dynamic_update_slice(
            group_coarse, other, (0, (1 - g) * (cells_y // 2), 0))
    else:
        group_coarse = lax.all_gather(coarse, "grp", axis=1, tiled=True)
    return phi_smooth, group_coarse


def solution(mesh):
    placed = (P("box", "grp", None), P("box", "grp", None), P("box", "grp", None))
    return jax.shard_map(
        local,
        mesh=mesh,
        in_specs=placed,
        out_specs=(P("box", "grp", None), P("box", None, None)),
        check_vma=False,
    )
```

```python
import functools

import jax
import jax.numpy as jnp
import numpy as np
from jax import lax
from jax.experimental import pallas as pl
from jax.experimental.pallas import tpu as pltpu
from jax.sharding import PartitionSpec as P

SWEEPS = 2
HALO = 2 * SWEEPS + 1
ROW_PAD = 8
PHI_ROWS = ((0, (1, 2)), (0, (3, 4)), (0, (5,)))
Y_ROWS = {
    "lo": PHI_ROWS + tuple((2, (d,)) for d in range(HALO, 0, -1))
    + tuple((1, (d,)) for d in range(HALO - 1, 0, -1)),
    "hi": PHI_ROWS + tuple((2, (d,)) for d in range(1, HALO + 1))
    + tuple((1, (d,)) for d in range(1, HALO)),
}


def harmonic(s, t):
    return 2.0 * s * t / (s + t)


def smooth_kernel(nx, ny, idx_ref, pz_ref, own_phi, own_rhs, own_sig,
                  x_lo, x_hi, y_lo, y_hi, cl_lo, cl_hi, ch_lo, ch_hi,
                  phi_out, coarse_out, group_out, ph, rs, sg, fx, fy, fz, fzl, dg, inv, par,
                  pair_buf, y_sums, sems):
    planes, rows, lanes = ph.shape
    h = HALO
    cells_x = planes - 2 * h
    cells_y = rows - 2 * ROW_PAD
    gx0 = idx_ref[0]
    gy0 = idx_ref[1]
    mid = pl.ds(h, cells_x)
    lo_p = pl.ds(0, h)
    hi_p = pl.ds(h + cells_x, h)
    own_r = pl.ds(ROW_PAD, cells_y)
    copies = []
    for a, dst, own in ((2, sg, own_sig), (0, ph, own_phi), (1, rs, own_rhs)):
        pieces = [
            (own, dst.at[mid, own_r]),
            (x_lo.at[a], dst.at[lo_p, own_r]),
            (x_hi.at[a], dst.at[hi_p, own_r]),
        ]
        for side, y_part, below, above in (("lo", y_lo, cl_lo, ch_lo), ("hi", y_hi, cl_hi, ch_hi)):
            for k, (which, depths) in enumerate(Y_ROWS[side]):
                for d in depths if which == a else ():
                    row = ROW_PAD - d if side == "lo" else ROW_PAD + cells_y - 1 + d
                    pieces += [
                        (y_part.at[k], dst.at[mid, row]),
                        (below.at[k], dst.at[lo_p, row]),
                        (above.at[k], dst.at[hi_p, row]),
                    ]
        for src_ref, dst_ref in pieces:
            cp = pltpu.make_async_copy(src_ref, dst_ref, sems.at[len(copies)])
            cp.start()
            copies.append(cp)
        if a == 2:
            per_array = len(copies)
    for cp in copies[:per_array]:
        cp.wait()
    row = lax.broadcasted_iota(jnp.int32, (rows, lanes), 0)
    lane = lax.broadcasted_iota(jnp.int32, (rows, lanes), 1)
    gy = gy0 + row
    iny = (gy >= 0) & (gy < ny)
    par[...] = jnp.where(iny, (gy + lane) & 1, 2)

    def faces_x(i, carry):
        gx = gx0 + i
        ok = (gx >= 0) & (gx + 1 < nx)
        s0 = sg[i]
        s1 = sg[i + 1]
        gyv = gy0 + lax.broadcasted_iota(jnp.int32, (rows, lanes), 0)
        inside = (gyv >= 0) & (gyv < ny) & ok
        fx[i] = jnp.where(inside, harmonic(s0, s1), 0.0)
        return carry

    lax.fori_loop(0, planes - 1, faces_x, 0, unroll=2)

    def faces_yz(i, carry):
        gx = gx0 + i
        inx = (gx >= 0) & (gx < nx)
        r = lax.broadcasted_iota(jnp.int32, (rows, lanes), 0)
        k = lax.broadcasted_iota(jnp.int32, (rows, lanes), 1)
        gyv = gy0 + r
        inyv = (gyv >= 0) & (gyv < ny)
        s = sg[i]
        s_yu = pltpu.roll(s, rows - 1, 0)
        s_zu = pltpu.roll(s, lanes - 1, 1)
        wy = jnp.where(inx & (gyv >= 0) & (gyv + 1 < ny), harmonic(s, s_yu), 0.0)
        wz = jnp.where(inx & inyv & (k < lanes - 1), harmonic(s, s_zu), 0.0)
        wy_lo = pltpu.roll(wy, 1, 0)
        wz_lo = pltpu.roll(wz, 1, 1)
        fy[i] = wy
        fz[i] = wz
        fzl[i] = wz_lo
        wxl = jnp.where(gx == 0, s, fx[i - 1])
        wxu = jnp.where(gx == nx - 1, s, fx[i])
        wyl = jnp.where(gyv == 0, s, wy_lo)
        wyu = jnp.where(gyv == ny - 1, s, wy)
        wzl = jnp.where(k == 0, s, wz_lo)
        wzu = jnp.where(k == lanes - 1, s, wz)
        d = wxl + wxu + wyl + wyu + wzl + wzu
        dg[i] = d
        inv[i] = 1.0 / d
        sg[i] = wy_lo
        return carry

    lax.fori_loop(1, planes - 1, faces_yz, 0, unroll=2)
    for cp in copies[per_array:]:
        cp.wait()

    def coupled_sum(i, pc):
        wy = fy[i]
        wz = fz[i]
        terms = (
            (fx[i - 1], ph[i - 1]),
            (fx[i], ph[i + 1]),
            (sg[i], pltpu.roll(pc, 1, 0)),
            (wy, pltpu.roll(pc, rows - 1, 0)),
            (fzl[i], pltpu.roll(pc, 1, 1)),
            (wz, pltpu.roll(pc, lanes - 1, 1)),
        )
        return terms

    for turn in range(2 * SWEEPS):
        colour = turn % 2

        def relax(i, carry, colour=colour):
            gx = gx0 + i
            inx = (gx >= 0) & (gx < nx)
            target = jnp.where(inx, (gx + colour) & 1, 3)
            pc = ph[i]
            summed = rs[i]
            for w, nb in coupled_sum(i, pc):
                summed = summed + w * nb
            ph[i] = jnp.where(par[...] == target, summed * inv[i], pc)
            return carry

        lax.fori_loop(turn + 1, planes - 1 - turn, relax, 0, unroll=2)

    own_rows = rows - 2 * ROW_PAD
    half_rows = own_rows // 2

    def defect_plane(i):
        pc = ph[i]
        terms = coupled_sum(i, pc)
        coupled = terms[0][0] * terms[0][1]
        for w, nb in terms[1:]:
            coupled = coupled + w * nb
        d = rs[i] - (dg[i] * pc - coupled)
        phi_out[i - HALO] = pc[ROW_PAD:ROW_PAD + own_rows]
        return d[ROW_PAD:ROW_PAD + own_rows]

    def restrict(j, carry):
        i = HALO + 2 * j
        pair = defect_plane(i) + defect_plane(i + 1)
        halves = []
        for q in range(lanes // 128):
            pair_buf[q] = pair[:, q * 128:(q + 1) * 128]
            even = pair_buf[q, pl.ds(0, half_rows, stride=2), :]
            odd = pair_buf[q, pl.ds(1, half_rows, stride=2), :]
            halves.append(even + odd)
        y_sums[pl.ds(pl.multiple_of(j * half_rows, half_rows), half_rows), :] = (
            jnp.concatenate(halves, axis=1))
        return carry

    lax.fori_loop(0, (planes - 2 * HALO) // 2, restrict, 0)
    coarse = 0.125 * jnp.dot(
        y_sums[...], pz_ref[...], precision=lax.Precision.HIGHEST,
        preferred_element_type=jnp.float32)
    coarse_out[...] = coarse
    first = idx_ref[2]
    for j in range(cells_x // 2):
        group_out[j, pl.ds(first, half_rows), :] = coarse[j * half_rows:(j + 1) * half_rows]


def exchange(arrays):
    boxes = lax.axis_size("box")
    grps = lax.axis_size("grp")
    h = HALO
    down_box = [(i, i + 1) for i in range(boxes - 1)]
    up_box = [(i + 1, i) for i in range(boxes - 1)]
    down_grp = [(i, i + 1) for i in range(grps - 1)]
    up_grp = [(i + 1, i) for i in range(grps - 1)]
    cells_x, cells_y, cells_z = arrays[0].shape
    gx = lax.axis_index("box") * cells_x + jnp.arange(cells_x, dtype=jnp.int32)[:, None]
    z = jnp.arange(cells_z, dtype=jnp.int32)[None, :]

    gy0 = lax.axis_index("grp") * cells_y

    def y_piece(side, block, slab_of):
        slabs = [jnp.swapaxes(a[:, block], 0, 1) for a in arrays]
        row_of = (lambda d: cells_y - d) if side == "lo" else (lambda d: d - 1)
        pairs = [depths for _, depths in PHI_ROWS if len(depths) == 2]
        colour1 = jnp.stack([(gx + gy0 + row_of(p[0]) + z) % 2 == 1 for p in pairs])
        first = jnp.stack([slabs[0][slab_of(p[0])] for p in pairs])
        second = jnp.stack([slabs[0][slab_of(p[1])] for p in pairs])
        single = [slabs[0][slab_of(d)][None] for _, (d, *more) in PHI_ROWS if not more]
        sig = slabs[2]
        rhs = slabs[1][1:] if side == "lo" else slabs[1][:-1]
        return jnp.concatenate([jnp.where(colour1, first, second)] + single + [sig, rhs])

    y_lo_send = y_piece("lo", slice(-h, None), lambda d: h - d)
    y_hi_send = y_piece("hi", slice(0, h), lambda d: d - 1)
    g = lax.axis_index("grp")
    swap = [(0, 1), (1, 0)]
    if grps == 2:
        y_lo = y_hi = lax.ppermute(jnp.where(g == 0, y_lo_send, y_hi_send), "grp", swap)
    else:
        y_lo = lax.ppermute(y_lo_send, "grp", down_grp)
        y_hi = lax.ppermute(y_hi_send, "grp", up_grp)
    x_lo = lax.ppermute(jnp.stack([a[-h:] for a in arrays]), "box", down_box)
    x_hi = lax.ppermute(jnp.stack([a[:h] for a in arrays]), "box", up_box)
    corners = {}
    for name, part in (("lo", y_lo), ("hi", y_hi)):
        if name == "hi" and part is y_lo:
            corners["hi"] = corners["lo"]
            continue
        corners[name] = (
            lax.ppermute(part[:, -h:], "box", down_box),
            lax.ppermute(part[:, :h], "box", up_box),
        )
    (cl_lo, ch_lo), (cl_hi, ch_hi) = corners["lo"], corners["hi"]
    return x_lo, x_hi, y_lo, y_hi, cl_lo, cl_hi, ch_lo, ch_hi


def local(phi_start, right_side, sigma):
    cells_x, cells_y, cells_z = phi_start.shape
    boxes = lax.axis_size("box")
    grps = lax.axis_size("grp")
    nx = cells_x * boxes
    ny = cells_y * grps
    b = lax.axis_index("box")
    g = lax.axis_index("grp")
    pieces = exchange((phi_start, right_side, sigma))
    planes = cells_x + 2 * HALO
    rows = cells_y + 2 * ROW_PAD
    lanes = cells_z
    idx = jnp.stack([b * cells_x - HALO, g * cells_y - ROW_PAD, g * (cells_y // 2)]).astype(jnp.int32)
    pz = jnp.asarray(np.kron(np.eye(cells_z // 2), np.ones((2, 1))), jnp.float32)
    full = pl.BlockSpec(memory_space=pltpu.MemorySpace.VMEM)
    anywhere = pl.BlockSpec(memory_space=pltpu.MemorySpace.HBM)
    big = pltpu.VMEM((planes, rows, lanes), jnp.float32)
    phi_smooth, coarse, group_coarse = pl.pallas_call(
        functools.partial(smooth_kernel, nx, ny),
        out_shape=(
            jax.ShapeDtypeStruct((cells_x, cells_y, cells_z), jnp.float32),
            jax.ShapeDtypeStruct((cells_x // 2 * (cells_y // 2), cells_z // 2), jnp.float32),
            jax.ShapeDtypeStruct((cells_x // 2, ny // 2, cells_z // 2), jnp.float32),
        ),
        in_specs=[pl.BlockSpec(memory_space=pltpu.MemorySpace.SMEM), full]
        + [anywhere] * 11,
        out_specs=(full, full, full),
        scratch_shapes=[big] * 9
        + [
            pltpu.VMEM((rows, lanes), jnp.int32),
            pltpu.VMEM((lanes // 128, cells_y, 128), jnp.float32),
            pltpu.VMEM((cells_x // 2 * (cells_y // 2), lanes), jnp.float32),
            pltpu.SemaphoreType.DMA((3 * (3 + 4 * HALO) + 2 * (2 * HALO + HALO - 1),)),
        ],
        compiler_params=pltpu.CompilerParams(vmem_limit_bytes=60 * 1024 * 1024),
    )(idx, pz, phi_start, right_side, sigma, *pieces)
    coarse = coarse.reshape(cells_x // 2, cells_y // 2, cells_z // 2)
    if grps == 2:
        other = lax.ppermute(coarse, "grp", [(0, 1), (1, 0)])
        group_coarse = lax.dynamic_update_slice(
            group_coarse, other, (0, (1 - g) * (cells_y // 2), 0))
    else:
        group_coarse = lax.all_gather(coarse, "grp", axis=1, tiled=True)
    return phi_smooth, group_coarse


def solution(mesh):
    placed = (P("box", "grp", None), P("box", "grp", None), P("box", "grp", None))
    return jax.shard_map(
        local,
        mesh=mesh,
        in_specs=placed,
        out_specs=(P("box", "grp", None), P("box", None, None)),
        check_vma=False,
    )
```

```python
import functools

import jax
import jax.numpy as jnp
import numpy as np
from jax import lax
from jax.experimental import pallas as pl
from jax.experimental.pallas import tpu as pltpu
from jax.sharding import PartitionSpec as P

SWEEPS = 2
HALO = 2 * SWEEPS + 1
ROW_PAD = 8
PHI_ROWS = ((0, (1, 2)), (0, (3, 4)), (0, (5,)))
Y_ROWS = {
    "lo": PHI_ROWS + tuple((2, (d,)) for d in range(HALO, 0, -1))
    + tuple((1, (d,)) for d in range(HALO - 1, 0, -1)),
    "hi": PHI_ROWS + tuple((2, (d,)) for d in range(1, HALO + 1))
    + tuple((1, (d,)) for d in range(1, HALO)),
}


def harmonic(s, t):
    return 2.0 * s * t / (s + t)


def smooth_kernel(nx, ny, idx_ref, pz_ref, own_phi, own_rhs, own_sig,
                  x_lo, x_hi, y_lo, y_hi, cl_lo, cl_hi, ch_lo, ch_hi,
                  phi_out, coarse_out, group_out, ph, rs, sg, fx, fy, fz, fzl, dg, inv, par,
                  pair_buf, y_sums, sems):
    planes, rows, lanes = ph.shape
    h = HALO
    cells_x = planes - 2 * h
    cells_y = rows - 2 * ROW_PAD
    gx0 = idx_ref[0]
    gy0 = idx_ref[1]
    mid = pl.ds(h, cells_x)
    lo_p = pl.ds(0, h)
    hi_p = pl.ds(h + cells_x, h)
    own_r = pl.ds(ROW_PAD, cells_y)
    copies = []
    for a, dst, own in ((2, sg, own_sig), (0, ph, own_phi), (1, rs, own_rhs)):
        pieces = [
            (own, dst.at[mid, own_r]),
            (x_lo.at[a], dst.at[lo_p, own_r]),
            (x_hi.at[a], dst.at[hi_p, own_r]),
        ]
        for side, y_part, below, above in (("lo", y_lo, cl_lo, ch_lo), ("hi", y_hi, cl_hi, ch_hi)):
            for k, (which, depths) in enumerate(Y_ROWS[side]):
                for d in depths if which == a else ():
                    row = ROW_PAD - d if side == "lo" else ROW_PAD + cells_y - 1 + d
                    pieces += [
                        (y_part.at[k], dst.at[mid, row]),
                        (below.at[k], dst.at[lo_p, row]),
                        (above.at[k], dst.at[hi_p, row]),
                    ]
        for src_ref, dst_ref in pieces:
            cp = pltpu.make_async_copy(src_ref, dst_ref, sems.at[len(copies)])
            cp.start()
            copies.append(cp)
        if a == 2:
            per_array = len(copies)
    for cp in copies[:per_array]:
        cp.wait()
    row = lax.broadcasted_iota(jnp.int32, (rows, lanes), 0)
    lane = lax.broadcasted_iota(jnp.int32, (rows, lanes), 1)
    gy = gy0 + row
    iny = (gy >= 0) & (gy < ny)
    par[...] = jnp.where(iny, (gy + lane) & 1, 2)

    def faces_x(i, carry):
        gx = gx0 + i
        ok = (gx >= 0) & (gx + 1 < nx)
        s0 = sg[i]
        s1 = sg[i + 1]
        gyv = gy0 + lax.broadcasted_iota(jnp.int32, (rows, lanes), 0)
        inside = (gyv >= 0) & (gyv < ny) & ok
        fx[i] = jnp.where(inside, harmonic(s0, s1), 0.0)
        return carry

    lax.fori_loop(0, planes - 1, faces_x, 0, unroll=2)

    def faces_yz(i, carry):
        gx = gx0 + i
        inx = (gx >= 0) & (gx < nx)
        r = lax.broadcasted_iota(jnp.int32, (rows, lanes), 0)
        k = lax.broadcasted_iota(jnp.int32, (rows, lanes), 1)
        gyv = gy0 + r
        inyv = (gyv >= 0) & (gyv < ny)
        s = sg[i]
        s_yu = pltpu.roll(s, rows - 1, 0)
        s_zu = pltpu.roll(s, lanes - 1, 1)
        wy = jnp.where(inx & (gyv >= 0) & (gyv + 1 < ny), harmonic(s, s_yu), 0.0)
        wz = jnp.where(inx & inyv & (k < lanes - 1), harmonic(s, s_zu), 0.0)
        wy_lo = pltpu.roll(wy, 1, 0)
        wz_lo = pltpu.roll(wz, 1, 1)
        fy[i] = wy
        fz[i] = wz
        fzl[i] = wz_lo
        wxl = jnp.where(gx == 0, s, fx[i - 1])
        wxu = jnp.where(gx == nx - 1, s, fx[i])
        wyl = jnp.where(gyv == 0, s, wy_lo)
        wyu = jnp.where(gyv == ny - 1, s, wy)
        wzl = jnp.where(k == 0, s, wz_lo)
        wzu = jnp.where(k == lanes - 1, s, wz)
        d = wxl + wxu + wyl + wyu + wzl + wzu
        dg[i] = d
        inv[i] = 1.0 / d
        sg[i] = wy_lo
        return carry

    lax.fori_loop(1, planes - 1, faces_yz, 0, unroll=2)
    for cp in copies[per_array:]:
        cp.wait()

    def coupled_sum(i, pc):
        wy = fy[i]
        wz = fz[i]
        terms = (
            (fx[i - 1], ph[i - 1]),
            (fx[i], ph[i + 1]),
            (sg[i], pltpu.roll(pc, 1, 0)),
            (wy, pltpu.roll(pc, rows - 1, 0)),
            (fzl[i], pltpu.roll(pc, 1, 1)),
            (wz, pltpu.roll(pc, lanes - 1, 1)),
        )
        return terms

    for turn in range(2 * SWEEPS):
        colour = turn % 2

        def relax(i, carry, colour=colour):
            gx = gx0 + i
            inx = (gx >= 0) & (gx < nx)
            target = jnp.where(inx, (gx + colour) & 1, 3)
            pc = ph[i]
            summed = rs[i]
            for w, nb in coupled_sum(i, pc):
                summed = summed + w * nb
            ph[i] = jnp.where(par[...] == target, summed * inv[i], pc)
            return carry

        lax.fori_loop(turn + 1, planes - 1 - turn, relax, 0, unroll=2)

    own_rows = rows - 2 * ROW_PAD
    half_rows = own_rows // 2

    def defect_plane(i):
        pc = ph[i]
        terms = coupled_sum(i, pc)
        coupled = terms[0][0] * terms[0][1]
        for w, nb in terms[1:]:
            coupled = coupled + w * nb
        d = rs[i] - (dg[i] * pc - coupled)
        phi_out[i - HALO] = pc[ROW_PAD:ROW_PAD + own_rows]
        return d[ROW_PAD:ROW_PAD + own_rows]

    def restrict(j, carry):
        i = HALO + 2 * j
        pair = defect_plane(i) + defect_plane(i + 1)
        halves = []
        for q in range(lanes // 128):
            pair_buf[q] = pair[:, q * 128:(q + 1) * 128]
            even = pair_buf[q, pl.ds(0, half_rows, stride=2), :]
            odd = pair_buf[q, pl.ds(1, half_rows, stride=2), :]
            halves.append(even + odd)
        y_sums[pl.ds(pl.multiple_of(j * half_rows, half_rows), half_rows), :] = (
            jnp.concatenate(halves, axis=1))
        return carry

    lax.fori_loop(0, (planes - 2 * HALO) // 2, restrict, 0)
    coarse = 0.125 * jnp.dot(
        y_sums[...], pz_ref[...], precision=lax.Precision.HIGHEST,
        preferred_element_type=jnp.float32)
    coarse_out[...] = coarse
    first = idx_ref[2]
    for j in range(cells_x // 2):
        group_out[j, pl.ds(first, half_rows), :] = coarse[j * half_rows:(j + 1) * half_rows]


def exchange(arrays):
    boxes = lax.axis_size("box")
    grps = lax.axis_size("grp")
    h = HALO
    down_box = [(i, i + 1) for i in range(boxes - 1)]
    up_box = [(i + 1, i) for i in range(boxes - 1)]
    down_grp = [(i, i + 1) for i in range(grps - 1)]
    up_grp = [(i + 1, i) for i in range(grps - 1)]
    cells_x, cells_y, cells_z = arrays[0].shape
    gx = lax.axis_index("box") * cells_x + jnp.arange(cells_x, dtype=jnp.int32)[:, None]
    z = jnp.arange(cells_z, dtype=jnp.int32)[None, :]

    gy0 = lax.axis_index("grp") * cells_y

    def y_piece(side, block, slab_of):
        slabs = [jnp.swapaxes(a[:, block], 0, 1) for a in arrays]
        row_of = (lambda d: cells_y - d) if side == "lo" else (lambda d: d - 1)
        pairs = [depths for _, depths in PHI_ROWS if len(depths) == 2]
        colour1 = jnp.stack([(gx + gy0 + row_of(p[0]) + z) % 2 == 1 for p in pairs])
        first = jnp.stack([slabs[0][slab_of(p[0])] for p in pairs])
        second = jnp.stack([slabs[0][slab_of(p[1])] for p in pairs])
        single = [slabs[0][slab_of(d)][None] for _, (d, *more) in PHI_ROWS if not more]
        sig = slabs[2]
        rhs = slabs[1][1:] if side == "lo" else slabs[1][:-1]
        return jnp.concatenate([jnp.where(colour1, first, second)] + single + [sig, rhs])

    y_lo_send = y_piece("lo", slice(-h, None), lambda d: h - d)
    y_hi_send = y_piece("hi", slice(0, h), lambda d: d - 1)
    g = lax.axis_index("grp")
    swap = [(0, 1), (1, 0)]
    if grps == 2:
        y_lo = y_hi = lax.ppermute(jnp.where(g == 0, y_lo_send, y_hi_send), "grp", swap)
    else:
        y_lo = lax.ppermute(y_lo_send, "grp", down_grp)
        y_hi = lax.ppermute(y_hi_send, "grp", up_grp)
    x_lo = lax.ppermute(jnp.stack([a[-h:] for a in arrays]), "box", down_box)
    x_hi = lax.ppermute(jnp.stack([a[:h] for a in arrays]), "box", up_box)
    if grps == 2:
        def diag(db):
            return [((b - db) * 2 + 1 - g_, b * 2 + g_)
                    for b in range(boxes) if 0 <= b - db < boxes for g_ in range(2)]

        y_send = jnp.where(g == 0, y_lo_send, y_hi_send)
        cl = lax.ppermute(y_send[:, -h:], ("box", "grp"), diag(1))
        ch = lax.ppermute(y_send[:, :h], ("box", "grp"), diag(-1))
        return x_lo, x_hi, y_lo, y_hi, cl, cl, ch, ch
    corners = {}
    for name, part in (("lo", y_lo), ("hi", y_hi)):
        if name == "hi" and part is y_lo:
            corners["hi"] = corners["lo"]
            continue
        corners[name] = (
            lax.ppermute(part[:, -h:], "box", down_box),
            lax.ppermute(part[:, :h], "box", up_box),
        )
    (cl_lo, ch_lo), (cl_hi, ch_hi) = corners["lo"], corners["hi"]
    return x_lo, x_hi, y_lo, y_hi, cl_lo, cl_hi, ch_lo, ch_hi


def local(phi_start, right_side, sigma):
    cells_x, cells_y, cells_z = phi_start.shape
    boxes = lax.axis_size("box")
    grps = lax.axis_size("grp")
    nx = cells_x * boxes
    ny = cells_y * grps
    b = lax.axis_index("box")
    g = lax.axis_index("grp")
    pieces = exchange((phi_start, right_side, sigma))
    planes = cells_x + 2 * HALO
    rows = cells_y + 2 * ROW_PAD
    lanes = cells_z
    idx = jnp.stack([b * cells_x - HALO, g * cells_y - ROW_PAD, g * (cells_y // 2)]).astype(jnp.int32)
    pz = jnp.asarray(np.kron(np.eye(cells_z // 2), np.ones((2, 1))), jnp.float32)
    full = pl.BlockSpec(memory_space=pltpu.MemorySpace.VMEM)
    anywhere = pl.BlockSpec(memory_space=pltpu.MemorySpace.HBM)
    big = pltpu.VMEM((planes, rows, lanes), jnp.float32)
    phi_smooth, coarse, group_coarse = pl.pallas_call(
        functools.partial(smooth_kernel, nx, ny),
        out_shape=(
            jax.ShapeDtypeStruct((cells_x, cells_y, cells_z), jnp.float32),
            jax.ShapeDtypeStruct((cells_x // 2 * (cells_y // 2), cells_z // 2), jnp.float32),
            jax.ShapeDtypeStruct((cells_x // 2, ny // 2, cells_z // 2), jnp.float32),
        ),
        in_specs=[pl.BlockSpec(memory_space=pltpu.MemorySpace.SMEM), full]
        + [anywhere] * 11,
        out_specs=(full, full, full),
        scratch_shapes=[big] * 9
        + [
            pltpu.VMEM((rows, lanes), jnp.int32),
            pltpu.VMEM((lanes // 128, cells_y, 128), jnp.float32),
            pltpu.VMEM((cells_x // 2 * (cells_y // 2), lanes), jnp.float32),
            pltpu.SemaphoreType.DMA((3 * (3 + 4 * HALO) + 2 * (2 * HALO + HALO - 1),)),
        ],
        compiler_params=pltpu.CompilerParams(vmem_limit_bytes=60 * 1024 * 1024),
    )(idx, pz, phi_start, right_side, sigma, *pieces)
    coarse = coarse.reshape(cells_x // 2, cells_y // 2, cells_z // 2)
    if grps == 2:
        other = lax.ppermute(coarse, "grp", [(0, 1), (1, 0)])
        group_coarse = lax.dynamic_update_slice(
            group_coarse, other, (0, (1 - g) * (cells_y // 2), 0))
    else:
        group_coarse = lax.all_gather(coarse, "grp", axis=1, tiled=True)
    return phi_smooth, group_coarse


def solution(mesh):
    placed = (P("box", "grp", None), P("box", "grp", None), P("box", "grp", None))
    return jax.shard_map(
        local,
        mesh=mesh,
        in_specs=placed,
        out_specs=(P("box", "grp", None), P("box", None, None)),
        check_vma=False,
    )
```

```python
import functools

import jax
import jax.numpy as jnp
import numpy as np
from jax import lax
from jax.experimental import pallas as pl
from jax.experimental.pallas import tpu as pltpu
from jax.sharding import PartitionSpec as P

SWEEPS = 2
HALO = 2 * SWEEPS + 1
ROW_PAD = 8
PHI_ROWS = ((0, (1, 2)), (0, (3, 4)), (0, (5,)))
Y_ROWS = {
    "lo": PHI_ROWS + tuple((2, (d,)) for d in range(HALO, 0, -1))
    + tuple((1, (d,)) for d in range(HALO - 1, 0, -1)),
    "hi": PHI_ROWS + tuple((2, (d,)) for d in range(1, HALO + 1))
    + tuple((1, (d,)) for d in range(1, HALO)),
}


def harmonic(s, t):
    return 2.0 * s * t / (s + t)


def smooth_kernel(nx, ny, idx_ref, pz_ref, own_phi, own_rhs, own_sig,
                  x_lo, x_hi, y_lo, y_hi, cl_lo, cl_hi, ch_lo, ch_hi,
                  phi_out, coarse_out, group_out, ph, rs, sg, fx, fy, fz, fzl, dg, inv, par,
                  pair_buf, y_sums, sems):
    planes, rows, lanes = ph.shape
    h = HALO
    cells_x = planes - 2 * h
    cells_y = rows - 2 * ROW_PAD
    gx0 = idx_ref[0]
    gy0 = idx_ref[1]
    mid = pl.ds(h, cells_x)
    lo_p = pl.ds(0, h)
    hi_p = pl.ds(h + cells_x, h)
    own_r = pl.ds(ROW_PAD, cells_y)
    copies = []
    for a, dst, own in ((2, sg, own_sig), (0, ph, own_phi), (1, rs, own_rhs)):
        pieces = [
            (own, dst.at[mid, own_r]),
            (x_lo.at[a], dst.at[lo_p, own_r]),
            (x_hi.at[a], dst.at[hi_p, own_r]),
        ]
        for side, y_part, below, above in (("lo", y_lo, cl_lo, ch_lo), ("hi", y_hi, cl_hi, ch_hi)):
            for k, (which, depths) in enumerate(Y_ROWS[side]):
                for d in depths if which == a else ():
                    row = ROW_PAD - d if side == "lo" else ROW_PAD + cells_y - 1 + d
                    pieces += [
                        (y_part.at[k], dst.at[mid, row]),
                        (below.at[k], dst.at[lo_p, row]),
                        (above.at[k], dst.at[hi_p, row]),
                    ]
        for src_ref, dst_ref in pieces:
            cp = pltpu.make_async_copy(src_ref, dst_ref, sems.at[len(copies)])
            cp.start()
            copies.append(cp)
        if a == 2:
            per_array = len(copies)
    for cp in copies[:per_array]:
        cp.wait()
    row = lax.broadcasted_iota(jnp.int32, (rows, lanes), 0)
    lane = lax.broadcasted_iota(jnp.int32, (rows, lanes), 1)
    gy = gy0 + row
    iny = (gy >= 0) & (gy < ny)
    par[...] = jnp.where(iny, (gy + lane) & 1, 2)

    def faces_x(i, carry):
        gx = gx0 + i
        ok = (gx >= 0) & (gx + 1 < nx)
        s0 = sg[i]
        s1 = sg[i + 1]
        gyv = gy0 + lax.broadcasted_iota(jnp.int32, (rows, lanes), 0)
        inside = (gyv >= 0) & (gyv < ny) & ok
        fx[i] = jnp.where(inside, harmonic(s0, s1), 0.0)
        return carry

    lax.fori_loop(0, planes - 1, faces_x, 0, unroll=2)

    def faces_yz(i, carry):
        gx = gx0 + i
        inx = (gx >= 0) & (gx < nx)
        r = lax.broadcasted_iota(jnp.int32, (rows, lanes), 0)
        k = lax.broadcasted_iota(jnp.int32, (rows, lanes), 1)
        gyv = gy0 + r
        inyv = (gyv >= 0) & (gyv < ny)
        s = sg[i]
        s_yu = pltpu.roll(s, rows - 1, 0)
        s_zu = pltpu.roll(s, lanes - 1, 1)
        wy = jnp.where(inx & (gyv >= 0) & (gyv + 1 < ny), harmonic(s, s_yu), 0.0)
        wz = jnp.where(inx & inyv & (k < lanes - 1), harmonic(s, s_zu), 0.0)
        wy_lo = pltpu.roll(wy, 1, 0)
        wz_lo = pltpu.roll(wz, 1, 1)
        fy[i] = wy
        fz[i] = wz
        fzl[i] = wz_lo
        wxl = jnp.where(gx == 0, s, fx[i - 1])
        wxu = jnp.where(gx == nx - 1, s, fx[i])
        wyl = jnp.where(gyv == 0, s, wy_lo)
        wyu = jnp.where(gyv == ny - 1, s, wy)
        wzl = jnp.where(k == 0, s, wz_lo)
        wzu = jnp.where(k == lanes - 1, s, wz)
        d = wxl + wxu + wyl + wyu + wzl + wzu
        dg[i] = d
        inv[i] = 1.0 / d
        sg[i] = wy_lo
        return carry

    lax.fori_loop(1, planes - 1, faces_yz, 0, unroll=2)
    for cp in copies[per_array:]:
        cp.wait()

    def coupled_sum(i, pc):
        wy = fy[i]
        wz = fz[i]
        terms = (
            (fx[i - 1], ph[i - 1]),
            (fx[i], ph[i + 1]),
            (sg[i], pltpu.roll(pc, 1, 0)),
            (wy, pltpu.roll(pc, rows - 1, 0)),
            (fzl[i], pltpu.roll(pc, 1, 1)),
            (wz, pltpu.roll(pc, lanes - 1, 1)),
        )
        return terms

    for turn in range(2 * SWEEPS):
        colour = turn % 2

        def relax(i, carry, colour=colour):
            gx = gx0 + i
            inx = (gx >= 0) & (gx < nx)
            target = jnp.where(inx, (gx + colour) & 1, 3)
            pc = ph[i]
            summed = rs[i]
            for w, nb in coupled_sum(i, pc):
                summed = summed + w * nb
            ph[i] = jnp.where(par[...] == target, summed * inv[i], pc)
            return carry

        lax.fori_loop(turn + 1, planes - 1 - turn, relax, 0, unroll=2)

    own_rows = rows - 2 * ROW_PAD
    half_rows = own_rows // 2

    def defect_plane(i):
        pc = ph[i]
        terms = coupled_sum(i, pc)
        coupled = terms[0][0] * terms[0][1]
        for w, nb in terms[1:]:
            coupled = coupled + w * nb
        d = rs[i] - (dg[i] * pc - coupled)
        phi_out[i - HALO] = pc[ROW_PAD:ROW_PAD + own_rows]
        return d[ROW_PAD:ROW_PAD + own_rows]

    def restrict(j, carry):
        i = HALO + 2 * j
        pair = defect_plane(i) + defect_plane(i + 1)
        halves = []
        for q in range(lanes // 128):
            pair_buf[q] = pair[:, q * 128:(q + 1) * 128]
            even = pair_buf[q, pl.ds(0, half_rows, stride=2), :]
            odd = pair_buf[q, pl.ds(1, half_rows, stride=2), :]
            halves.append(even + odd)
        y_sums[pl.ds(pl.multiple_of(j * half_rows, half_rows), half_rows), :] = (
            jnp.concatenate(halves, axis=1))
        return carry

    lax.fori_loop(0, (planes - 2 * HALO) // 2, restrict, 0)
    coarse = 0.125 * jnp.dot(
        y_sums[...], pz_ref[...], precision=lax.Precision.HIGHEST,
        preferred_element_type=jnp.float32)
    coarse_out[...] = coarse
    first = idx_ref[2]
    for j in range(cells_x // 2):
        group_out[j, pl.ds(first, half_rows), :] = coarse[j * half_rows:(j + 1) * half_rows]


def exchange(arrays):
    boxes = lax.axis_size("box")
    grps = lax.axis_size("grp")
    h = HALO
    down_box = [(i, i + 1) for i in range(boxes - 1)]
    up_box = [(i + 1, i) for i in range(boxes - 1)]
    down_grp = [(i, i + 1) for i in range(grps - 1)]
    up_grp = [(i + 1, i) for i in range(grps - 1)]
    cells_x, cells_y, cells_z = arrays[0].shape
    gx = lax.axis_index("box") * cells_x + jnp.arange(cells_x, dtype=jnp.int32)[:, None]
    z = jnp.arange(cells_z, dtype=jnp.int32)[None, :]

    gy0 = lax.axis_index("grp") * cells_y

    def y_piece(side, block, slab_of):
        slabs = [jnp.swapaxes(a[:, block], 0, 1) for a in arrays]
        row_of = (lambda d: cells_y - d) if side == "lo" else (lambda d: d - 1)
        pairs = [depths for _, depths in PHI_ROWS if len(depths) == 2]
        colour1 = jnp.stack([(gx + gy0 + row_of(p[0]) + z) % 2 == 1 for p in pairs])
        first = jnp.stack([slabs[0][slab_of(p[0])] for p in pairs])
        second = jnp.stack([slabs[0][slab_of(p[1])] for p in pairs])
        single = [slabs[0][slab_of(d)][None] for _, (d, *more) in PHI_ROWS if not more]
        sig = slabs[2]
        rhs = slabs[1][1:] if side == "lo" else slabs[1][:-1]
        return jnp.concatenate([jnp.where(colour1, first, second)] + single + [sig, rhs])

    g = lax.axis_index("grp")
    swap = [(0, 1), (1, 0)]
    if grps == 2:
        top = g == 0
        slabs = [
            jnp.swapaxes(lax.dynamic_slice_in_dim(a, jnp.where(top, cells_y - h, 0), h, 1), 0, 1)
            for a in arrays
        ]
        lo_phi = [(h - 1, h - 2), (h - 3, h - 4), (0,)]
        hi_phi = [(0, 1), (2, 3), (h - 1,)]
        rows = []
        for lo_idx, hi_idx in zip(lo_phi, hi_phi):
            pick = lambda n: jnp.where(top, slabs[0][lo_idx[n]], slabs[0][hi_idx[n]])
            if len(lo_idx) == 2:
                gy = g * cells_y + jnp.where(top, cells_y - 1 - (lo_idx == lo_phi[1]) * 2,
                                             (lo_idx == lo_phi[1]) * 2)
                rows.append(jnp.where((gx + gy + z) % 2 == 1, pick(0), pick(1))[None])
            else:
                rows.append(pick(0)[None])
        rhs = jnp.swapaxes(
            lax.dynamic_slice_in_dim(arrays[1], jnp.where(top, cells_y - h + 1, 0), h - 1, 1), 0, 1)
        y_send = jnp.concatenate(rows + [slabs[2], rhs])
        y_lo = y_hi = lax.ppermute(y_send, "grp", swap)
    else:
        y_lo_send = y_piece("lo", slice(-h, None), lambda d: h - d)
        y_hi_send = y_piece("hi", slice(0, h), lambda d: d - 1)
        y_lo = lax.ppermute(y_lo_send, "grp", down_grp)
        y_hi = lax.ppermute(y_hi_send, "grp", up_grp)
    x_lo = lax.ppermute(jnp.stack([a[-h:] for a in arrays]), "box", down_box)
    x_hi = lax.ppermute(jnp.stack([a[:h] for a in arrays]), "box", up_box)
    if grps == 2:
        def diag(db):
            return [((b - db) * 2 + 1 - g_, b * 2 + g_)
                    for b in range(boxes) if 0 <= b - db < boxes for g_ in range(2)]

        cl = lax.ppermute(y_send[:, -h:], ("box", "grp"), diag(1))
        ch = lax.ppermute(y_send[:, :h], ("box", "grp"), diag(-1))
        return x_lo, x_hi, y_lo, y_hi, cl, cl, ch, ch
    corners = {}
    for name, part in (("lo", y_lo), ("hi", y_hi)):
        if name == "hi" and part is y_lo:
            corners["hi"] = corners["lo"]
            continue
        corners[name] = (
            lax.ppermute(part[:, -h:], "box", down_box),
            lax.ppermute(part[:, :h], "box", up_box),
        )
    (cl_lo, ch_lo), (cl_hi, ch_hi) = corners["lo"], corners["hi"]
    return x_lo, x_hi, y_lo, y_hi, cl_lo, cl_hi, ch_lo, ch_hi


def local(phi_start, right_side, sigma):
    cells_x, cells_y, cells_z = phi_start.shape
    boxes = lax.axis_size("box")
    grps = lax.axis_size("grp")
    nx = cells_x * boxes
    ny = cells_y * grps
    b = lax.axis_index("box")
    g = lax.axis_index("grp")
    pieces = exchange((phi_start, right_side, sigma))
    planes = cells_x + 2 * HALO
    rows = cells_y + 2 * ROW_PAD
    lanes = cells_z
    idx = jnp.stack([b * cells_x - HALO, g * cells_y - ROW_PAD, g * (cells_y // 2)]).astype(jnp.int32)
    pz = jnp.asarray(np.kron(np.eye(cells_z // 2), np.ones((2, 1))), jnp.float32)
    full = pl.BlockSpec(memory_space=pltpu.MemorySpace.VMEM)
    anywhere = pl.BlockSpec(memory_space=pltpu.MemorySpace.HBM)
    big = pltpu.VMEM((planes, rows, lanes), jnp.float32)
    phi_smooth, coarse, group_coarse = pl.pallas_call(
        functools.partial(smooth_kernel, nx, ny),
        out_shape=(
            jax.ShapeDtypeStruct((cells_x, cells_y, cells_z), jnp.float32),
            jax.ShapeDtypeStruct((cells_x // 2 * (cells_y // 2), cells_z // 2), jnp.float32),
            jax.ShapeDtypeStruct((cells_x // 2, ny // 2, cells_z // 2), jnp.float32),
        ),
        in_specs=[pl.BlockSpec(memory_space=pltpu.MemorySpace.SMEM), full]
        + [anywhere] * 11,
        out_specs=(full, full, full),
        scratch_shapes=[big] * 9
        + [
            pltpu.VMEM((rows, lanes), jnp.int32),
            pltpu.VMEM((lanes // 128, cells_y, 128), jnp.float32),
            pltpu.VMEM((cells_x // 2 * (cells_y // 2), lanes), jnp.float32),
            pltpu.SemaphoreType.DMA((3 * (3 + 4 * HALO) + 2 * (2 * HALO + HALO - 1),)),
        ],
        compiler_params=pltpu.CompilerParams(vmem_limit_bytes=60 * 1024 * 1024),
    )(idx, pz, phi_start, right_side, sigma, *pieces)
    coarse = coarse.reshape(cells_x // 2, cells_y // 2, cells_z // 2)
    if grps == 2:
        other = lax.ppermute(coarse, "grp", [(0, 1), (1, 0)])
        group_coarse = lax.dynamic_update_slice(
            group_coarse, other, (0, (1 - g) * (cells_y // 2), 0))
    else:
        group_coarse = lax.all_gather(coarse, "grp", axis=1, tiled=True)
    return phi_smooth, group_coarse


def solution(mesh):
    placed = (P("box", "grp", None), P("box", "grp", None), P("box", "grp", None))
    return jax.shard_map(
        local,
        mesh=mesh,
        in_specs=placed,
        out_specs=(P("box", "grp", None), P("box", None, None)),
        check_vma=False,
    )
```

```python
import functools

import jax
import jax.numpy as jnp
import numpy as np
from jax import lax
from jax.experimental import pallas as pl
from jax.experimental.pallas import tpu as pltpu
from jax.sharding import PartitionSpec as P

SWEEPS = 2
HALO = 2 * SWEEPS + 1
ROW_PAD = 8
PHI_ROWS = ((0, (1, 2)), (0, (3, 4)), (0, (5,)))
Y_ROWS = {
    "lo": PHI_ROWS + tuple((2, (d,)) for d in range(HALO, 0, -1))
    + tuple((1, (d,)) for d in range(HALO - 1, 0, -1)),
    "hi": PHI_ROWS + tuple((2, (d,)) for d in range(1, HALO + 1))
    + tuple((1, (d,)) for d in range(1, HALO)),
}


def harmonic(s, t):
    return 2.0 * s * t / (s + t)


def smooth_kernel(nx, ny, idx_ref, pz_ref, own_phi, own_rhs, own_sig,
                  x_lo, x_hi, y_lo, y_hi, cl_lo, cl_hi, ch_lo, ch_hi,
                  phi_out, coarse_out, group_out, ph, rs, sg, fx, fy, fz, fzl, dg, inv, par,
                  pair_buf, y_sums, sems):
    planes, rows, lanes = ph.shape
    h = HALO
    cells_x = planes - 2 * h
    cells_y = rows - 2 * ROW_PAD
    gx0 = idx_ref[0]
    gy0 = idx_ref[1]
    mid = pl.ds(h, cells_x)
    lo_p = pl.ds(0, h)
    hi_p = pl.ds(h + cells_x, h)
    own_r = pl.ds(ROW_PAD, cells_y)
    copies = []
    for a, dst, own in ((2, sg, own_sig), (0, ph, own_phi), (1, rs, own_rhs)):
        pieces = [
            (own, dst.at[mid, own_r]),
            (x_lo.at[a], dst.at[lo_p, own_r]),
            (x_hi.at[a], dst.at[hi_p, own_r]),
        ]
        for side, y_part, below, above in (("lo", y_lo, cl_lo, ch_lo), ("hi", y_hi, cl_hi, ch_hi)):
            for k, (which, depths) in enumerate(Y_ROWS[side]):
                for d in depths if which == a else ():
                    row = ROW_PAD - d if side == "lo" else ROW_PAD + cells_y - 1 + d
                    pieces += [
                        (y_part.at[k], dst.at[mid, row]),
                        (below.at[k], dst.at[lo_p, row]),
                        (above.at[k], dst.at[hi_p, row]),
                    ]
        for src_ref, dst_ref in pieces:
            cp = pltpu.make_async_copy(src_ref, dst_ref, sems.at[len(copies)])
            cp.start()
            copies.append(cp)
        if a == 2:
            per_array = len(copies)
    for cp in copies[:per_array]:
        cp.wait()
    row = lax.broadcasted_iota(jnp.int32, (rows, lanes), 0)
    lane = lax.broadcasted_iota(jnp.int32, (rows, lanes), 1)
    gy = gy0 + row
    iny = (gy >= 0) & (gy < ny)
    par[...] = jnp.where(iny, (gy + lane) & 1, 2)

    def faces_x(i, carry):
        gx = gx0 + i
        ok = (gx >= 0) & (gx + 1 < nx)
        s0 = sg[i]
        s1 = sg[i + 1]
        gyv = gy0 + lax.broadcasted_iota(jnp.int32, (rows, lanes), 0)
        inside = (gyv >= 0) & (gyv < ny) & ok
        fx[i] = jnp.where(inside, harmonic(s0, s1), 0.0)
        return carry

    lax.fori_loop(0, planes - 1, faces_x, 0, unroll=2)

    def faces_yz(i, carry):
        gx = gx0 + i
        inx = (gx >= 0) & (gx < nx)
        r = lax.broadcasted_iota(jnp.int32, (rows, lanes), 0)
        k = lax.broadcasted_iota(jnp.int32, (rows, lanes), 1)
        gyv = gy0 + r
        inyv = (gyv >= 0) & (gyv < ny)
        s = sg[i]
        s_yu = pltpu.roll(s, rows - 1, 0)
        s_zu = pltpu.roll(s, lanes - 1, 1)
        wy = jnp.where(inx & (gyv >= 0) & (gyv + 1 < ny), harmonic(s, s_yu), 0.0)
        wz = jnp.where(inx & inyv & (k < lanes - 1), harmonic(s, s_zu), 0.0)
        wy_lo = pltpu.roll(wy, 1, 0)
        wz_lo = pltpu.roll(wz, 1, 1)
        fy[i] = wy
        fz[i] = wz
        fzl[i] = wz_lo
        wxl = jnp.where(gx == 0, s, fx[i - 1])
        wxu = jnp.where(gx == nx - 1, s, fx[i])
        wyl = jnp.where(gyv == 0, s, wy_lo)
        wyu = jnp.where(gyv == ny - 1, s, wy)
        wzl = jnp.where(k == 0, s, wz_lo)
        wzu = jnp.where(k == lanes - 1, s, wz)
        d = wxl + wxu + wyl + wyu + wzl + wzu
        dg[i] = d
        inv[i] = 1.0 / d
        sg[i] = wy_lo
        return carry

    lax.fori_loop(1, planes - 1, faces_yz, 0, unroll=2)
    for cp in copies[per_array:]:
        cp.wait()

    def coupled_sum(i, pc):
        wy = fy[i]
        wz = fz[i]
        terms = (
            (fx[i - 1], ph[i - 1]),
            (fx[i], ph[i + 1]),
            (sg[i], pltpu.roll(pc, 1, 0)),
            (wy, pltpu.roll(pc, rows - 1, 0)),
            (fzl[i], pltpu.roll(pc, 1, 1)),
            (wz, pltpu.roll(pc, lanes - 1, 1)),
        )
        return terms

    for turn in range(2 * SWEEPS):
        colour = turn % 2

        def relax(i, carry, colour=colour):
            gx = gx0 + i
            inx = (gx >= 0) & (gx < nx)
            target = jnp.where(inx, (gx + colour) & 1, 3)
            pc = ph[i]
            summed = rs[i]
            for w, nb in coupled_sum(i, pc):
                summed = summed + w * nb
            ph[i] = jnp.where(par[...] == target, summed * inv[i], pc)
            return carry

        lax.fori_loop(turn + 1, planes - 1 - turn, relax, 0, unroll=2)

    own_rows = rows - 2 * ROW_PAD
    half_rows = own_rows // 2

    def defect_plane(i):
        pc = ph[i]
        terms = coupled_sum(i, pc)
        coupled = terms[0][0] * terms[0][1]
        for w, nb in terms[1:]:
            coupled = coupled + w * nb
        d = rs[i] - (dg[i] * pc - coupled)
        phi_out[i - HALO] = pc[ROW_PAD:ROW_PAD + own_rows]
        return d[ROW_PAD:ROW_PAD + own_rows]

    def restrict(j, carry):
        i = HALO + 2 * j
        pair = defect_plane(i) + defect_plane(i + 1)
        halves = []
        for q in range(lanes // 128):
            pair_buf[q] = pair[:, q * 128:(q + 1) * 128]
            even = pair_buf[q, pl.ds(0, half_rows, stride=2), :]
            odd = pair_buf[q, pl.ds(1, half_rows, stride=2), :]
            halves.append(even + odd)
        y_sums[pl.ds(pl.multiple_of(j * half_rows, half_rows), half_rows), :] = (
            jnp.concatenate(halves, axis=1))
        return carry

    lax.fori_loop(0, (planes - 2 * HALO) // 2, restrict, 0)
    coarse = 0.125 * jnp.dot(
        y_sums[...], pz_ref[...], precision=lax.Precision.HIGHEST,
        preferred_element_type=jnp.float32)
    coarse_out[...] = coarse
    first = idx_ref[2]
    for j in range(cells_x // 2):
        group_out[j, pl.ds(first, half_rows), :] = coarse[j * half_rows:(j + 1) * half_rows]


def y_send_kernel(pos_ref, phi, rhs, sig, out, stage, sems):
    planes, lanes = stage.shape[2], stage.shape[3]
    h = HALO
    top = pos_ref[2] == 0
    first = pos_ref[3]
    copies = []
    for a, src_ref in ((0, phi), (1, rhs), (2, sig)):
        for r in range(h):
            cp = pltpu.make_async_copy(src_ref.at[:, first + r], stage.at[a, r], sems.at[len(copies)])
            cp.start()
            copies.append(cp)
    for cp in copies:
        cp.wait()
    plane = lax.broadcasted_iota(jnp.int32, (planes, lanes), 0)
    z = lax.broadcasted_iota(jnp.int32, (planes, lanes), 1)
    parity = (pos_ref[0] + pos_ref[1] + first + plane + z) & 1
    for k, (lo_pair, hi_pair) in enumerate((((4, 3), (0, 1)), ((2, 1), (2, 3)))):
        a0 = jnp.where(top, stage[0, lo_pair[0]], stage[0, hi_pair[0]])
        a1 = jnp.where(top, stage[0, lo_pair[1]], stage[0, hi_pair[1]])
        offset = jnp.where(top, lo_pair[0], hi_pair[0])
        colour1 = ((parity + offset) & 1) == 1
        out[k] = jnp.where(colour1, a0, a1)
    out[2] = jnp.where(top, stage[0, 0], stage[0, h - 1])
    for r in range(h):
        out[3 + r] = stage[2, r]
    for r in range(h - 1):
        out[3 + h + r] = jnp.where(top, stage[1, r + 1], stage[1, r])


def exchange(arrays):
    boxes = lax.axis_size("box")
    grps = lax.axis_size("grp")
    h = HALO
    down_box = [(i, i + 1) for i in range(boxes - 1)]
    up_box = [(i + 1, i) for i in range(boxes - 1)]
    down_grp = [(i, i + 1) for i in range(grps - 1)]
    up_grp = [(i + 1, i) for i in range(grps - 1)]
    cells_x, cells_y, cells_z = arrays[0].shape
    gx = lax.axis_index("box") * cells_x + jnp.arange(cells_x, dtype=jnp.int32)[:, None]
    z = jnp.arange(cells_z, dtype=jnp.int32)[None, :]

    gy0 = lax.axis_index("grp") * cells_y

    def y_piece(side, block, slab_of):
        slabs = [jnp.swapaxes(a[:, block], 0, 1) for a in arrays]
        row_of = (lambda d: cells_y - d) if side == "lo" else (lambda d: d - 1)
        pairs = [depths for _, depths in PHI_ROWS if len(depths) == 2]
        colour1 = jnp.stack([(gx + gy0 + row_of(p[0]) + z) % 2 == 1 for p in pairs])
        first = jnp.stack([slabs[0][slab_of(p[0])] for p in pairs])
        second = jnp.stack([slabs[0][slab_of(p[1])] for p in pairs])
        single = [slabs[0][slab_of(d)][None] for _, (d, *more) in PHI_ROWS if not more]
        sig = slabs[2]
        rhs = slabs[1][1:] if side == "lo" else slabs[1][:-1]
        return jnp.concatenate([jnp.where(colour1, first, second)] + single + [sig, rhs])

    g = lax.axis_index("grp")
    swap = [(0, 1), (1, 0)]
    if grps == 2:
        first = jnp.where(g == 0, cells_y - h, 0)
        pos = jnp.stack([lax.axis_index("box") * cells_x, g * cells_y, g, first]).astype(jnp.int32)
        hbm = pl.BlockSpec(memory_space=pltpu.MemorySpace.HBM)
        y_send = pl.pallas_call(
            y_send_kernel,
            out_shape=jax.ShapeDtypeStruct((len(Y_ROWS["lo"]), cells_x, cells_z), jnp.float32),
            in_specs=[pl.BlockSpec(memory_space=pltpu.MemorySpace.SMEM), hbm, hbm, hbm],
            out_specs=pl.BlockSpec(memory_space=pltpu.MemorySpace.VMEM),
            scratch_shapes=[
                pltpu.VMEM((3, h, cells_x, cells_z), jnp.float32),
                pltpu.SemaphoreType.DMA((3 * h,)),
            ],
        )(pos, *arrays)
        y_lo = y_hi = lax.ppermute(y_send, "grp", swap)
    else:
        y_lo_send = y_piece("lo", slice(-h, None), lambda d: h - d)
        y_hi_send = y_piece("hi", slice(0, h), lambda d: d - 1)
        y_lo = lax.ppermute(y_lo_send, "grp", down_grp)
        y_hi = lax.ppermute(y_hi_send, "grp", up_grp)
    x_lo = lax.ppermute(jnp.stack([a[-h:] for a in arrays]), "box", down_box)
    x_hi = lax.ppermute(jnp.stack([a[:h] for a in arrays]), "box", up_box)
    if grps == 2:
        def diag(db):
            return [((b - db) * 2 + 1 - g_, b * 2 + g_)
                    for b in range(boxes) if 0 <= b - db < boxes for g_ in range(2)]

        cl = lax.ppermute(y_send[:, -h:], ("box", "grp"), diag(1))
        ch = lax.ppermute(y_send[:, :h], ("box", "grp"), diag(-1))
        return x_lo, x_hi, y_lo, y_hi, cl, cl, ch, ch
    corners = {}
    for name, part in (("lo", y_lo), ("hi", y_hi)):
        if name == "hi" and part is y_lo:
            corners["hi"] = corners["lo"]
            continue
        corners[name] = (
            lax.ppermute(part[:, -h:], "box", down_box),
            lax.ppermute(part[:, :h], "box", up_box),
        )
    (cl_lo, ch_lo), (cl_hi, ch_hi) = corners["lo"], corners["hi"]
    return x_lo, x_hi, y_lo, y_hi, cl_lo, cl_hi, ch_lo, ch_hi


def local(phi_start, right_side, sigma):
    cells_x, cells_y, cells_z = phi_start.shape
    boxes = lax.axis_size("box")
    grps = lax.axis_size("grp")
    nx = cells_x * boxes
    ny = cells_y * grps
    b = lax.axis_index("box")
    g = lax.axis_index("grp")
    pieces = exchange((phi_start, right_side, sigma))
    planes = cells_x + 2 * HALO
    rows = cells_y + 2 * ROW_PAD
    lanes = cells_z
    idx = jnp.stack([b * cells_x - HALO, g * cells_y - ROW_PAD, g * (cells_y // 2)]).astype(jnp.int32)
    pz = jnp.asarray(np.kron(np.eye(cells_z // 2), np.ones((2, 1))), jnp.float32)
    full = pl.BlockSpec(memory_space=pltpu.MemorySpace.VMEM)
    anywhere = pl.BlockSpec(memory_space=pltpu.MemorySpace.HBM)
    big = pltpu.VMEM((planes, rows, lanes), jnp.float32)
    phi_smooth, coarse, group_coarse = pl.pallas_call(
        functools.partial(smooth_kernel, nx, ny),
        out_shape=(
            jax.ShapeDtypeStruct((cells_x, cells_y, cells_z), jnp.float32),
            jax.ShapeDtypeStruct((cells_x // 2 * (cells_y // 2), cells_z // 2), jnp.float32),
            jax.ShapeDtypeStruct((cells_x // 2, ny // 2, cells_z // 2), jnp.float32),
        ),
        in_specs=[pl.BlockSpec(memory_space=pltpu.MemorySpace.SMEM), full]
        + [anywhere] * 11,
        out_specs=(full, full, full),
        scratch_shapes=[big] * 9
        + [
            pltpu.VMEM((rows, lanes), jnp.int32),
            pltpu.VMEM((lanes // 128, cells_y, 128), jnp.float32),
            pltpu.VMEM((cells_x // 2 * (cells_y // 2), lanes), jnp.float32),
            pltpu.SemaphoreType.DMA((3 * (3 + 4 * HALO) + 2 * (2 * HALO + HALO - 1),)),
        ],
        compiler_params=pltpu.CompilerParams(vmem_limit_bytes=60 * 1024 * 1024),
    )(idx, pz, phi_start, right_side, sigma, *pieces)
    coarse = coarse.reshape(cells_x // 2, cells_y // 2, cells_z // 2)
    if grps == 2:
        other = lax.ppermute(coarse, "grp", [(0, 1), (1, 0)])
        group_coarse = lax.dynamic_update_slice(
            group_coarse, other, (0, (1 - g) * (cells_y // 2), 0))
    else:
        group_coarse = lax.all_gather(coarse, "grp", axis=1, tiled=True)
    return phi_smooth, group_coarse


def solution(mesh):
    placed = (P("box", "grp", None), P("box", "grp", None), P("box", "grp", None))
    return jax.shard_map(
        local,
        mesh=mesh,
        in_specs=placed,
        out_specs=(P("box", "grp", None), P("box", None, None)),
        check_vma=False,
    )
```

```python
import functools

import jax
import jax.numpy as jnp
import numpy as np
from jax import lax
from jax.experimental import pallas as pl
from jax.experimental.pallas import tpu as pltpu
from jax.sharding import PartitionSpec as P

SWEEPS = 2
HALO = 2 * SWEEPS + 1
ROW_PAD = 8
PHI_ROWS = ((0, (1, 2)), (0, (3, 4)), (0, (5,)))
Y_ROWS = {
    "lo": PHI_ROWS + tuple((2, (d,)) for d in range(HALO, 0, -1))
    + tuple((1, (d,)) for d in range(HALO - 1, 0, -1)),
    "hi": PHI_ROWS + tuple((2, (d,)) for d in range(1, HALO + 1))
    + tuple((1, (d,)) for d in range(1, HALO)),
}


def harmonic(s, t):
    return 2.0 * s * t / (s + t)


def smooth_kernel(nx, ny, idx_ref, pz_ref, own_phi, own_rhs, own_sig,
                  x_lo, x_hi, y_lo, y_hi, cl_lo, cl_hi, ch_lo, ch_hi,
                  phi_out, coarse_out, group_out, ph, rs, sg, fx, fy, fz, fzl, dg, inv, par,
                  pair_buf, y_sums, sems):
    planes, rows, lanes = ph.shape
    h = HALO
    cells_x = planes - 2 * h
    cells_y = rows - 2 * ROW_PAD
    gx0 = idx_ref[0]
    gy0 = idx_ref[1]
    mid = pl.ds(h, cells_x)
    lo_p = pl.ds(0, h)
    hi_p = pl.ds(h + cells_x, h)
    own_r = pl.ds(ROW_PAD, cells_y)
    copies = []
    for a, dst, own in ((2, sg, own_sig), (0, ph, own_phi), (1, rs, own_rhs)):
        pieces = [
            (own, dst.at[mid, own_r]),
            (x_lo.at[a], dst.at[lo_p, own_r]),
            (x_hi.at[a], dst.at[hi_p, own_r]),
        ]
        for side, y_part, below, above in (("lo", y_lo, cl_lo, ch_lo), ("hi", y_hi, cl_hi, ch_hi)):
            for k, (which, depths) in enumerate(Y_ROWS[side]):
                for d in depths if which == a else ():
                    row = ROW_PAD - d if side == "lo" else ROW_PAD + cells_y - 1 + d
                    pieces += [
                        (y_part.at[k], dst.at[mid, row]),
                        (below.at[k], dst.at[lo_p, row]),
                        (above.at[k], dst.at[hi_p, row]),
                    ]
        for src_ref, dst_ref in pieces:
            cp = pltpu.make_async_copy(src_ref, dst_ref, sems.at[len(copies)])
            cp.start()
            copies.append(cp)
        if a == 2:
            per_array = len(copies)
    for cp in copies[:per_array]:
        cp.wait()
    row = lax.broadcasted_iota(jnp.int32, (rows, lanes), 0)
    lane = lax.broadcasted_iota(jnp.int32, (rows, lanes), 1)
    gy = gy0 + row
    iny = (gy >= 0) & (gy < ny)
    par[...] = jnp.where(iny, (gy + lane) & 1, 2)

    def faces_x(i, carry):
        gx = gx0 + i
        ok = (gx >= 0) & (gx + 1 < nx)
        s0 = sg[i]
        s1 = sg[i + 1]
        gyv = gy0 + lax.broadcasted_iota(jnp.int32, (rows, lanes), 0)
        inside = (gyv >= 0) & (gyv < ny) & ok
        fx[i] = jnp.where(inside, harmonic(s0, s1), 0.0)
        return carry

    lax.fori_loop(0, planes - 1, faces_x, 0, unroll=2)

    def faces_yz(i, carry):
        gx = gx0 + i
        inx = (gx >= 0) & (gx < nx)
        r = lax.broadcasted_iota(jnp.int32, (rows, lanes), 0)
        k = lax.broadcasted_iota(jnp.int32, (rows, lanes), 1)
        gyv = gy0 + r
        inyv = (gyv >= 0) & (gyv < ny)
        s = sg[i]
        s_yu = pltpu.roll(s, rows - 1, 0)
        s_zu = pltpu.roll(s, lanes - 1, 1)
        wy = jnp.where(inx & (gyv >= 0) & (gyv + 1 < ny), harmonic(s, s_yu), 0.0)
        wz = jnp.where(inx & inyv & (k < lanes - 1), harmonic(s, s_zu), 0.0)
        wy_lo = pltpu.roll(wy, 1, 0)
        wz_lo = pltpu.roll(wz, 1, 1)
        fy[i] = wy
        fz[i] = wz
        fzl[i] = wz_lo
        wxl = jnp.where(gx == 0, s, fx[i - 1])
        wxu = jnp.where(gx == nx - 1, s, fx[i])
        wyl = jnp.where(gyv == 0, s, wy_lo)
        wyu = jnp.where(gyv == ny - 1, s, wy)
        wzl = jnp.where(k == 0, s, wz_lo)
        wzu = jnp.where(k == lanes - 1, s, wz)
        d = wxl + wxu + wyl + wyu + wzl + wzu
        dg[i] = d
        inv[i] = 1.0 / d
        sg[i] = wy_lo
        return carry

    lax.fori_loop(1, planes - 1, faces_yz, 0, unroll=2)
    for cp in copies[per_array:]:
        cp.wait()

    def coupled_sum(i, pc):
        wy = fy[i]
        wz = fz[i]
        terms = (
            (fx[i - 1], ph[i - 1]),
            (fx[i], ph[i + 1]),
            (sg[i], pltpu.roll(pc, 1, 0)),
            (wy, pltpu.roll(pc, rows - 1, 0)),
            (fzl[i], pltpu.roll(pc, 1, 1)),
            (wz, pltpu.roll(pc, lanes - 1, 1)),
        )
        return terms

    for turn in range(2 * SWEEPS):
        colour = turn % 2

        def relax(i, carry, colour=colour):
            gx = gx0 + i
            inx = (gx >= 0) & (gx < nx)
            target = jnp.where(inx, (gx + colour) & 1, 3)
            pc = ph[i]
            summed = rs[i]
            for w, nb in coupled_sum(i, pc):
                summed = summed + w * nb
            ph[i] = jnp.where(par[...] == target, summed * inv[i], pc)
            return carry

        lax.fori_loop(turn + 1, planes - 1 - turn, relax, 0, unroll=2)

    own_rows = rows - 2 * ROW_PAD
    half_rows = own_rows // 2

    def defect_plane(i):
        pc = ph[i]
        terms = coupled_sum(i, pc)
        coupled = terms[0][0] * terms[0][1]
        for w, nb in terms[1:]:
            coupled = coupled + w * nb
        d = rs[i] - (dg[i] * pc - coupled)
        phi_out[i - HALO] = pc[ROW_PAD:ROW_PAD + own_rows]
        return d[ROW_PAD:ROW_PAD + own_rows]

    def restrict(j, carry):
        i = HALO + 2 * j
        pair = defect_plane(i) + defect_plane(i + 1)
        halves = []
        for q in range(lanes // 128):
            pair_buf[q] = pair[:, q * 128:(q + 1) * 128]
            even = pair_buf[q, pl.ds(0, half_rows, stride=2), :]
            odd = pair_buf[q, pl.ds(1, half_rows, stride=2), :]
            halves.append(even + odd)
        y_sums[pl.ds(pl.multiple_of(j * half_rows, half_rows), half_rows), :] = (
            jnp.concatenate(halves, axis=1))
        return carry

    lax.fori_loop(0, (planes - 2 * HALO) // 2, restrict, 0)
    coarse = 0.125 * jnp.dot(
        y_sums[...], pz_ref[...], precision=lax.Precision.HIGHEST,
        preferred_element_type=jnp.float32)
    coarse_out[...] = coarse
    first = idx_ref[2]
    for j in range(cells_x // 2):
        group_out[j, pl.ds(first, half_rows), :] = coarse[j * half_rows:(j + 1) * half_rows]


def y_send_kernel(pos_ref, phi, rhs, sig, out, stage, sems):
    planes, lanes = stage.shape[1], stage.shape[2]
    h = HALO
    top = pos_ref[2] == 0
    first = pos_ref[3]
    shift = jnp.where(top, 1, 0)
    moves = [(phi.at[:, first + shift + r], stage.at[r]) for r in range(h - 1)]
    moves.append((phi.at[:, first + jnp.where(top, 0, h - 1)], out.at[2]))
    moves += [(sig.at[:, first + r], out.at[3 + r]) for r in range(h)]
    moves += [(rhs.at[:, first + r + jnp.where(top, 1, 0)], out.at[3 + h + r]) for r in range(h - 1)]
    copies = []
    for src_ref, dst_ref in moves:
        cp = pltpu.make_async_copy(src_ref, dst_ref, sems.at[len(copies)])
        cp.start()
        copies.append(cp)
    for cp in copies[:h - 1]:
        cp.wait()
    plane = lax.broadcasted_iota(jnp.int32, (planes, lanes), 0)
    z = lax.broadcasted_iota(jnp.int32, (planes, lanes), 1)
    parity = (pos_ref[0] + pos_ref[1] + first + plane + z) & 1
    for k, (lo_pair, hi_pair) in enumerate((((4, 3), (0, 1)), ((2, 1), (2, 3)))):
        a0 = stage[jnp.where(top, lo_pair[0] - 1, hi_pair[0])]
        a1 = stage[jnp.where(top, lo_pair[1] - 1, hi_pair[1])]
        offset = jnp.where(top, lo_pair[0], hi_pair[0])
        colour1 = ((parity + offset) & 1) == 1
        out[k] = jnp.where(colour1, a0, a1)
    for cp in copies[h - 1:]:
        cp.wait()


def exchange(arrays):
    boxes = lax.axis_size("box")
    grps = lax.axis_size("grp")
    h = HALO
    down_box = [(i, i + 1) for i in range(boxes - 1)]
    up_box = [(i + 1, i) for i in range(boxes - 1)]
    down_grp = [(i, i + 1) for i in range(grps - 1)]
    up_grp = [(i + 1, i) for i in range(grps - 1)]
    cells_x, cells_y, cells_z = arrays[0].shape
    gx = lax.axis_index("box") * cells_x + jnp.arange(cells_x, dtype=jnp.int32)[:, None]
    z = jnp.arange(cells_z, dtype=jnp.int32)[None, :]

    gy0 = lax.axis_index("grp") * cells_y

    def y_piece(side, block, slab_of):
        slabs = [jnp.swapaxes(a[:, block], 0, 1) for a in arrays]
        row_of = (lambda d: cells_y - d) if side == "lo" else (lambda d: d - 1)
        pairs = [depths for _, depths in PHI_ROWS if len(depths) == 2]
        colour1 = jnp.stack([(gx + gy0 + row_of(p[0]) + z) % 2 == 1 for p in pairs])
        first = jnp.stack([slabs[0][slab_of(p[0])] for p in pairs])
        second = jnp.stack([slabs[0][slab_of(p[1])] for p in pairs])
        single = [slabs[0][slab_of(d)][None] for _, (d, *more) in PHI_ROWS if not more]
        sig = slabs[2]
        rhs = slabs[1][1:] if side == "lo" else slabs[1][:-1]
        return jnp.concatenate([jnp.where(colour1, first, second)] + single + [sig, rhs])

    g = lax.axis_index("grp")
    swap = [(0, 1), (1, 0)]
    if grps == 2:
        first = jnp.where(g == 0, cells_y - h, 0)
        pos = jnp.stack([lax.axis_index("box") * cells_x, g * cells_y, g, first]).astype(jnp.int32)
        hbm = pl.BlockSpec(memory_space=pltpu.MemorySpace.HBM)
        y_send = pl.pallas_call(
            y_send_kernel,
            out_shape=jax.ShapeDtypeStruct((len(Y_ROWS["lo"]), cells_x, cells_z), jnp.float32),
            in_specs=[pl.BlockSpec(memory_space=pltpu.MemorySpace.SMEM), hbm, hbm, hbm],
            out_specs=pl.BlockSpec(memory_space=pltpu.MemorySpace.VMEM),
            scratch_shapes=[
                pltpu.VMEM((h - 1, cells_x, cells_z), jnp.float32),
                pltpu.SemaphoreType.DMA((3 * h,)),
            ],
        )(pos, *arrays)
        y_lo = y_hi = lax.ppermute(y_send, "grp", swap)
    else:
        y_lo_send = y_piece("lo", slice(-h, None), lambda d: h - d)
        y_hi_send = y_piece("hi", slice(0, h), lambda d: d - 1)
        y_lo = lax.ppermute(y_lo_send, "grp", down_grp)
        y_hi = lax.ppermute(y_hi_send, "grp", up_grp)
    x_lo = lax.ppermute(jnp.stack([a[-h:] for a in arrays]), "box", down_box)
    x_hi = lax.ppermute(jnp.stack([a[:h] for a in arrays]), "box", up_box)
    if grps == 2:
        def diag(db):
            return [((b - db) * 2 + 1 - g_, b * 2 + g_)
                    for b in range(boxes) if 0 <= b - db < boxes for g_ in range(2)]

        cl = lax.ppermute(y_send[:, -h:], ("box", "grp"), diag(1))
        ch = lax.ppermute(y_send[:, :h], ("box", "grp"), diag(-1))
        return x_lo, x_hi, y_lo, y_hi, cl, cl, ch, ch
    corners = {}
    for name, part in (("lo", y_lo), ("hi", y_hi)):
        if name == "hi" and part is y_lo:
            corners["hi"] = corners["lo"]
            continue
        corners[name] = (
            lax.ppermute(part[:, -h:], "box", down_box),
            lax.ppermute(part[:, :h], "box", up_box),
        )
    (cl_lo, ch_lo), (cl_hi, ch_hi) = corners["lo"], corners["hi"]
    return x_lo, x_hi, y_lo, y_hi, cl_lo, cl_hi, ch_lo, ch_hi


def local(phi_start, right_side, sigma):
    cells_x, cells_y, cells_z = phi_start.shape
    boxes = lax.axis_size("box")
    grps = lax.axis_size("grp")
    nx = cells_x * boxes
    ny = cells_y * grps
    b = lax.axis_index("box")
    g = lax.axis_index("grp")
    pieces = exchange((phi_start, right_side, sigma))
    planes = cells_x + 2 * HALO
    rows = cells_y + 2 * ROW_PAD
    lanes = cells_z
    idx = jnp.stack([b * cells_x - HALO, g * cells_y - ROW_PAD, g * (cells_y // 2)]).astype(jnp.int32)
    pz = jnp.asarray(np.kron(np.eye(cells_z // 2), np.ones((2, 1))), jnp.float32)
    full = pl.BlockSpec(memory_space=pltpu.MemorySpace.VMEM)
    anywhere = pl.BlockSpec(memory_space=pltpu.MemorySpace.HBM)
    big = pltpu.VMEM((planes, rows, lanes), jnp.float32)
    phi_smooth, coarse, group_coarse = pl.pallas_call(
        functools.partial(smooth_kernel, nx, ny),
        out_shape=(
            jax.ShapeDtypeStruct((cells_x, cells_y, cells_z), jnp.float32),
            jax.ShapeDtypeStruct((cells_x // 2 * (cells_y // 2), cells_z // 2), jnp.float32),
            jax.ShapeDtypeStruct((cells_x // 2, ny // 2, cells_z // 2), jnp.float32),
        ),
        in_specs=[pl.BlockSpec(memory_space=pltpu.MemorySpace.SMEM), full]
        + [anywhere] * 11,
        out_specs=(full, full, full),
        scratch_shapes=[big] * 9
        + [
            pltpu.VMEM((rows, lanes), jnp.int32),
            pltpu.VMEM((lanes // 128, cells_y, 128), jnp.float32),
            pltpu.VMEM((cells_x // 2 * (cells_y // 2), lanes), jnp.float32),
            pltpu.SemaphoreType.DMA((3 * (3 + 4 * HALO) + 2 * (2 * HALO + HALO - 1),)),
        ],
        compiler_params=pltpu.CompilerParams(vmem_limit_bytes=60 * 1024 * 1024),
    )(idx, pz, phi_start, right_side, sigma, *pieces)
    coarse = coarse.reshape(cells_x // 2, cells_y // 2, cells_z // 2)
    if grps == 2:
        other = lax.ppermute(coarse, "grp", [(0, 1), (1, 0)])
        group_coarse = lax.dynamic_update_slice(
            group_coarse, other, (0, (1 - g) * (cells_y // 2), 0))
    else:
        group_coarse = lax.all_gather(coarse, "grp", axis=1, tiled=True)
    return phi_smooth, group_coarse


def solution(mesh):
    placed = (P("box", "grp", None), P("box", "grp", None), P("box", "grp", None))
    return jax.shard_map(
        local,
        mesh=mesh,
        in_specs=placed,
        out_specs=(P("box", "grp", None), P("box", None, None)),
        check_vma=False,
    )
```

```python
import functools

import jax
import jax.numpy as jnp
import numpy as np
from jax import lax
from jax.experimental import pallas as pl
from jax.experimental.pallas import tpu as pltpu
from jax.sharding import PartitionSpec as P

SWEEPS = 2
HALO = 2 * SWEEPS + 1
ROW_PAD = 8
PHI_ROWS = ((0, (1, 2)), (0, (3, 4)), (0, (5,)))
Y_ROWS = {
    "lo": PHI_ROWS + tuple((2, (d,)) for d in range(HALO, 0, -1))
    + tuple((1, (d,)) for d in range(HALO - 1, 0, -1)),
    "hi": PHI_ROWS + tuple((2, (d,)) for d in range(1, HALO + 1))
    + tuple((1, (d,)) for d in range(1, HALO)),
}


def harmonic(s, t):
    return 2.0 * s * t / (s + t)


def smooth_kernel(nx, ny, idx_ref, pz_ref, own_phi, own_rhs, own_sig,
                  x_lo, x_hi, y_lo, y_hi, cl_lo, cl_hi, ch_lo, ch_hi,
                  phi_out, coarse_out, group_out, ph, rs, sg, fx, fy, fz, fzl, dg, inv, par,
                  pair_buf, y_sums, sems, out_sems):
    planes, rows, lanes = ph.shape
    h = HALO
    cells_x = planes - 2 * h
    cells_y = rows - 2 * ROW_PAD
    gx0 = idx_ref[0]
    gy0 = idx_ref[1]
    mid = pl.ds(h, cells_x)
    lo_p = pl.ds(0, h)
    hi_p = pl.ds(h + cells_x, h)
    own_r = pl.ds(ROW_PAD, cells_y)
    copies = []
    for a, dst, own in ((2, sg, own_sig), (0, ph, own_phi), (1, rs, own_rhs)):
        pieces = [
            (own, dst.at[mid, own_r]),
            (x_lo.at[a], dst.at[lo_p, own_r]),
            (x_hi.at[a], dst.at[hi_p, own_r]),
        ]
        for side, y_part, below, above in (("lo", y_lo, cl_lo, ch_lo), ("hi", y_hi, cl_hi, ch_hi)):
            for k, (which, depths) in enumerate(Y_ROWS[side]):
                for d in depths if which == a else ():
                    row = ROW_PAD - d if side == "lo" else ROW_PAD + cells_y - 1 + d
                    pieces += [
                        (y_part.at[k], dst.at[mid, row]),
                        (below.at[k], dst.at[lo_p, row]),
                        (above.at[k], dst.at[hi_p, row]),
                    ]
        for src_ref, dst_ref in pieces:
            cp = pltpu.make_async_copy(src_ref, dst_ref, sems.at[len(copies)])
            cp.start()
            copies.append(cp)
        if a == 2:
            per_array = len(copies)
    for cp in copies[:per_array]:
        cp.wait()
    row = lax.broadcasted_iota(jnp.int32, (rows, lanes), 0)
    lane = lax.broadcasted_iota(jnp.int32, (rows, lanes), 1)
    gy = gy0 + row
    iny = (gy >= 0) & (gy < ny)
    par[...] = jnp.where(iny, (gy + lane) & 1, 2)

    def faces_x(i, carry):
        gx = gx0 + i
        ok = (gx >= 0) & (gx + 1 < nx)
        s0 = sg[i]
        s1 = sg[i + 1]
        gyv = gy0 + lax.broadcasted_iota(jnp.int32, (rows, lanes), 0)
        inside = (gyv >= 0) & (gyv < ny) & ok
        fx[i] = jnp.where(inside, harmonic(s0, s1), 0.0)
        return carry

    lax.fori_loop(0, planes - 1, faces_x, 0, unroll=2)

    def faces_yz(i, carry):
        gx = gx0 + i
        inx = (gx >= 0) & (gx < nx)
        r = lax.broadcasted_iota(jnp.int32, (rows, lanes), 0)
        k = lax.broadcasted_iota(jnp.int32, (rows, lanes), 1)
        gyv = gy0 + r
        inyv = (gyv >= 0) & (gyv < ny)
        s = sg[i]
        s_yu = pltpu.roll(s, rows - 1, 0)
        s_zu = pltpu.roll(s, lanes - 1, 1)
        wy = jnp.where(inx & (gyv >= 0) & (gyv + 1 < ny), harmonic(s, s_yu), 0.0)
        wz = jnp.where(inx & inyv & (k < lanes - 1), harmonic(s, s_zu), 0.0)
        wy_lo = pltpu.roll(wy, 1, 0)
        wz_lo = pltpu.roll(wz, 1, 1)
        fy[i] = wy
        fz[i] = wz
        fzl[i] = wz_lo
        wxl = jnp.where(gx == 0, s, fx[i - 1])
        wxu = jnp.where(gx == nx - 1, s, fx[i])
        wyl = jnp.where(gyv == 0, s, wy_lo)
        wyu = jnp.where(gyv == ny - 1, s, wy)
        wzl = jnp.where(k == 0, s, wz_lo)
        wzu = jnp.where(k == lanes - 1, s, wz)
        d = wxl + wxu + wyl + wyu + wzl + wzu
        dg[i] = d
        inv[i] = 1.0 / d
        sg[i] = wy_lo
        return carry

    lax.fori_loop(1, planes - 1, faces_yz, 0, unroll=2)
    for cp in copies[per_array:]:
        cp.wait()

    def coupled_sum(i, pc):
        wy = fy[i]
        wz = fz[i]
        terms = (
            (fx[i - 1], ph[i - 1]),
            (fx[i], ph[i + 1]),
            (sg[i], pltpu.roll(pc, 1, 0)),
            (wy, pltpu.roll(pc, rows - 1, 0)),
            (fzl[i], pltpu.roll(pc, 1, 1)),
            (wz, pltpu.roll(pc, lanes - 1, 1)),
        )
        return terms

    for turn in range(2 * SWEEPS):
        colour = turn % 2

        def relax(i, carry, colour=colour):
            gx = gx0 + i
            inx = (gx >= 0) & (gx < nx)
            target = jnp.where(inx, (gx + colour) & 1, 3)
            pc = ph[i]
            summed = rs[i]
            for w, nb in coupled_sum(i, pc):
                summed = summed + w * nb
            ph[i] = jnp.where(par[...] == target, summed * inv[i], pc)
            return carry

        lax.fori_loop(turn + 1, planes - 1 - turn, relax, 0, unroll=2)

    own_rows = rows - 2 * ROW_PAD
    half_rows = own_rows // 2

    def defect_plane(i):
        pc = ph[i]
        terms = coupled_sum(i, pc)
        coupled = terms[0][0] * terms[0][1]
        for w, nb in terms[1:]:
            coupled = coupled + w * nb
        d = rs[i] - (dg[i] * pc - coupled)
        return d[ROW_PAD:ROW_PAD + own_rows]

    def phi_copy(j):
        i = HALO + 2 * j
        return pltpu.make_async_copy(
            ph.at[pl.ds(i, 2), pl.ds(ROW_PAD, own_rows)], phi_out.at[pl.ds(i - HALO, 2)],
            out_sems.at[j])

    def restrict(j, carry):
        i = HALO + 2 * j
        phi_copy(j).start()
        pair = defect_plane(i) + defect_plane(i + 1)
        halves = []
        for q in range(lanes // 128):
            pair_buf[q] = pair[:, q * 128:(q + 1) * 128]
            even = pair_buf[q, pl.ds(0, half_rows, stride=2), :]
            odd = pair_buf[q, pl.ds(1, half_rows, stride=2), :]
            halves.append(even + odd)
        y_sums[pl.ds(pl.multiple_of(j * half_rows, half_rows), half_rows), :] = (
            jnp.concatenate(halves, axis=1))
        return carry

    lax.fori_loop(0, (planes - 2 * HALO) // 2, restrict, 0)
    coarse = 0.125 * jnp.dot(
        y_sums[...], pz_ref[...], precision=lax.Precision.HIGHEST,
        preferred_element_type=jnp.float32)
    coarse_out[...] = coarse
    for j in range(cells_x // 2):
        phi_copy(j).wait()
    first = idx_ref[2]
    for j in range(cells_x // 2):
        group_out[j, pl.ds(first, half_rows), :] = coarse[j * half_rows:(j + 1) * half_rows]


def y_send_kernel(pos_ref, phi, rhs, sig, out, stage, sems):
    planes, lanes = stage.shape[2], stage.shape[3]
    h = HALO
    top = pos_ref[2] == 0
    first = pos_ref[3]
    copies = []
    for a, src_ref in ((0, phi), (1, rhs), (2, sig)):
        for r in range(h):
            cp = pltpu.make_async_copy(src_ref.at[:, first + r], stage.at[a, r], sems.at[len(copies)])
            cp.start()
            copies.append(cp)
    for cp in copies:
        cp.wait()
    plane = lax.broadcasted_iota(jnp.int32, (planes, lanes), 0)
    z = lax.broadcasted_iota(jnp.int32, (planes, lanes), 1)
    parity = (pos_ref[0] + pos_ref[1] + first + plane + z) & 1
    for k, (lo_pair, hi_pair) in enumerate((((4, 3), (0, 1)), ((2, 1), (2, 3)))):
        a0 = jnp.where(top, stage[0, lo_pair[0]], stage[0, hi_pair[0]])
        a1 = jnp.where(top, stage[0, lo_pair[1]], stage[0, hi_pair[1]])
        offset = jnp.where(top, lo_pair[0], hi_pair[0])
        colour1 = ((parity + offset) & 1) == 1
        out[k] = jnp.where(colour1, a0, a1)
    out[2] = jnp.where(top, stage[0, 0], stage[0, h - 1])
    for r in range(h):
        out[3 + r] = stage[2, r]
    for r in range(h - 1):
        out[3 + h + r] = jnp.where(top, stage[1, r + 1], stage[1, r])


def exchange(arrays):
    boxes = lax.axis_size("box")
    grps = lax.axis_size("grp")
    h = HALO
    down_box = [(i, i + 1) for i in range(boxes - 1)]
    up_box = [(i + 1, i) for i in range(boxes - 1)]
    down_grp = [(i, i + 1) for i in range(grps - 1)]
    up_grp = [(i + 1, i) for i in range(grps - 1)]
    cells_x, cells_y, cells_z = arrays[0].shape
    gx = lax.axis_index("box") * cells_x + jnp.arange(cells_x, dtype=jnp.int32)[:, None]
    z = jnp.arange(cells_z, dtype=jnp.int32)[None, :]

    gy0 = lax.axis_index("grp") * cells_y

    def y_piece(side, block, slab_of):
        slabs = [jnp.swapaxes(a[:, block], 0, 1) for a in arrays]
        row_of = (lambda d: cells_y - d) if side == "lo" else (lambda d: d - 1)
        pairs = [depths for _, depths in PHI_ROWS if len(depths) == 2]
        colour1 = jnp.stack([(gx + gy0 + row_of(p[0]) + z) % 2 == 1 for p in pairs])
        first = jnp.stack([slabs[0][slab_of(p[0])] for p in pairs])
        second = jnp.stack([slabs[0][slab_of(p[1])] for p in pairs])
        single = [slabs[0][slab_of(d)][None] for _, (d, *more) in PHI_ROWS if not more]
        sig = slabs[2]
        rhs = slabs[1][1:] if side == "lo" else slabs[1][:-1]
        return jnp.concatenate([jnp.where(colour1, first, second)] + single + [sig, rhs])

    g = lax.axis_index("grp")
    swap = [(0, 1), (1, 0)]
    if grps == 2:
        first = jnp.where(g == 0, cells_y - h, 0)
        pos = jnp.stack([lax.axis_index("box") * cells_x, g * cells_y, g, first]).astype(jnp.int32)
        hbm = pl.BlockSpec(memory_space=pltpu.MemorySpace.HBM)
        y_send = pl.pallas_call(
            y_send_kernel,
            out_shape=jax.ShapeDtypeStruct((len(Y_ROWS["lo"]), cells_x, cells_z), jnp.float32),
            in_specs=[pl.BlockSpec(memory_space=pltpu.MemorySpace.SMEM), hbm, hbm, hbm],
            out_specs=pl.BlockSpec(memory_space=pltpu.MemorySpace.VMEM),
            scratch_shapes=[
                pltpu.VMEM((3, h, cells_x, cells_z), jnp.float32),
                pltpu.SemaphoreType.DMA((3 * h,)),
            ],
        )(pos, *arrays)
        y_lo = y_hi = lax.ppermute(y_send, "grp", swap)
    else:
        y_lo_send = y_piece("lo", slice(-h, None), lambda d: h - d)
        y_hi_send = y_piece("hi", slice(0, h), lambda d: d - 1)
        y_lo = lax.ppermute(y_lo_send, "grp", down_grp)
        y_hi = lax.ppermute(y_hi_send, "grp", up_grp)
    x_lo = lax.ppermute(jnp.stack([a[-h:] for a in arrays]), "box", down_box)
    x_hi = lax.ppermute(jnp.stack([a[:h] for a in arrays]), "box", up_box)
    if grps == 2:
        def diag(db):
            return [((b - db) * 2 + 1 - g_, b * 2 + g_)
                    for b in range(boxes) if 0 <= b - db < boxes for g_ in range(2)]

        cl = lax.ppermute(y_send[:, -h:], ("box", "grp"), diag(1))
        ch = lax.ppermute(y_send[:, :h], ("box", "grp"), diag(-1))
        return x_lo, x_hi, y_lo, y_hi, cl, cl, ch, ch
    corners = {}
    for name, part in (("lo", y_lo), ("hi", y_hi)):
        if name == "hi" and part is y_lo:
            corners["hi"] = corners["lo"]
            continue
        corners[name] = (
            lax.ppermute(part[:, -h:], "box", down_box),
            lax.ppermute(part[:, :h], "box", up_box),
        )
    (cl_lo, ch_lo), (cl_hi, ch_hi) = corners["lo"], corners["hi"]
    return x_lo, x_hi, y_lo, y_hi, cl_lo, cl_hi, ch_lo, ch_hi


def local(phi_start, right_side, sigma):
    cells_x, cells_y, cells_z = phi_start.shape
    boxes = lax.axis_size("box")
    grps = lax.axis_size("grp")
    nx = cells_x * boxes
    ny = cells_y * grps
    b = lax.axis_index("box")
    g = lax.axis_index("grp")
    pieces = exchange((phi_start, right_side, sigma))
    planes = cells_x + 2 * HALO
    rows = cells_y + 2 * ROW_PAD
    lanes = cells_z
    idx = jnp.stack([b * cells_x - HALO, g * cells_y - ROW_PAD, g * (cells_y // 2)]).astype(jnp.int32)
    pz = jnp.asarray(np.kron(np.eye(cells_z // 2), np.ones((2, 1))), jnp.float32)
    full = pl.BlockSpec(memory_space=pltpu.MemorySpace.VMEM)
    anywhere = pl.BlockSpec(memory_space=pltpu.MemorySpace.HBM)
    big = pltpu.VMEM((planes, rows, lanes), jnp.float32)
    phi_smooth, coarse, group_coarse = pl.pallas_call(
        functools.partial(smooth_kernel, nx, ny),
        out_shape=(
            jax.ShapeDtypeStruct((cells_x, cells_y, cells_z), jnp.float32),
            jax.ShapeDtypeStruct((cells_x // 2 * (cells_y // 2), cells_z // 2), jnp.float32),
            jax.ShapeDtypeStruct((cells_x // 2, ny // 2, cells_z // 2), jnp.float32),
        ),
        in_specs=[pl.BlockSpec(memory_space=pltpu.MemorySpace.SMEM), full]
        + [anywhere] * 11,
        out_specs=(anywhere, full, full),
        scratch_shapes=[big] * 9
        + [
            pltpu.VMEM((rows, lanes), jnp.int32),
            pltpu.VMEM((lanes // 128, cells_y, 128), jnp.float32),
            pltpu.VMEM((cells_x // 2 * (cells_y // 2), lanes), jnp.float32),
            pltpu.SemaphoreType.DMA((3 * (3 + 4 * HALO) + 2 * (2 * HALO + HALO - 1),)),
            pltpu.SemaphoreType.DMA((cells_x // 2,)),
        ],
        compiler_params=pltpu.CompilerParams(vmem_limit_bytes=60 * 1024 * 1024),
    )(idx, pz, phi_start, right_side, sigma, *pieces)
    coarse = coarse.reshape(cells_x // 2, cells_y // 2, cells_z // 2)
    if grps == 2:
        other = lax.ppermute(coarse, "grp", [(0, 1), (1, 0)])
        group_coarse = lax.dynamic_update_slice(
            group_coarse, other, (0, (1 - g) * (cells_y // 2), 0))
    else:
        group_coarse = lax.all_gather(coarse, "grp", axis=1, tiled=True)
    return phi_smooth, group_coarse


def solution(mesh):
    placed = (P("box", "grp", None), P("box", "grp", None), P("box", "grp", None))
    return jax.shard_map(
        local,
        mesh=mesh,
        in_specs=placed,
        out_specs=(P("box", "grp", None), P("box", None, None)),
        check_vma=False,
    )
```

```python
import functools

import jax
import jax.numpy as jnp
import numpy as np
from jax import lax
from jax.experimental import pallas as pl
from jax.experimental.pallas import tpu as pltpu
from jax.sharding import PartitionSpec as P

SWEEPS = 2
HALO = 2 * SWEEPS + 1
ROW_PAD = 8
PHI_ROWS = ((0, (1, 2)), (0, (3, 4)), (0, (5,)))
Y_ROWS = {
    "lo": PHI_ROWS + tuple((2, (d,)) for d in range(HALO, 0, -1))
    + tuple((1, (d,)) for d in range(HALO - 1, 0, -1)),
    "hi": PHI_ROWS + tuple((2, (d,)) for d in range(1, HALO + 1))
    + tuple((1, (d,)) for d in range(1, HALO)),
}


def harmonic(s, t):
    return 2.0 * s * t / (s + t)


def smooth_kernel(nx, ny, idx_ref, pz_ref, own_phi, own_rhs, own_sig,
                  x_lo, x_hi, y_lo, y_hi, cl_lo, cl_hi, ch_lo, ch_hi,
                  phi_out, coarse_out, group_out, ph, rs, sg, fx, fy, fz, fzl, dg, inv, par,
                  pair_buf, y_sums, sems):
    planes, rows, lanes = ph.shape
    h = HALO
    cells_x = planes - 2 * h
    cells_y = rows - 2 * ROW_PAD
    gx0 = idx_ref[0]
    gy0 = idx_ref[1]
    mid = pl.ds(h, cells_x)
    lo_p = pl.ds(0, h)
    hi_p = pl.ds(h + cells_x, h)
    own_r = pl.ds(ROW_PAD, cells_y)
    copies = []
    for a, dst, own in ((2, sg, own_sig), (0, ph, own_phi), (1, rs, own_rhs)):
        pieces = [
            (own, dst.at[mid, own_r]),
            (x_lo.at[a], dst.at[lo_p, own_r]),
            (x_hi.at[a], dst.at[hi_p, own_r]),
        ]
        for side, y_part, below, above in (("lo", y_lo, cl_lo, ch_lo), ("hi", y_hi, cl_hi, ch_hi)):
            for k, (which, depths) in enumerate(Y_ROWS[side]):
                for d in depths if which == a else ():
                    row = ROW_PAD - d if side == "lo" else ROW_PAD + cells_y - 1 + d
                    pieces += [
                        (y_part.at[k], dst.at[mid, row]),
                        (below.at[k], dst.at[lo_p, row]),
                        (above.at[k], dst.at[hi_p, row]),
                    ]
        for src_ref, dst_ref in pieces:
            cp = pltpu.make_async_copy(src_ref, dst_ref, sems.at[len(copies)])
            cp.start()
            copies.append(cp)
        if a == 2:
            per_array = len(copies)
    for cp in copies[:per_array]:
        cp.wait()
    row = lax.broadcasted_iota(jnp.int32, (rows, lanes), 0)
    lane = lax.broadcasted_iota(jnp.int32, (rows, lanes), 1)
    gy = gy0 + row
    iny = (gy >= 0) & (gy < ny)
    par[...] = jnp.where(iny, (gy + lane) & 1, 2)

    def faces_x(i, carry):
        gx = gx0 + i
        ok = (gx >= 0) & (gx + 1 < nx)
        s0 = sg[i]
        s1 = sg[i + 1]
        gyv = gy0 + lax.broadcasted_iota(jnp.int32, (rows, lanes), 0)
        inside = (gyv >= 0) & (gyv < ny) & ok
        fx[i] = jnp.where(inside, harmonic(s0, s1), 0.0)
        return carry

    lax.fori_loop(0, planes - 1, faces_x, 0, unroll=2)

    def faces_yz(i, carry):
        gx = gx0 + i
        inx = (gx >= 0) & (gx < nx)
        r = lax.broadcasted_iota(jnp.int32, (rows, lanes), 0)
        k = lax.broadcasted_iota(jnp.int32, (rows, lanes), 1)
        gyv = gy0 + r
        inyv = (gyv >= 0) & (gyv < ny)
        s = sg[i]
        s_yu = pltpu.roll(s, rows - 1, 0)
        s_zu = pltpu.roll(s, lanes - 1, 1)
        wy = jnp.where(inx & (gyv >= 0) & (gyv + 1 < ny), harmonic(s, s_yu), 0.0)
        wz = jnp.where(inx & inyv & (k < lanes - 1), harmonic(s, s_zu), 0.0)
        wy_lo = pltpu.roll(wy, 1, 0)
        wz_lo = pltpu.roll(wz, 1, 1)
        fy[i] = wy
        fz[i] = wz
        fzl[i] = wz_lo
        wxl = jnp.where(gx == 0, s, fx[i - 1])
        wxu = jnp.where(gx == nx - 1, s, fx[i])
        wyl = jnp.where(gyv == 0, s, wy_lo)
        wyu = jnp.where(gyv == ny - 1, s, wy)
        wzl = jnp.where(k == 0, s, wz_lo)
        wzu = jnp.where(k == lanes - 1, s, wz)
        d = wxl + wxu + wyl + wyu + wzl + wzu
        dg[i] = d
        inv[i] = 1.0 / d
        sg[i] = wy_lo
        return carry

    lax.fori_loop(1, planes - 1, faces_yz, 0, unroll=2)
    for cp in copies[per_array:]:
        cp.wait()

    def coupled_sum(i, pc):
        wy = fy[i]
        wz = fz[i]
        terms = (
            (fx[i - 1], ph[i - 1]),
            (fx[i], ph[i + 1]),
            (sg[i], pltpu.roll(pc, 1, 0)),
            (wy, pltpu.roll(pc, rows - 1, 0)),
            (fzl[i], pltpu.roll(pc, 1, 1)),
            (wz, pltpu.roll(pc, lanes - 1, 1)),
        )
        return terms

    for turn in range(2 * SWEEPS):
        colour = turn % 2

        def relax(i, carry, colour=colour):
            gx = gx0 + i
            inx = (gx >= 0) & (gx < nx)
            target = jnp.where(inx, (gx + colour) & 1, 3)
            pc = ph[i]
            summed = rs[i]
            for w, nb in coupled_sum(i, pc):
                summed = summed + w * nb
            ph[i] = jnp.where(par[...] == target, summed * inv[i], pc)
            return carry

        lax.fori_loop(turn + 1, planes - 1 - turn, relax, 0, unroll=2)

    own_rows = rows - 2 * ROW_PAD
    half_rows = own_rows // 2

    def defect_plane(i):
        pc = ph[i]
        terms = coupled_sum(i, pc)
        coupled = terms[0][0] * terms[0][1]
        for w, nb in terms[1:]:
            coupled = coupled + w * nb
        d = rs[i] - (dg[i] * pc - coupled)
        phi_out[i - HALO] = pc[ROW_PAD:ROW_PAD + own_rows]
        return d[ROW_PAD:ROW_PAD + own_rows]

    def restrict(j, carry):
        i = HALO + 2 * j
        pair = defect_plane(i) + defect_plane(i + 1)
        halves = []
        for q in range(lanes // 128):
            pair_buf[q] = pair[:, q * 128:(q + 1) * 128]
            even = pair_buf[q, pl.ds(0, half_rows, stride=2), :]
            odd = pair_buf[q, pl.ds(1, half_rows, stride=2), :]
            halves.append(even + odd)
        y_sums[pl.ds(pl.multiple_of(j * half_rows, half_rows), half_rows), :] = (
            jnp.concatenate(halves, axis=1))
        return carry

    lax.fori_loop(0, (planes - 2 * HALO) // 2, restrict, 0)
    coarse = 0.125 * jnp.dot(
        y_sums[...], pz_ref[...], precision=lax.Precision.HIGHEST,
        preferred_element_type=jnp.float32)
    coarse_out[...] = coarse
    first = idx_ref[2]
    for j in range(cells_x // 2):
        group_out[j, pl.ds(first, half_rows), :] = coarse[j * half_rows:(j + 1) * half_rows]


def y_send_kernel(pos_ref, phi, rhs, sig, out, c_lo, c_hi, x_lo, x_hi, stage, sems):
    planes, lanes = stage.shape[2], stage.shape[3]
    h = HALO
    top = pos_ref[2] == 0
    first = pos_ref[3]
    copies = []
    for a, src_ref in ((0, phi), (1, rhs), (2, sig)):
        for r in range(h):
            cp = pltpu.make_async_copy(src_ref.at[:, first + r], stage.at[a, r], sems.at[len(copies)])
            cp.start()
            copies.append(cp)
    cells = phi.shape[0]
    for a, src_ref in ((0, phi), (1, rhs), (2, sig)):
        for src_part, dst in ((src_ref.at[pl.ds(cells - h, h)], x_lo.at[a]),
                              (src_ref.at[pl.ds(0, h)], x_hi.at[a])):
            cp = pltpu.make_async_copy(src_part, dst, sems.at[len(copies)])
            cp.start()
            copies.append(cp)
    for cp in copies:
        cp.wait()
    plane = lax.broadcasted_iota(jnp.int32, (planes, lanes), 0)
    z = lax.broadcasted_iota(jnp.int32, (planes, lanes), 1)
    parity = (pos_ref[0] + pos_ref[1] + first + plane + z) & 1
    for k, (lo_pair, hi_pair) in enumerate((((4, 3), (0, 1)), ((2, 1), (2, 3)))):
        a0 = jnp.where(top, stage[0, lo_pair[0]], stage[0, hi_pair[0]])
        a1 = jnp.where(top, stage[0, lo_pair[1]], stage[0, hi_pair[1]])
        offset = jnp.where(top, lo_pair[0], hi_pair[0])
        colour1 = ((parity + offset) & 1) == 1
        out[k] = jnp.where(colour1, a0, a1)
    out[2] = jnp.where(top, stage[0, 0], stage[0, h - 1])
    for r in range(h):
        out[3 + r] = stage[2, r]
    for r in range(h - 1):
        out[3 + h + r] = jnp.where(top, stage[1, r + 1], stage[1, r])
    for k in range(out.shape[0]):
        c_lo[k] = out[k, pl.ds(planes - h, h), :]
        c_hi[k] = out[k, pl.ds(0, h), :]


def exchange(arrays):
    boxes = lax.axis_size("box")
    grps = lax.axis_size("grp")
    h = HALO
    down_box = [(i, i + 1) for i in range(boxes - 1)]
    up_box = [(i + 1, i) for i in range(boxes - 1)]
    down_grp = [(i, i + 1) for i in range(grps - 1)]
    up_grp = [(i + 1, i) for i in range(grps - 1)]
    cells_x, cells_y, cells_z = arrays[0].shape
    gx = lax.axis_index("box") * cells_x + jnp.arange(cells_x, dtype=jnp.int32)[:, None]
    z = jnp.arange(cells_z, dtype=jnp.int32)[None, :]

    gy0 = lax.axis_index("grp") * cells_y

    def y_piece(side, block, slab_of):
        slabs = [jnp.swapaxes(a[:, block], 0, 1) for a in arrays]
        row_of = (lambda d: cells_y - d) if side == "lo" else (lambda d: d - 1)
        pairs = [depths for _, depths in PHI_ROWS if len(depths) == 2]
        colour1 = jnp.stack([(gx + gy0 + row_of(p[0]) + z) % 2 == 1 for p in pairs])
        first = jnp.stack([slabs[0][slab_of(p[0])] for p in pairs])
        second = jnp.stack([slabs[0][slab_of(p[1])] for p in pairs])
        single = [slabs[0][slab_of(d)][None] for _, (d, *more) in PHI_ROWS if not more]
        sig = slabs[2]
        rhs = slabs[1][1:] if side == "lo" else slabs[1][:-1]
        return jnp.concatenate([jnp.where(colour1, first, second)] + single + [sig, rhs])

    g = lax.axis_index("grp")
    swap = [(0, 1), (1, 0)]
    if grps == 2:
        first = jnp.where(g == 0, cells_y - h, 0)
        pos = jnp.stack([lax.axis_index("box") * cells_x, g * cells_y, g, first]).astype(jnp.int32)
        hbm = pl.BlockSpec(memory_space=pltpu.MemorySpace.HBM)
        n_rows = len(Y_ROWS["lo"])
        vmem = pl.BlockSpec(memory_space=pltpu.MemorySpace.VMEM)
        y_send, c_lo_send, c_hi_send, x_lo_send, x_hi_send = pl.pallas_call(
            y_send_kernel,
            out_shape=(
                jax.ShapeDtypeStruct((n_rows, cells_x, cells_z), jnp.float32),
                jax.ShapeDtypeStruct((n_rows, h, cells_z), jnp.float32),
                jax.ShapeDtypeStruct((n_rows, h, cells_z), jnp.float32),
                jax.ShapeDtypeStruct((3, h, cells_y, cells_z), jnp.float32),
                jax.ShapeDtypeStruct((3, h, cells_y, cells_z), jnp.float32),
            ),
            in_specs=[pl.BlockSpec(memory_space=pltpu.MemorySpace.SMEM), hbm, hbm, hbm],
            out_specs=(vmem,) * 5,
            scratch_shapes=[
                pltpu.VMEM((3, h, cells_x, cells_z), jnp.float32),
                pltpu.SemaphoreType.DMA((5 * h,)),
            ],
        )(pos, *arrays)
        y_lo = y_hi = lax.ppermute(y_send, "grp", swap)
    else:
        y_lo_send = y_piece("lo", slice(-h, None), lambda d: h - d)
        y_hi_send = y_piece("hi", slice(0, h), lambda d: d - 1)
        y_lo = lax.ppermute(y_lo_send, "grp", down_grp)
        y_hi = lax.ppermute(y_hi_send, "grp", up_grp)
    if grps != 2:
        x_lo_send = jnp.stack([a[-h:] for a in arrays])
        x_hi_send = jnp.stack([a[:h] for a in arrays])
    x_lo = lax.ppermute(x_lo_send, "box", down_box)
    x_hi = lax.ppermute(x_hi_send, "box", up_box)
    if grps == 2:
        def diag(db):
            return [((b - db) * 2 + 1 - g_, b * 2 + g_)
                    for b in range(boxes) if 0 <= b - db < boxes for g_ in range(2)]

        cl = lax.ppermute(c_lo_send, ("box", "grp"), diag(1))
        ch = lax.ppermute(c_hi_send, ("box", "grp"), diag(-1))
        return x_lo, x_hi, y_lo, y_hi, cl, cl, ch, ch
    corners = {}
    for name, part in (("lo", y_lo), ("hi", y_hi)):
        if name == "hi" and part is y_lo:
            corners["hi"] = corners["lo"]
            continue
        corners[name] = (
            lax.ppermute(part[:, -h:], "box", down_box),
            lax.ppermute(part[:, :h], "box", up_box),
        )
    (cl_lo, ch_lo), (cl_hi, ch_hi) = corners["lo"], corners["hi"]
    return x_lo, x_hi, y_lo, y_hi, cl_lo, cl_hi, ch_lo, ch_hi


def local(phi_start, right_side, sigma):
    cells_x, cells_y, cells_z = phi_start.shape
    boxes = lax.axis_size("box")
    grps = lax.axis_size("grp")
    nx = cells_x * boxes
    ny = cells_y * grps
    b = lax.axis_index("box")
    g = lax.axis_index("grp")
    pieces = exchange((phi_start, right_side, sigma))
    planes = cells_x + 2 * HALO
    rows = cells_y + 2 * ROW_PAD
    lanes = cells_z
    idx = jnp.stack([b * cells_x - HALO, g * cells_y - ROW_PAD, g * (cells_y // 2)]).astype(jnp.int32)
    pz = jnp.asarray(np.kron(np.eye(cells_z // 2), np.ones((2, 1))), jnp.float32)
    full = pl.BlockSpec(memory_space=pltpu.MemorySpace.VMEM)
    anywhere = pl.BlockSpec(memory_space=pltpu.MemorySpace.HBM)
    big = pltpu.VMEM((planes, rows, lanes), jnp.float32)
    phi_smooth, coarse, group_coarse = pl.pallas_call(
        functools.partial(smooth_kernel, nx, ny),
        out_shape=(
            jax.ShapeDtypeStruct((cells_x, cells_y, cells_z), jnp.float32),
            jax.ShapeDtypeStruct((cells_x // 2 * (cells_y // 2), cells_z // 2), jnp.float32),
            jax.ShapeDtypeStruct((cells_x // 2, ny // 2, cells_z // 2), jnp.float32),
        ),
        in_specs=[pl.BlockSpec(memory_space=pltpu.MemorySpace.SMEM), full]
        + [anywhere] * 11,
        out_specs=(full, full, full),
        scratch_shapes=[big] * 9
        + [
            pltpu.VMEM((rows, lanes), jnp.int32),
            pltpu.VMEM((lanes // 128, cells_y, 128), jnp.float32),
            pltpu.VMEM((cells_x // 2 * (cells_y // 2), lanes), jnp.float32),
            pltpu.SemaphoreType.DMA((3 * (3 + 4 * HALO) + 2 * (2 * HALO + HALO - 1),)),
        ],
        compiler_params=pltpu.CompilerParams(vmem_limit_bytes=60 * 1024 * 1024),
    )(idx, pz, phi_start, right_side, sigma, *pieces)
    coarse = coarse.reshape(cells_x // 2, cells_y // 2, cells_z // 2)
    if grps == 2:
        other = lax.ppermute(coarse, "grp", [(0, 1), (1, 0)])
        group_coarse = lax.dynamic_update_slice(
            group_coarse, other, (0, (1 - g) * (cells_y // 2), 0))
    else:
        group_coarse = lax.all_gather(coarse, "grp", axis=1, tiled=True)
    return phi_smooth, group_coarse


def solution(mesh):
    placed = (P("box", "grp", None), P("box", "grp", None), P("box", "grp", None))
    return jax.shard_map(
        local,
        mesh=mesh,
        in_specs=placed,
        out_specs=(P("box", "grp", None), P("box", None, None)),
        check_vma=False,
    )
```

```python
import functools

import jax
import jax.numpy as jnp
import numpy as np
from jax import lax
from jax.experimental import pallas as pl
from jax.experimental.pallas import tpu as pltpu
from jax.sharding import PartitionSpec as P

SWEEPS = 2
HALO = 2 * SWEEPS + 1
ROW_PAD = 8
PHI_ROWS = ((0, (1, 2)), (0, (3, 4)), (0, (5,)))
Y_ROWS = {
    "lo": PHI_ROWS + tuple((2, (d,)) for d in range(HALO, 0, -1))
    + tuple((1, (d,)) for d in range(HALO - 1, 0, -1)),
    "hi": PHI_ROWS + tuple((2, (d,)) for d in range(1, HALO + 1))
    + tuple((1, (d,)) for d in range(1, HALO)),
}


def harmonic(s, t):
    return 2.0 * s * t / (s + t)


def smooth_kernel(nx, ny, idx_ref, pz_ref, own_phi, own_rhs, own_sig,
                  x_lo, x_hi, y_lo, y_hi, cl_lo, cl_hi, ch_lo, ch_hi,
                  phi_out, coarse_out, group_out, ph, rs, sg, fx, fy, fz, fzl, dg, inv, par,
                  pair_buf, y_sums, sems):
    planes, rows, lanes = ph.shape
    h = HALO
    cells_x = planes - 2 * h
    cells_y = rows - 2 * ROW_PAD
    gx0 = idx_ref[0]
    gy0 = idx_ref[1]
    mid = pl.ds(h, cells_x)
    lo_p = pl.ds(0, h)
    hi_p = pl.ds(h + cells_x, h)
    own_r = pl.ds(ROW_PAD, cells_y)
    copies = []
    for a, dst, own in ((2, sg, own_sig), (0, ph, own_phi), (1, rs, own_rhs)):
        pieces = [
            (own, dst.at[mid, own_r]),
            (x_lo.at[a], dst.at[lo_p, own_r]),
            (x_hi.at[a], dst.at[hi_p, own_r]),
        ]
        for side, y_part, below, above in (("lo", y_lo, cl_lo, ch_lo), ("hi", y_hi, cl_hi, ch_hi)):
            for k, (which, depths) in enumerate(Y_ROWS[side]):
                for d in depths if which == a else ():
                    row = ROW_PAD - d if side == "lo" else ROW_PAD + cells_y - 1 + d
                    pieces += [
                        (y_part.at[k], dst.at[mid, row]),
                        (below.at[k], dst.at[lo_p, row]),
                        (above.at[k], dst.at[hi_p, row]),
                    ]
        for src_ref, dst_ref in pieces:
            cp = pltpu.make_async_copy(src_ref, dst_ref, sems.at[len(copies)])
            cp.start()
            copies.append(cp)
        if a == 2:
            per_array = len(copies)
    for cp in copies[:per_array]:
        cp.wait()
    row = lax.broadcasted_iota(jnp.int32, (rows, lanes), 0)
    lane = lax.broadcasted_iota(jnp.int32, (rows, lanes), 1)
    gy = gy0 + row
    iny = (gy >= 0) & (gy < ny)
    par[...] = jnp.where(iny, (gy + lane) & 1, 2)

    def face_x(i):
        gx = gx0 + i
        ok = (gx >= 0) & (gx + 1 < nx)
        s0 = sg[i]
        s1 = sg[i + 1]
        gyv = gy0 + lax.broadcasted_iota(jnp.int32, (rows, lanes), 0)
        inside = (gyv >= 0) & (gyv < ny) & ok
        fx[i] = jnp.where(inside, harmonic(s0, s1), 0.0)

    face_x(0)

    def faces_yz(i, carry):
        face_x(i)
        gx = gx0 + i
        inx = (gx >= 0) & (gx < nx)
        r = lax.broadcasted_iota(jnp.int32, (rows, lanes), 0)
        k = lax.broadcasted_iota(jnp.int32, (rows, lanes), 1)
        gyv = gy0 + r
        inyv = (gyv >= 0) & (gyv < ny)
        s = sg[i]
        s_yu = pltpu.roll(s, rows - 1, 0)
        s_zu = pltpu.roll(s, lanes - 1, 1)
        wy = jnp.where(inx & (gyv >= 0) & (gyv + 1 < ny), harmonic(s, s_yu), 0.0)
        wz = jnp.where(inx & inyv & (k < lanes - 1), harmonic(s, s_zu), 0.0)
        wy_lo = pltpu.roll(wy, 1, 0)
        wz_lo = pltpu.roll(wz, 1, 1)
        fy[i] = wy
        fz[i] = wz
        fzl[i] = wz_lo
        wxl = jnp.where(gx == 0, s, fx[i - 1])
        wxu = jnp.where(gx == nx - 1, s, fx[i])
        wyl = jnp.where(gyv == 0, s, wy_lo)
        wyu = jnp.where(gyv == ny - 1, s, wy)
        wzl = jnp.where(k == 0, s, wz_lo)
        wzu = jnp.where(k == lanes - 1, s, wz)
        d = wxl + wxu + wyl + wyu + wzl + wzu
        dg[i] = d
        inv[i] = 1.0 / d
        sg[i] = wy_lo
        return carry

    lax.fori_loop(1, planes - 1, faces_yz, 0, unroll=2)
    for cp in copies[per_array:]:
        cp.wait()

    def coupled_sum(i, pc):
        wy = fy[i]
        wz = fz[i]
        terms = (
            (fx[i - 1], ph[i - 1]),
            (fx[i], ph[i + 1]),
            (sg[i], pltpu.roll(pc, 1, 0)),
            (wy, pltpu.roll(pc, rows - 1, 0)),
            (fzl[i], pltpu.roll(pc, 1, 1)),
            (wz, pltpu.roll(pc, lanes - 1, 1)),
        )
        return terms

    for turn in range(2 * SWEEPS):
        colour = turn % 2

        def relax(i, carry, colour=colour):
            gx = gx0 + i
            inx = (gx >= 0) & (gx < nx)
            target = jnp.where(inx, (gx + colour) & 1, 3)
            pc = ph[i]
            summed = rs[i]
            for w, nb in coupled_sum(i, pc):
                summed = summed + w * nb
            ph[i] = jnp.where(par[...] == target, summed * inv[i], pc)
            return carry

        lax.fori_loop(turn + 1, planes - 1 - turn, relax, 0, unroll=2)

    own_rows = rows - 2 * ROW_PAD
    half_rows = own_rows // 2

    def defect_plane(i):
        pc = ph[i]
        terms = coupled_sum(i, pc)
        coupled = terms[0][0] * terms[0][1]
        for w, nb in terms[1:]:
            coupled = coupled + w * nb
        d = rs[i] - (dg[i] * pc - coupled)
        phi_out[i - HALO] = pc[ROW_PAD:ROW_PAD + own_rows]
        return d[ROW_PAD:ROW_PAD + own_rows]

    def restrict(j, carry):
        i = HALO + 2 * j
        pair = defect_plane(i) + defect_plane(i + 1)
        halves = []
        for q in range(lanes // 128):
            pair_buf[q] = pair[:, q * 128:(q + 1) * 128]
            even = pair_buf[q, pl.ds(0, half_rows, stride=2), :]
            odd = pair_buf[q, pl.ds(1, half_rows, stride=2), :]
            halves.append(even + odd)
        y_sums[pl.ds(pl.multiple_of(j * half_rows, half_rows), half_rows), :] = (
            jnp.concatenate(halves, axis=1))
        return carry

    lax.fori_loop(0, (planes - 2 * HALO) // 2, restrict, 0)
    coarse = 0.125 * jnp.dot(
        y_sums[...], pz_ref[...], precision=lax.Precision.HIGHEST,
        preferred_element_type=jnp.float32)
    coarse_out[...] = coarse
    first = idx_ref[2]
    for j in range(cells_x // 2):
        group_out[j, pl.ds(first, half_rows), :] = coarse[j * half_rows:(j + 1) * half_rows]


def y_send_kernel(pos_ref, phi, rhs, sig, out, stage, sems):
    planes, lanes = stage.shape[2], stage.shape[3]
    h = HALO
    top = pos_ref[2] == 0
    first = pos_ref[3]
    copies = []
    for a, src_ref in ((0, phi), (1, rhs), (2, sig)):
        for r in range(h):
            cp = pltpu.make_async_copy(src_ref.at[:, first + r], stage.at[a, r], sems.at[len(copies)])
            cp.start()
            copies.append(cp)
    for cp in copies:
        cp.wait()
    plane = lax.broadcasted_iota(jnp.int32, (planes, lanes), 0)
    z = lax.broadcasted_iota(jnp.int32, (planes, lanes), 1)
    parity = (pos_ref[0] + pos_ref[1] + first + plane + z) & 1
    for k, (lo_pair, hi_pair) in enumerate((((4, 3), (0, 1)), ((2, 1), (2, 3)))):
        a0 = jnp.where(top, stage[0, lo_pair[0]], stage[0, hi_pair[0]])
        a1 = jnp.where(top, stage[0, lo_pair[1]], stage[0, hi_pair[1]])
        offset = jnp.where(top, lo_pair[0], hi_pair[0])
        colour1 = ((parity + offset) & 1) == 1
        out[k] = jnp.where(colour1, a0, a1)
    out[2] = jnp.where(top, stage[0, 0], stage[0, h - 1])
    for r in range(h):
        out[3 + r] = stage[2, r]
    for r in range(h - 1):
        out[3 + h + r] = jnp.where(top, stage[1, r + 1], stage[1, r])


def exchange(arrays):
    boxes = lax.axis_size("box")
    grps = lax.axis_size("grp")
    h = HALO
    down_box = [(i, i + 1) for i in range(boxes - 1)]
    up_box = [(i + 1, i) for i in range(boxes - 1)]
    down_grp = [(i, i + 1) for i in range(grps - 1)]
    up_grp = [(i + 1, i) for i in range(grps - 1)]
    cells_x, cells_y, cells_z = arrays[0].shape
    gx = lax.axis_index("box") * cells_x + jnp.arange(cells_x, dtype=jnp.int32)[:, None]
    z = jnp.arange(cells_z, dtype=jnp.int32)[None, :]

    gy0 = lax.axis_index("grp") * cells_y

    def y_piece(side, block, slab_of):
        slabs = [jnp.swapaxes(a[:, block], 0, 1) for a in arrays]
        row_of = (lambda d: cells_y - d) if side == "lo" else (lambda d: d - 1)
        pairs = [depths for _, depths in PHI_ROWS if len(depths) == 2]
        colour1 = jnp.stack([(gx + gy0 + row_of(p[0]) + z) % 2 == 1 for p in pairs])
        first = jnp.stack([slabs[0][slab_of(p[0])] for p in pairs])
        second = jnp.stack([slabs[0][slab_of(p[1])] for p in pairs])
        single = [slabs[0][slab_of(d)][None] for _, (d, *more) in PHI_ROWS if not more]
        sig = slabs[2]
        rhs = slabs[1][1:] if side == "lo" else slabs[1][:-1]
        return jnp.concatenate([jnp.where(colour1, first, second)] + single + [sig, rhs])

    g = lax.axis_index("grp")
    swap = [(0, 1), (1, 0)]
    if grps == 2:
        first = jnp.where(g == 0, cells_y - h, 0)
        pos = jnp.stack([lax.axis_index("box") * cells_x, g * cells_y, g, first]).astype(jnp.int32)
        hbm = pl.BlockSpec(memory_space=pltpu.MemorySpace.HBM)
        y_send = pl.pallas_call(
            y_send_kernel,
            out_shape=jax.ShapeDtypeStruct((len(Y_ROWS["lo"]), cells_x, cells_z), jnp.float32),
            in_specs=[pl.BlockSpec(memory_space=pltpu.MemorySpace.SMEM), hbm, hbm, hbm],
            out_specs=pl.BlockSpec(memory_space=pltpu.MemorySpace.VMEM),
            scratch_shapes=[
                pltpu.VMEM((3, h, cells_x, cells_z), jnp.float32),
                pltpu.SemaphoreType.DMA((3 * h,)),
            ],
        )(pos, *arrays)
        y_lo = y_hi = lax.ppermute(y_send, "grp", swap)
    else:
        y_lo_send = y_piece("lo", slice(-h, None), lambda d: h - d)
        y_hi_send = y_piece("hi", slice(0, h), lambda d: d - 1)
        y_lo = lax.ppermute(y_lo_send, "grp", down_grp)
        y_hi = lax.ppermute(y_hi_send, "grp", up_grp)
    x_lo = lax.ppermute(jnp.stack([a[-h:] for a in arrays]), "box", down_box)
    x_hi = lax.ppermute(jnp.stack([a[:h] for a in arrays]), "box", up_box)
    if grps == 2:
        def diag(db):
            return [((b - db) * 2 + 1 - g_, b * 2 + g_)
                    for b in range(boxes) if 0 <= b - db < boxes for g_ in range(2)]

        cl = lax.ppermute(y_send[:, -h:], ("box", "grp"), diag(1))
        ch = lax.ppermute(y_send[:, :h], ("box", "grp"), diag(-1))
        return x_lo, x_hi, y_lo, y_hi, cl, cl, ch, ch
    corners = {}
    for name, part in (("lo", y_lo), ("hi", y_hi)):
        if name == "hi" and part is y_lo:
            corners["hi"] = corners["lo"]
            continue
        corners[name] = (
            lax.ppermute(part[:, -h:], "box", down_box),
            lax.ppermute(part[:, :h], "box", up_box),
        )
    (cl_lo, ch_lo), (cl_hi, ch_hi) = corners["lo"], corners["hi"]
    return x_lo, x_hi, y_lo, y_hi, cl_lo, cl_hi, ch_lo, ch_hi


def local(phi_start, right_side, sigma):
    cells_x, cells_y, cells_z = phi_start.shape
    boxes = lax.axis_size("box")
    grps = lax.axis_size("grp")
    nx = cells_x * boxes
    ny = cells_y * grps
    b = lax.axis_index("box")
    g = lax.axis_index("grp")
    pieces = exchange((phi_start, right_side, sigma))
    planes = cells_x + 2 * HALO
    rows = cells_y + 2 * ROW_PAD
    lanes = cells_z
    idx = jnp.stack([b * cells_x - HALO, g * cells_y - ROW_PAD, g * (cells_y // 2)]).astype(jnp.int32)
    pz = jnp.asarray(np.kron(np.eye(cells_z // 2), np.ones((2, 1))), jnp.float32)
    full = pl.BlockSpec(memory_space=pltpu.MemorySpace.VMEM)
    anywhere = pl.BlockSpec(memory_space=pltpu.MemorySpace.HBM)
    big = pltpu.VMEM((planes, rows, lanes), jnp.float32)
    phi_smooth, coarse, group_coarse = pl.pallas_call(
        functools.partial(smooth_kernel, nx, ny),
        out_shape=(
            jax.ShapeDtypeStruct((cells_x, cells_y, cells_z), jnp.float32),
            jax.ShapeDtypeStruct((cells_x // 2 * (cells_y // 2), cells_z // 2), jnp.float32),
            jax.ShapeDtypeStruct((cells_x // 2, ny // 2, cells_z // 2), jnp.float32),
        ),
        in_specs=[pl.BlockSpec(memory_space=pltpu.MemorySpace.SMEM), full]
        + [anywhere] * 11,
        out_specs=(full, full, full),
        scratch_shapes=[big] * 9
        + [
            pltpu.VMEM((rows, lanes), jnp.int32),
            pltpu.VMEM((lanes // 128, cells_y, 128), jnp.float32),
            pltpu.VMEM((cells_x // 2 * (cells_y // 2), lanes), jnp.float32),
            pltpu.SemaphoreType.DMA((3 * (3 + 4 * HALO) + 2 * (2 * HALO + HALO - 1),)),
        ],
        compiler_params=pltpu.CompilerParams(vmem_limit_bytes=60 * 1024 * 1024),
    )(idx, pz, phi_start, right_side, sigma, *pieces)
    coarse = coarse.reshape(cells_x // 2, cells_y // 2, cells_z // 2)
    if grps == 2:
        other = lax.ppermute(coarse, "grp", [(0, 1), (1, 0)])
        group_coarse = lax.dynamic_update_slice(
            group_coarse, other, (0, (1 - g) * (cells_y // 2), 0))
    else:
        group_coarse = lax.all_gather(coarse, "grp", axis=1, tiled=True)
    return phi_smooth, group_coarse


def solution(mesh):
    placed = (P("box", "grp", None), P("box", "grp", None), P("box", "grp", None))
    return jax.shard_map(
        local,
        mesh=mesh,
        in_specs=placed,
        out_specs=(P("box", "grp", None), P("box", None, None)),
        check_vma=False,
    )
```

```python
import functools

import jax
import jax.numpy as jnp
import numpy as np
from jax import lax
from jax.experimental import pallas as pl
from jax.experimental.pallas import tpu as pltpu
from jax.sharding import PartitionSpec as P

SWEEPS = 2
HALO = 2 * SWEEPS + 1
ROW_PAD = 8
PHI_ROWS = ((0, (1, 2)), (0, (3, 4)), (0, (5,)))
Y_ROWS = {
    "lo": PHI_ROWS + tuple((2, (d,)) for d in range(HALO, 0, -1))
    + tuple((1, (d,)) for d in range(HALO - 1, 0, -1)),
    "hi": PHI_ROWS + tuple((2, (d,)) for d in range(1, HALO + 1))
    + tuple((1, (d,)) for d in range(1, HALO)),
}


def harmonic(s, t):
    return 2.0 * s * t / (s + t)


def smooth_kernel(nx, ny, idx_ref, pz_ref, own_phi, own_rhs, own_sig,
                  x_lo, x_hi, y_lo, y_hi, cl_lo, cl_hi, ch_lo, ch_hi,
                  phi_out, coarse_out, group_out, ph, rs, sg, fx, fy, fz, fzl, dg, inv, par,
                  pair_buf, y_sums, sems):
    planes, rows, lanes = ph.shape
    h = HALO
    cells_x = planes - 2 * h
    cells_y = rows - 2 * ROW_PAD
    gx0 = idx_ref[0]
    gy0 = idx_ref[1]
    mid = pl.ds(h, cells_x)
    lo_p = pl.ds(0, h)
    hi_p = pl.ds(h + cells_x, h)
    own_r = pl.ds(ROW_PAD, cells_y)
    copies = []
    for a, dst, own in ((2, sg, own_sig), (0, ph, own_phi), (1, rs, own_rhs)):
        pieces = [
            (own, dst.at[mid, own_r]),
            (x_lo.at[a], dst.at[lo_p, own_r]),
            (x_hi.at[a], dst.at[hi_p, own_r]),
        ]
        for side, y_part, below, above in (("lo", y_lo, cl_lo, ch_lo), ("hi", y_hi, cl_hi, ch_hi)):
            for k, (which, depths) in enumerate(Y_ROWS[side]):
                for d in depths if which == a else ():
                    row = ROW_PAD - d if side == "lo" else ROW_PAD + cells_y - 1 + d
                    pieces += [
                        (y_part.at[k], dst.at[mid, row]),
                        (below.at[k], dst.at[lo_p, row]),
                        (above.at[k], dst.at[hi_p, row]),
                    ]
        for src_ref, dst_ref in pieces:
            cp = pltpu.make_async_copy(src_ref, dst_ref, sems.at[len(copies)])
            copies.append(cp)
        if a == 2:
            per_array = len(copies)
    for cp in copies[:per_array]:
        cp.start()
    for cp in copies[:per_array]:
        cp.wait()
    for cp in copies[per_array:]:
        cp.start()
    row = lax.broadcasted_iota(jnp.int32, (rows, lanes), 0)
    lane = lax.broadcasted_iota(jnp.int32, (rows, lanes), 1)
    gy = gy0 + row
    iny = (gy >= 0) & (gy < ny)
    par[...] = jnp.where(iny, (gy + lane) & 1, 2)

    def face_x(i):
        gx = gx0 + i
        ok = (gx >= 0) & (gx + 1 < nx)
        s0 = sg[i]
        s1 = sg[i + 1]
        gyv = gy0 + lax.broadcasted_iota(jnp.int32, (rows, lanes), 0)
        inside = (gyv >= 0) & (gyv < ny) & ok
        fx[i] = jnp.where(inside, harmonic(s0, s1), 0.0)

    face_x(0)

    def faces_yz(i, carry):
        face_x(i)
        gx = gx0 + i
        inx = (gx >= 0) & (gx < nx)
        r = lax.broadcasted_iota(jnp.int32, (rows, lanes), 0)
        k = lax.broadcasted_iota(jnp.int32, (rows, lanes), 1)
        gyv = gy0 + r
        inyv = (gyv >= 0) & (gyv < ny)
        s = sg[i]
        s_yu = pltpu.roll(s, rows - 1, 0)
        s_zu = pltpu.roll(s, lanes - 1, 1)
        wy = jnp.where(inx & (gyv >= 0) & (gyv + 1 < ny), harmonic(s, s_yu), 0.0)
        wz = jnp.where(inx & inyv & (k < lanes - 1), harmonic(s, s_zu), 0.0)
        wy_lo = pltpu.roll(wy, 1, 0)
        wz_lo = pltpu.roll(wz, 1, 1)
        fy[i] = wy
        fz[i] = wz
        fzl[i] = wz_lo
        wxl = jnp.where(gx == 0, s, fx[i - 1])
        wxu = jnp.where(gx == nx - 1, s, fx[i])
        wyl = jnp.where(gyv == 0, s, wy_lo)
        wyu = jnp.where(gyv == ny - 1, s, wy)
        wzl = jnp.where(k == 0, s, wz_lo)
        wzu = jnp.where(k == lanes - 1, s, wz)
        d = wxl + wxu + wyl + wyu + wzl + wzu
        dg[i] = d
        inv[i] = 1.0 / d
        sg[i] = wy_lo
        return carry

    lax.fori_loop(1, planes - 1, faces_yz, 0, unroll=2)
    for cp in copies[per_array:]:
        cp.wait()

    def coupled_sum(i, pc):
        wy = fy[i]
        wz = fz[i]
        terms = (
            (fx[i - 1], ph[i - 1]),
            (fx[i], ph[i + 1]),
            (sg[i], pltpu.roll(pc, 1, 0)),
            (wy, pltpu.roll(pc, rows - 1, 0)),
            (fzl[i], pltpu.roll(pc, 1, 1)),
            (wz, pltpu.roll(pc, lanes - 1, 1)),
        )
        return terms

    for turn in range(2 * SWEEPS):
        colour = turn % 2

        def relax(i, carry, colour=colour):
            gx = gx0 + i
            inx = (gx >= 0) & (gx < nx)
            target = jnp.where(inx, (gx + colour) & 1, 3)
            pc = ph[i]
            summed = rs[i]
            for w, nb in coupled_sum(i, pc):
                summed = summed + w * nb
            ph[i] = jnp.where(par[...] == target, summed * inv[i], pc)
            return carry

        lax.fori_loop(turn + 1, planes - 1 - turn, relax, 0, unroll=2)

    own_rows = rows - 2 * ROW_PAD
    half_rows = own_rows // 2

    def defect_plane(i):
        pc = ph[i]
        terms = coupled_sum(i, pc)
        coupled = terms[0][0] * terms[0][1]
        for w, nb in terms[1:]:
            coupled = coupled + w * nb
        d = rs[i] - (dg[i] * pc - coupled)
        phi_out[i - HALO] = pc[ROW_PAD:ROW_PAD + own_rows]
        return d[ROW_PAD:ROW_PAD + own_rows]

    def restrict(j, carry):
        i = HALO + 2 * j
        pair = defect_plane(i) + defect_plane(i + 1)
        halves = []
        for q in range(lanes // 128):
            pair_buf[q] = pair[:, q * 128:(q + 1) * 128]
            even = pair_buf[q, pl.ds(0, half_rows, stride=2), :]
            odd = pair_buf[q, pl.ds(1, half_rows, stride=2), :]
            halves.append(even + odd)
        y_sums[pl.ds(pl.multiple_of(j * half_rows, half_rows), half_rows), :] = (
            jnp.concatenate(halves, axis=1))
        return carry

    lax.fori_loop(0, (planes - 2 * HALO) // 2, restrict, 0)
    coarse = 0.125 * jnp.dot(
        y_sums[...], pz_ref[...], precision=lax.Precision.HIGHEST,
        preferred_element_type=jnp.float32)
    coarse_out[...] = coarse
    first = idx_ref[2]
    for j in range(cells_x // 2):
        group_out[j, pl.ds(first, half_rows), :] = coarse[j * half_rows:(j + 1) * half_rows]


def y_send_kernel(pos_ref, phi, rhs, sig, out, stage, sems):
    planes, lanes = stage.shape[2], stage.shape[3]
    h = HALO
    top = pos_ref[2] == 0
    first = pos_ref[3]
    copies = []
    for a, src_ref in ((0, phi), (1, rhs), (2, sig)):
        for r in range(h):
            cp = pltpu.make_async_copy(src_ref.at[:, first + r], stage.at[a, r], sems.at[len(copies)])
            cp.start()
            copies.append(cp)
    for cp in copies:
        cp.wait()
    plane = lax.broadcasted_iota(jnp.int32, (planes, lanes), 0)
    z = lax.broadcasted_iota(jnp.int32, (planes, lanes), 1)
    parity = (pos_ref[0] + pos_ref[1] + first + plane + z) & 1
    for k, (lo_pair, hi_pair) in enumerate((((4, 3), (0, 1)), ((2, 1), (2, 3)))):
        a0 = jnp.where(top, stage[0, lo_pair[0]], stage[0, hi_pair[0]])
        a1 = jnp.where(top, stage[0, lo_pair[1]], stage[0, hi_pair[1]])
        offset = jnp.where(top, lo_pair[0], hi_pair[0])
        colour1 = ((parity + offset) & 1) == 1
        out[k] = jnp.where(colour1, a0, a1)
    out[2] = jnp.where(top, stage[0, 0], stage[0, h - 1])
    for r in range(h):
        out[3 + r] = stage[2, r]
    for r in range(h - 1):
        out[3 + h + r] = jnp.where(top, stage[1, r + 1], stage[1, r])


def exchange(arrays):
    boxes = lax.axis_size("box")
    grps = lax.axis_size("grp")
    h = HALO
    down_box = [(i, i + 1) for i in range(boxes - 1)]
    up_box = [(i + 1, i) for i in range(boxes - 1)]
    down_grp = [(i, i + 1) for i in range(grps - 1)]
    up_grp = [(i + 1, i) for i in range(grps - 1)]
    cells_x, cells_y, cells_z = arrays[0].shape
    gx = lax.axis_index("box") * cells_x + jnp.arange(cells_x, dtype=jnp.int32)[:, None]
    z = jnp.arange(cells_z, dtype=jnp.int32)[None, :]

    gy0 = lax.axis_index("grp") * cells_y

    def y_piece(side, block, slab_of):
        slabs = [jnp.swapaxes(a[:, block], 0, 1) for a in arrays]
        row_of = (lambda d: cells_y - d) if side == "lo" else (lambda d: d - 1)
        pairs = [depths for _, depths in PHI_ROWS if len(depths) == 2]
        colour1 = jnp.stack([(gx + gy0 + row_of(p[0]) + z) % 2 == 1 for p in pairs])
        first = jnp.stack([slabs[0][slab_of(p[0])] for p in pairs])
        second = jnp.stack([slabs[0][slab_of(p[1])] for p in pairs])
        single = [slabs[0][slab_of(d)][None] for _, (d, *more) in PHI_ROWS if not more]
        sig = slabs[2]
        rhs = slabs[1][1:] if side == "lo" else slabs[1][:-1]
        return jnp.concatenate([jnp.where(colour1, first, second)] + single + [sig, rhs])

    g = lax.axis_index("grp")
    swap = [(0, 1), (1, 0)]
    if grps == 2:
        first = jnp.where(g == 0, cells_y - h, 0)
        pos = jnp.stack([lax.axis_index("box") * cells_x, g * cells_y, g, first]).astype(jnp.int32)
        hbm = pl.BlockSpec(memory_space=pltpu.MemorySpace.HBM)
        y_send = pl.pallas_call(
            y_send_kernel,
            out_shape=jax.ShapeDtypeStruct((len(Y_ROWS["lo"]), cells_x, cells_z), jnp.float32),
            in_specs=[pl.BlockSpec(memory_space=pltpu.MemorySpace.SMEM), hbm, hbm, hbm],
            out_specs=pl.BlockSpec(memory_space=pltpu.MemorySpace.VMEM),
            scratch_shapes=[
                pltpu.VMEM((3, h, cells_x, cells_z), jnp.float32),
                pltpu.SemaphoreType.DMA((3 * h,)),
            ],
        )(pos, *arrays)
        y_lo = y_hi = lax.ppermute(y_send, "grp", swap)
    else:
        y_lo_send = y_piece("lo", slice(-h, None), lambda d: h - d)
        y_hi_send = y_piece("hi", slice(0, h), lambda d: d - 1)
        y_lo = lax.ppermute(y_lo_send, "grp", down_grp)
        y_hi = lax.ppermute(y_hi_send, "grp", up_grp)
    x_lo = lax.ppermute(jnp.stack([a[-h:] for a in arrays]), "box", down_box)
    x_hi = lax.ppermute(jnp.stack([a[:h] for a in arrays]), "box", up_box)
    if grps == 2:
        def diag(db):
            return [((b - db) * 2 + 1 - g_, b * 2 + g_)
                    for b in range(boxes) if 0 <= b - db < boxes for g_ in range(2)]

        cl = lax.ppermute(y_send[:, -h:], ("box", "grp"), diag(1))
        ch = lax.ppermute(y_send[:, :h], ("box", "grp"), diag(-1))
        return x_lo, x_hi, y_lo, y_hi, cl, cl, ch, ch
    corners = {}
    for name, part in (("lo", y_lo), ("hi", y_hi)):
        if name == "hi" and part is y_lo:
            corners["hi"] = corners["lo"]
            continue
        corners[name] = (
            lax.ppermute(part[:, -h:], "box", down_box),
            lax.ppermute(part[:, :h], "box", up_box),
        )
    (cl_lo, ch_lo), (cl_hi, ch_hi) = corners["lo"], corners["hi"]
    return x_lo, x_hi, y_lo, y_hi, cl_lo, cl_hi, ch_lo, ch_hi


def local(phi_start, right_side, sigma):
    cells_x, cells_y, cells_z = phi_start.shape
    boxes = lax.axis_size("box")
    grps = lax.axis_size("grp")
    nx = cells_x * boxes
    ny = cells_y * grps
    b = lax.axis_index("box")
    g = lax.axis_index("grp")
    pieces = exchange((phi_start, right_side, sigma))
    planes = cells_x + 2 * HALO
    rows = cells_y + 2 * ROW_PAD
    lanes = cells_z
    idx = jnp.stack([b * cells_x - HALO, g * cells_y - ROW_PAD, g * (cells_y // 2)]).astype(jnp.int32)
    pz = jnp.asarray(np.kron(np.eye(cells_z // 2), np.ones((2, 1))), jnp.float32)
    full = pl.BlockSpec(memory_space=pltpu.MemorySpace.VMEM)
    anywhere = pl.BlockSpec(memory_space=pltpu.MemorySpace.HBM)
    big = pltpu.VMEM((planes, rows, lanes), jnp.float32)
    phi_smooth, coarse, group_coarse = pl.pallas_call(
        functools.partial(smooth_kernel, nx, ny),
        out_shape=(
            jax.ShapeDtypeStruct((cells_x, cells_y, cells_z), jnp.float32),
            jax.ShapeDtypeStruct((cells_x // 2 * (cells_y // 2), cells_z // 2), jnp.float32),
            jax.ShapeDtypeStruct((cells_x // 2, ny // 2, cells_z // 2), jnp.float32),
        ),
        in_specs=[pl.BlockSpec(memory_space=pltpu.MemorySpace.SMEM), full]
        + [anywhere] * 11,
        out_specs=(full, full, full),
        scratch_shapes=[big] * 9
        + [
            pltpu.VMEM((rows, lanes), jnp.int32),
            pltpu.VMEM((lanes // 128, cells_y, 128), jnp.float32),
            pltpu.VMEM((cells_x // 2 * (cells_y // 2), lanes), jnp.float32),
            pltpu.SemaphoreType.DMA((3 * (3 + 4 * HALO) + 2 * (2 * HALO + HALO - 1),)),
        ],
        compiler_params=pltpu.CompilerParams(vmem_limit_bytes=60 * 1024 * 1024),
    )(idx, pz, phi_start, right_side, sigma, *pieces)
    coarse = coarse.reshape(cells_x // 2, cells_y // 2, cells_z // 2)
    if grps == 2:
        other = lax.ppermute(coarse, "grp", [(0, 1), (1, 0)])
        group_coarse = lax.dynamic_update_slice(
            group_coarse, other, (0, (1 - g) * (cells_y // 2), 0))
    else:
        group_coarse = lax.all_gather(coarse, "grp", axis=1, tiled=True)
    return phi_smooth, group_coarse


def solution(mesh):
    placed = (P("box", "grp", None), P("box", "grp", None), P("box", "grp", None))
    return jax.shard_map(
        local,
        mesh=mesh,
        in_specs=placed,
        out_specs=(P("box", "grp", None), P("box", None, None)),
        check_vma=False,
    )
```

```python
import functools

import jax
import jax.numpy as jnp
import numpy as np
from jax import lax
from jax.experimental import pallas as pl
from jax.experimental.pallas import tpu as pltpu
from jax.sharding import PartitionSpec as P

SWEEPS = 2
HALO = 2 * SWEEPS + 1
ROW_PAD = 8
PHI_ROWS = ((0, (1, 2)), (0, (3, 4)), (0, (5,)))
Y_ROWS = {
    "lo": PHI_ROWS + tuple((2, (d,)) for d in range(HALO, 0, -1))
    + tuple((1, (d,)) for d in range(HALO - 1, 0, -1)),
    "hi": PHI_ROWS + tuple((2, (d,)) for d in range(1, HALO + 1))
    + tuple((1, (d,)) for d in range(1, HALO)),
}


def harmonic(s, t):
    return 2.0 * s * t / (s + t)


def smooth_kernel(nx, ny, idx_ref, pz_ref, own_phi, own_rhs, own_sig,
                  x_lo, x_hi, y_lo, y_hi, cl_lo, cl_hi, ch_lo, ch_hi,
                  phi_out, coarse_out, group_out, ph, rs, sg, fx, fy, fz, fzl, dg, inv, par,
                  pair_buf, y_sums, sems):
    planes, rows, lanes = ph.shape
    h = HALO
    cells_x = planes - 2 * h
    cells_y = rows - 2 * ROW_PAD
    gx0 = idx_ref[0]
    gy0 = idx_ref[1]
    mid = pl.ds(h, cells_x)
    lo_p = pl.ds(0, h)
    hi_p = pl.ds(h + cells_x, h)
    own_r = pl.ds(ROW_PAD, cells_y)
    copies = []
    for a, dst, own in ((2, sg, own_sig), (0, ph, own_phi), (1, rs, own_rhs)):
        pieces = [
            (own, dst.at[mid, own_r]),
            (x_lo.at[a], dst.at[lo_p, own_r]),
            (x_hi.at[a], dst.at[hi_p, own_r]),
        ]
        for side, y_part, below, above in (("lo", y_lo, cl_lo, ch_lo), ("hi", y_hi, cl_hi, ch_hi)):
            for k, (which, depths) in enumerate(Y_ROWS[side]):
                for d in depths if which == a else ():
                    row = ROW_PAD - d if side == "lo" else ROW_PAD + cells_y - 1 + d
                    pieces += [
                        (y_part.at[k], dst.at[mid, row]),
                        (below.at[k], dst.at[lo_p, row]),
                        (above.at[k], dst.at[hi_p, row]),
                    ]
        for src_ref, dst_ref in pieces:
            cp = pltpu.make_async_copy(src_ref, dst_ref, sems.at[len(copies)])
            cp.start()
            copies.append(cp)
        if a == 2:
            per_array = len(copies)
    for cp in copies[:per_array]:
        cp.wait()
    row = lax.broadcasted_iota(jnp.int32, (rows, lanes), 0)
    lane = lax.broadcasted_iota(jnp.int32, (rows, lanes), 1)
    gy = gy0 + row
    iny = (gy >= 0) & (gy < ny)
    par[...] = jnp.where(iny, (gy + lane) & 1, 2)

    def face_x(i):
        gx = gx0 + i
        ok = (gx >= 0) & (gx + 1 < nx)
        s0 = sg[i]
        s1 = sg[i + 1]
        gyv = gy0 + lax.broadcasted_iota(jnp.int32, (rows, lanes), 0)
        inside = (gyv >= 0) & (gyv < ny) & ok
        fx[i] = jnp.where(inside, harmonic(s0, s1), 0.0)

    face_x(0)

    def faces_yz(i, carry):
        face_x(i)
        gx = gx0 + i
        inx = (gx >= 0) & (gx < nx)
        r = lax.broadcasted_iota(jnp.int32, (rows, lanes), 0)
        k = lax.broadcasted_iota(jnp.int32, (rows, lanes), 1)
        gyv = gy0 + r
        inyv = (gyv >= 0) & (gyv < ny)
        s = sg[i]
        s_yu = pltpu.roll(s, rows - 1, 0)
        s_zu = pltpu.roll(s, lanes - 1, 1)
        wy = jnp.where(inx & (gyv >= 0) & (gyv + 1 < ny), harmonic(s, s_yu), 0.0)
        wz = jnp.where(inx & inyv & (k < lanes - 1), harmonic(s, s_zu), 0.0)
        wy_lo = pltpu.roll(wy, 1, 0)
        wz_lo = pltpu.roll(wz, 1, 1)
        fy[i] = wy
        fz[i] = wz
        fzl[i] = wz_lo
        wxl = jnp.where(gx == 0, s, fx[i - 1])
        wxu = jnp.where(gx == nx - 1, s, fx[i])
        wyl = jnp.where(gyv == 0, s, wy_lo)
        wyu = jnp.where(gyv == ny - 1, s, wy)
        wzl = jnp.where(k == 0, s, wz_lo)
        wzu = jnp.where(k == lanes - 1, s, wz)
        d = wxl + wxu + wyl + wyu + wzl + wzu
        dg[i] = d
        inv[i] = 1.0 / d
        sg[i] = wy_lo
        return carry

    lax.fori_loop(1, planes - 1, faces_yz, 0, unroll=2)
    for cp in copies[per_array:]:
        cp.wait()

    def coupled_sum(i, pc):
        wy = fy[i]
        wz = fz[i]
        terms = (
            (fx[i - 1], ph[i - 1]),
            (fx[i], ph[i + 1]),
            (sg[i], pltpu.roll(pc, 1, 0)),
            (wy, pltpu.roll(pc, rows - 1, 0)),
            (fzl[i], pltpu.roll(pc, 1, 1)),
            (wz, pltpu.roll(pc, lanes - 1, 1)),
        )
        return terms

    for turn in range(2 * SWEEPS):
        colour = turn % 2

        def relax(i, carry, colour=colour):
            gx = gx0 + i
            inx = (gx >= 0) & (gx < nx)
            target = jnp.where(inx, (gx + colour) & 1, 3)
            pc = ph[i]
            summed = rs[i]
            for w, nb in coupled_sum(i, pc):
                summed = summed + w * nb
            ph[i] = jnp.where(par[...] == target, summed * inv[i], pc)
            return carry

        lax.fori_loop(turn + 1, planes - 1 - turn, relax, 0, unroll=2)

    own_rows = rows - 2 * ROW_PAD
    half_rows = own_rows // 2

    def defect_plane(i):
        pc = ph[i]
        terms = coupled_sum(i, pc)
        coupled = terms[0][0] * terms[0][1]
        for w, nb in terms[1:]:
            coupled = coupled + w * nb
        d = rs[i] - (dg[i] * pc - coupled)
        phi_out[i - HALO] = pc[ROW_PAD:ROW_PAD + own_rows]
        return d[ROW_PAD:ROW_PAD + own_rows]

    def restrict(j, carry):
        i = HALO + 2 * j
        pair = defect_plane(i) + defect_plane(i + 1)
        halves = []
        for q in range(lanes // 128):
            pair_buf[q] = pair[:, q * 128:(q + 1) * 128]
            even = pair_buf[q, pl.ds(0, half_rows, stride=2), :]
            odd = pair_buf[q, pl.ds(1, half_rows, stride=2), :]
            halves.append(even + odd)
        y_sums[pl.ds(pl.multiple_of(j * half_rows, half_rows), half_rows), :] = (
            jnp.concatenate(halves, axis=1))
        return carry

    lax.fori_loop(0, (planes - 2 * HALO) // 2, restrict, 0, unroll=2)
    coarse = 0.125 * jnp.dot(
        y_sums[...], pz_ref[...], precision=lax.Precision.HIGHEST,
        preferred_element_type=jnp.float32)
    coarse_out[...] = coarse
    first = idx_ref[2]
    for j in range(cells_x // 2):
        group_out[j, pl.ds(first, half_rows), :] = coarse[j * half_rows:(j + 1) * half_rows]


def y_send_kernel(pos_ref, phi, rhs, sig, out, stage, sems):
    planes, lanes = stage.shape[2], stage.shape[3]
    h = HALO
    top = pos_ref[2] == 0
    first = pos_ref[3]
    copies = []
    for a, src_ref in ((0, phi), (1, rhs), (2, sig)):
        for r in range(h):
            cp = pltpu.make_async_copy(src_ref.at[:, first + r], stage.at[a, r], sems.at[len(copies)])
            cp.start()
            copies.append(cp)
    for cp in copies:
        cp.wait()
    plane = lax.broadcasted_iota(jnp.int32, (planes, lanes), 0)
    z = lax.broadcasted_iota(jnp.int32, (planes, lanes), 1)
    parity = (pos_ref[0] + pos_ref[1] + first + plane + z) & 1
    for k, (lo_pair, hi_pair) in enumerate((((4, 3), (0, 1)), ((2, 1), (2, 3)))):
        a0 = jnp.where(top, stage[0, lo_pair[0]], stage[0, hi_pair[0]])
        a1 = jnp.where(top, stage[0, lo_pair[1]], stage[0, hi_pair[1]])
        offset = jnp.where(top, lo_pair[0], hi_pair[0])
        colour1 = ((parity + offset) & 1) == 1
        out[k] = jnp.where(colour1, a0, a1)
    out[2] = jnp.where(top, stage[0, 0], stage[0, h - 1])
    for r in range(h):
        out[3 + r] = stage[2, r]
    for r in range(h - 1):
        out[3 + h + r] = jnp.where(top, stage[1, r + 1], stage[1, r])


def exchange(arrays):
    boxes = lax.axis_size("box")
    grps = lax.axis_size("grp")
    h = HALO
    down_box = [(i, i + 1) for i in range(boxes - 1)]
    up_box = [(i + 1, i) for i in range(boxes - 1)]
    down_grp = [(i, i + 1) for i in range(grps - 1)]
    up_grp = [(i + 1, i) for i in range(grps - 1)]
    cells_x, cells_y, cells_z = arrays[0].shape
    gx = lax.axis_index("box") * cells_x + jnp.arange(cells_x, dtype=jnp.int32)[:, None]
    z = jnp.arange(cells_z, dtype=jnp.int32)[None, :]

    gy0 = lax.axis_index("grp") * cells_y

    def y_piece(side, block, slab_of):
        slabs = [jnp.swapaxes(a[:, block], 0, 1) for a in arrays]
        row_of = (lambda d: cells_y - d) if side == "lo" else (lambda d: d - 1)
        pairs = [depths for _, depths in PHI_ROWS if len(depths) == 2]
        colour1 = jnp.stack([(gx + gy0 + row_of(p[0]) + z) % 2 == 1 for p in pairs])
        first = jnp.stack([slabs[0][slab_of(p[0])] for p in pairs])
        second = jnp.stack([slabs[0][slab_of(p[1])] for p in pairs])
        single = [slabs[0][slab_of(d)][None] for _, (d, *more) in PHI_ROWS if not more]
        sig = slabs[2]
        rhs = slabs[1][1:] if side == "lo" else slabs[1][:-1]
        return jnp.concatenate([jnp.where(colour1, first, second)] + single + [sig, rhs])

    g = lax.axis_index("grp")
    swap = [(0, 1), (1, 0)]
    if grps == 2:
        first = jnp.where(g == 0, cells_y - h, 0)
        pos = jnp.stack([lax.axis_index("box") * cells_x, g * cells_y, g, first]).astype(jnp.int32)
        hbm = pl.BlockSpec(memory_space=pltpu.MemorySpace.HBM)
        y_send = pl.pallas_call(
            y_send_kernel,
            out_shape=jax.ShapeDtypeStruct((len(Y_ROWS["lo"]), cells_x, cells_z), jnp.float32),
            in_specs=[pl.BlockSpec(memory_space=pltpu.MemorySpace.SMEM), hbm, hbm, hbm],
            out_specs=pl.BlockSpec(memory_space=pltpu.MemorySpace.VMEM),
            scratch_shapes=[
                pltpu.VMEM((3, h, cells_x, cells_z), jnp.float32),
                pltpu.SemaphoreType.DMA((3 * h,)),
            ],
        )(pos, *arrays)
        y_lo = y_hi = lax.ppermute(y_send, "grp", swap)
    else:
        y_lo_send = y_piece("lo", slice(-h, None), lambda d: h - d)
        y_hi_send = y_piece("hi", slice(0, h), lambda d: d - 1)
        y_lo = lax.ppermute(y_lo_send, "grp", down_grp)
        y_hi = lax.ppermute(y_hi_send, "grp", up_grp)
    x_lo = lax.ppermute(jnp.stack([a[-h:] for a in arrays]), "box", down_box)
    x_hi = lax.ppermute(jnp.stack([a[:h] for a in arrays]), "box", up_box)
    if grps == 2:
        def diag(db):
            return [((b - db) * 2 + 1 - g_, b * 2 + g_)
                    for b in range(boxes) if 0 <= b - db < boxes for g_ in range(2)]

        cl = lax.ppermute(y_send[:, -h:], ("box", "grp"), diag(1))
        ch = lax.ppermute(y_send[:, :h], ("box", "grp"), diag(-1))
        return x_lo, x_hi, y_lo, y_hi, cl, cl, ch, ch
    corners = {}
    for name, part in (("lo", y_lo), ("hi", y_hi)):
        if name == "hi" and part is y_lo:
            corners["hi"] = corners["lo"]
            continue
        corners[name] = (
            lax.ppermute(part[:, -h:], "box", down_box),
            lax.ppermute(part[:, :h], "box", up_box),
        )
    (cl_lo, ch_lo), (cl_hi, ch_hi) = corners["lo"], corners["hi"]
    return x_lo, x_hi, y_lo, y_hi, cl_lo, cl_hi, ch_lo, ch_hi


def local(phi_start, right_side, sigma):
    cells_x, cells_y, cells_z = phi_start.shape
    boxes = lax.axis_size("box")
    grps = lax.axis_size("grp")
    nx = cells_x * boxes
    ny = cells_y * grps
    b = lax.axis_index("box")
    g = lax.axis_index("grp")
    pieces = exchange((phi_start, right_side, sigma))
    planes = cells_x + 2 * HALO
    rows = cells_y + 2 * ROW_PAD
    lanes = cells_z
    idx = jnp.stack([b * cells_x - HALO, g * cells_y - ROW_PAD, g * (cells_y // 2)]).astype(jnp.int32)
    pz = jnp.asarray(np.kron(np.eye(cells_z // 2), np.ones((2, 1))), jnp.float32)
    full = pl.BlockSpec(memory_space=pltpu.MemorySpace.VMEM)
    anywhere = pl.BlockSpec(memory_space=pltpu.MemorySpace.HBM)
    big = pltpu.VMEM((planes, rows, lanes), jnp.float32)
    phi_smooth, coarse, group_coarse = pl.pallas_call(
        functools.partial(smooth_kernel, nx, ny),
        out_shape=(
            jax.ShapeDtypeStruct((cells_x, cells_y, cells_z), jnp.float32),
            jax.ShapeDtypeStruct((cells_x // 2 * (cells_y // 2), cells_z // 2), jnp.float32),
            jax.ShapeDtypeStruct((cells_x // 2, ny // 2, cells_z // 2), jnp.float32),
        ),
        in_specs=[pl.BlockSpec(memory_space=pltpu.MemorySpace.SMEM), full]
        + [anywhere] * 11,
        out_specs=(full, full, full),
        scratch_shapes=[big] * 9
        + [
            pltpu.VMEM((rows, lanes), jnp.int32),
            pltpu.VMEM((lanes // 128, cells_y, 128), jnp.float32),
            pltpu.VMEM((cells_x // 2 * (cells_y // 2), lanes), jnp.float32),
            pltpu.SemaphoreType.DMA((3 * (3 + 4 * HALO) + 2 * (2 * HALO + HALO - 1),)),
        ],
        compiler_params=pltpu.CompilerParams(vmem_limit_bytes=60 * 1024 * 1024),
    )(idx, pz, phi_start, right_side, sigma, *pieces)
    coarse = coarse.reshape(cells_x // 2, cells_y // 2, cells_z // 2)
    if grps == 2:
        other = lax.ppermute(coarse, "grp", [(0, 1), (1, 0)])
        group_coarse = lax.dynamic_update_slice(
            group_coarse, other, (0, (1 - g) * (cells_y // 2), 0))
    else:
        group_coarse = lax.all_gather(coarse, "grp", axis=1, tiled=True)
    return phi_smooth, group_coarse


def solution(mesh):
    placed = (P("box", "grp", None), P("box", "grp", None), P("box", "grp", None))
    return jax.shard_map(
        local,
        mesh=mesh,
        in_specs=placed,
        out_specs=(P("box", "grp", None), P("box", None, None)),
        check_vma=False,
    )
```
